32 devices in a mesh: dp: 8 (over z, x), fsdp: 4 (over y, core).
Axes of the slice: x: 2, y: 2, z: 4, core: 2. Of those that a mesh axis runs over, the one named last changes fastest.
Arguments:
- inputs: bfloat16 [16384, 768], P(('dp', 'fsdp')), may hold values from -6 to 6
- cotangent: bfloat16 [16384, 768], P(('dp', 'fsdp')), may hold values from -6 to 6
- masked: int32 [32, 512], P(('dp', 'fsdp')), may hold values from 0 to 1, as said below
- query_weight: bfloat16 [768, 768], P(('dp', 'fsdp')), may hold values from -0.21875 to 0.21875
- query_bias: bfloat16 [768], P(('dp', 'fsdp')), may hold values from -3 to 3
- key_weight: bfloat16 [768, 768], P(('dp', 'fsdp')), may hold values from -0.21875 to 0.21875
- value_weight: bfloat16 [768, 768], P(('dp', 'fsdp')), may hold values from -0.21875 to 0.21875
- value_bias: bfloat16 [768], P(('dp', 'fsdp')), may hold values from -0.14941406 to 0.14941406
- output_weight: bfloat16 [768, 768], P(('dp', 'fsdp')), may hold values from -0.875 to 0.875
- output_bias: bfloat16 [768], P(('dp', 'fsdp')), may hold values from -0.5 to 0.5
- first_gain: bfloat16 [768], P(('dp', 'fsdp')), may hold values from 0.25 to 1.75
- first_shift: bfloat16 [768], P(('dp', 'fsdp')), may hold values from -0.5 to 0.5
- inner_weight: bfloat16 [768, 3072], P(('dp', 'fsdp')), may hold values from -0.21875 to 0.21875
- inner_bias: bfloat16 [3072], P(('dp', 'fsdp')), may hold values from -0.5 to 0.5
- outer_weight: bfloat16 [3072, 768], P(('dp', 'fsdp')), may hold values from -0.109375 to 0.109375
- outer_bias: bfloat16 [768], P(('dp', 'fsdp')), may hold values from -0.5 to 0.5
- second_gain: bfloat16 [768], P(('dp', 'fsdp')), may hold values from 0.25 to 1.75
- second_shift: bfloat16 [768], P(('dp', 'fsdp')), may hold values from -0.5 to 0.5
Outputs:
- outputs: bfloat16 [16384, 768], P(('dp', 'fsdp'))
- input_grad: bfloat16 [16384, 768], P(('dp', 'fsdp'))
- query_weight_grad: float32 [768, 768], P(('dp', 'fsdp'))
- query_bias_grad: float32 [768], P(('dp', 'fsdp'))
- key_weight_grad: float32 [768, 768], P(('dp', 'fsdp'))
- value_weight_grad: float32 [768, 768], P(('dp', 'fsdp'))
- value_bias_grad: float32 [768], P(('dp', 'fsdp'))
- output_weight_grad: float32 [768, 768], P(('dp', 'fsdp'))
- output_bias_grad: float32 [768], P(('dp', 'fsdp'))
- first_gain_grad: float32 [768], P(('dp', 'fsdp'))
- first_shift_grad: float32 [768], P(('dp', 'fsdp'))
- inner_weight_grad: float32 [768, 3072], P(('dp', 'fsdp'))
- inner_bias_grad: float32 [3072], P(('dp', 'fsdp'))
- outer_weight_grad: float32 [3072, 768], P(('dp', 'fsdp'))
- outer_bias_grad: float32 [768], P(('dp', 'fsdp'))
- second_gain_grad: float32 [768], P(('dp', 'fsdp'))
- second_shift_grad: float32 [768], P(('dp', 'fsdp'))
The draws below stay inside these ranges and needn't reach their ends.
Inputs may be any that keep to these rules, and one draw needn't show every extreme that they name: `masked`: each sequence has 1 to 80 ones, in runs of 1 to 3 positions; some sequence has exactly 80.
All inputs are finite; a program needn't handle non-finite values.
Results may differ from the reference program's by a relative error of at most 0.02.
Values may be sent and summed in bfloat16 or wider, within the bound.
No kernel may reach another device: no remote copies, remote signals or barrier semaphores. Data moves between devices by JAX's collectives and lax.ppermute only.
A program may use at most 256 MiB of HBM per device.

```python
import math
import jax
import jax.numpy as jnp
from jax import lax

D = 768
HEADS = 12
FF = 3072
SEQ = 512
LAYERS = 3
MASK_MOST = 80
SEQS = 32
TOKENS = 16384


def draw_masked(key, part):
    spans_most = (MASK_MOST + 2) // 3
    slot_count = SEQ // 4
    key_count, key_length, key_order, key_pick = jax.random.split(key, 4)
    counts = jax.random.randint(key_count, (SEQS,), 1, max(spans_most, 2))
    counts = jnp.minimum(counts, max(spans_most - 1, 1))
    lengths = jax.random.randint(key_length, (SEQS, spans_most), 1, 4)
    chosen = jax.random.randint(key_pick, (), 0, SEQS)
    span_index = jnp.arange(spans_most)
    full_lengths = jnp.where(span_index < spans_most - 1, 3, MASK_MOST - 3 * (spans_most - 1))
    is_chosen = jnp.arange(SEQS) == chosen
    counts = jnp.where(is_chosen, spans_most, counts)
    lengths = jnp.where(is_chosen[:, None], full_lengths[None, :], lengths)
    in_use = span_index[None, :] < counts[:, None]
    lengths = jnp.where(in_use, lengths, 0)

    def one_order(one_key):
        return jax.random.permutation(one_key, slot_count)
    slot_order = jax.vmap(one_order)(jax.random.split(key_order, SEQS))[:, :spans_most]
    per_slot = jnp.sum(jnp.where(slot_order[:, :, None] == jnp.arange(slot_count)[None, None, :], lengths[:, :, None], 0), axis=1)
    inside = jnp.arange(4)[None, None, :] < per_slot[:, :, None]
    return inside.reshape(SEQS, slot_count * 4).astype(jnp.int32)


def spiked(drawn, stream_key, source, target, parts, factor):
    owner, partner = [(jnp.arange(drawn.shape[axis_at]) // (drawn.shape[axis_at] // parts)).reshape([-1 if axis == axis_at else 1 for axis in range(drawn.ndim)]) for axis_at in (source, target)]
    chosen = jax.random.permutation(stream_key, parts)[partner]
    strong = (owner == chosen) | (owner == (partner + parts // 2) % parts)
    return jnp.where(strong, factor * drawn, drawn)


def block_scale(key, extent, cuts, low, high):
    def one(dim, shards_of):
        heights = jax.random.uniform(jax.random.fold_in(jax.random.fold_in(key, 6), dim), (shards_of,), jnp.float32, low / len(cuts), high / len(cuts))
        return jnp.repeat(jnp.exp(heights), extent[dim] // shards_of).reshape((-1,) + (1,) * (len(extent) - dim - 1))

    loudness = one(*cuts[0])
    for cut in cuts[1:]:
        loudness = loudness * one(*cut)
    return loudness


def scatter_about(own_key, dims, spread, limit, cuts=(), dtype=jnp.bfloat16):
    values = spread * jax.random.normal(own_key, dims, jnp.float32)
    if cuts:
        values = values * block_scale(own_key, dims, cuts, -0.22, 0.18)
    return jnp.clip(values, -limit, limit).astype(dtype)


def gaussian_with(stream_key, dims, spread, reach, cuts, heavy, held_as=jnp.bfloat16):
    values = spread * jax.random.normal(stream_key, dims, jnp.float32)
    if cuts:
        values = values * block_scale(stream_key, dims, cuts, -0.22, 0.18)
    return jnp.clip(spiked(values, jax.random.fold_in(stream_key, 3), *heavy), -reach, reach).astype(held_as)


def setup_inputs(seed: int = 0) -> dict:
    streams_of = jax.random.split(jax.random.key(seed), 19)
    return {
        "inputs": gaussian_with(streams_of[0], (TOKENS, D), 1.0, 6.0, ((0, 32),), (0, 1, 32, 2.75)),
        "cotangent": gaussian_with(streams_of[1], (TOKENS, D), 1.0, 6.0, ((0, 32),), (0, 1, 32, 2.75)),
        "masked": draw_masked(jax.random.fold_in(streams_of[18], 71), 0),
        "query_weight": scatter_about(streams_of[3], (D, D), D ** -0.5, 0.21875, ((0, 32),)),
        "query_bias": scatter_about(streams_of[4], (D,), 0.5, 3.0, ((0, 32),)),
        "key_weight": scatter_about(streams_of[5], (D, D), D ** -0.5, 0.21875, ((0, 32),)),
        "value_weight": scatter_about(streams_of[6], (D, D), D ** -0.5, 0.21875, ((0, 32),)),
        "value_bias": scatter_about(streams_of[7], (D,), 0.03, 0.14941406, ((0, 32),)),
        "output_weight": scatter_about(streams_of[8], (D, D), (D // 16) ** -0.5, 0.875, ((0, 32),)),
        "output_bias": scatter_about(streams_of[9], (D,), 0.1, 0.5, ((0, 32),)),
        "first_gain": jnp.clip(1.0 + 0.15 * jax.random.normal(streams_of[10], (D,), jnp.float32), 0.25, 1.75).astype(jnp.bfloat16),
        "first_shift": scatter_about(streams_of[11], (D,), 0.1, 0.5, ((0, 32),)),
        "inner_weight": scatter_about(streams_of[12], (D, FF), D ** -0.5, 0.21875, ((0, 32),)),
        "inner_bias": scatter_about(streams_of[13], (FF,), 0.1, 0.5, ((0, 32),)),
        "outer_weight": scatter_about(streams_of[14], (FF, D), FF ** -0.5, 0.109375, ((0, 32),)),
        "outer_bias": scatter_about(streams_of[15], (D,), 0.1, 0.5, ((0, 32),)),
        "second_gain": jnp.clip(1.0 + 0.15 * jax.random.normal(streams_of[16], (D,), jnp.float32), 0.25, 1.75).astype(jnp.bfloat16),
        "second_shift": scatter_about(streams_of[17], (D,), 0.1, 0.5, ((0, 32),)),
    }


@jax.custom_vjp
def low(v):
    return lax.optimization_barrier(v.astype(jnp.bfloat16)).astype(jnp.float32)

@jax.custom_vjp
def low_back(v):
    return v

def low_keep(v):
    return (low(v), None)

def low_pass(kept, grad):
    return (grad,)

def back_keep(v):
    return (v, None)

def back_low(kept, grad):
    return (low(grad),)
low.defvjp(low_keep, low_pass)
low_back.defvjp(back_keep, back_low)

def matmul(left, right):
    return jnp.dot(left, right, preferred_element_type=jnp.float32, precision=lax.Precision.HIGHEST)

def layer_norm(summed, gain, shift):
    centre = summed - lax.optimization_barrier(jnp.mean(summed, axis=-1, keepdims=True))
    inverse = lax.rsqrt(lax.optimization_barrier(jnp.mean(centre * centre, axis=-1, keepdims=True)) + 1e-05)
    return centre * inverse * gain + shift

def attention(query_rows, key_rows, value_rows):
    group_size = query_rows.shape[0] // SEQ
    head_size = query_rows.shape[1] // HEADS

    def by_heads(rows):
        return rows.reshape(group_size, SEQ, HEADS, head_size)
    scores = jnp.einsum('gqhd,gkhd->ghqk', by_heads(query_rows), by_heads(key_rows), precision=lax.Precision.HIGHEST) * head_size ** (-0.5)
    scores = low_back(scores)
    top_score = lax.optimization_barrier(jnp.max(scores, axis=-1, keepdims=True))
    weights = jnp.exp(scores - top_score)
    probs = low(weights / lax.optimization_barrier(jnp.sum(weights, axis=-1, keepdims=True)))
    context = jnp.einsum('ghqk,gkhd->gqhd', probs, by_heads(value_rows), precision=lax.Precision.HIGHEST)
    return context.reshape(group_size * SEQ, HEADS * head_size)

def layer(params, hidden):
    query_weight, query_bias, key_weight, value_weight, value_bias, output_weight, output_bias, first_gain, first_shift, inner_weight, inner_bias, outer_weight, outer_bias, second_gain, second_shift = params
    rows_low = low(hidden)
    query_rows = low(low_back(matmul(rows_low, query_weight) + query_bias))
    key_rows = low(low_back(matmul(rows_low, key_weight)))
    value_rows = low(low_back(matmul(rows_low, value_weight) + value_bias))
    context = low(low_back(attention(query_rows, key_rows, value_rows)))
    attended = low_back(matmul(context, output_weight) + output_bias)
    first_out = layer_norm(hidden + attended, first_gain, first_shift)
    inner_pre = low_back(matmul(low(first_out), inner_weight) + inner_bias)
    inner_low = low(jax.nn.gelu(inner_pre, approximate=True))
    outer_out = low_back(matmul(inner_low, outer_weight) + outer_bias)
    return layer_norm(first_out + outer_out, second_gain, second_shift)

def reference(inputs, cotangent, masked, query_weight, query_bias, key_weight, value_weight, value_bias, output_weight, output_bias, first_gain, first_shift, inner_weight, inner_bias, outer_weight, outer_bias, second_gain, second_shift):
    params = tuple((weight.astype(jnp.float32) for weight in (query_weight, query_bias, key_weight, value_weight, value_bias, output_weight, output_bias, first_gain, first_shift, inner_weight, inner_bias, outer_weight, outer_bias, second_gain, second_shift)))
    group_size = math.gcd(SEQS, max(1, 4096 // SEQ))
    blocks = SEQS // group_size
    starts = inputs.astype(jnp.float32).reshape(blocks, group_size * SEQ, D)
    pull_rows = (cotangent.astype(jnp.float32) * masked.astype(jnp.float32).reshape(TOKENS, 1)).reshape(blocks, group_size * SEQ, D)

    def network(weights, hidden):
        for applied in range(LAYERS):
            hidden = layer(weights, hidden)
        return hidden

    def advance(totals, pair):
        start_block, pull_block = pair
        result, backward = jax.vjp(network, params, start_block)
        weight_grads, row_grads = backward(pull_block)
        return (jax.tree.map(jnp.add, totals, weight_grads), (result, row_grads))
    zero_grads = tuple((jnp.zeros_like(weight) for weight in params))
    totals, (results, row_grads) = lax.scan(advance, zero_grads, (starts, pull_rows))
    return (results.reshape(TOKENS, D).astype(jnp.bfloat16), row_grads.reshape(TOKENS, D).astype(jnp.bfloat16), totals[0], totals[1], totals[2], totals[3], totals[4], totals[5], totals[6], totals[7], totals[8], totals[9], totals[10], totals[11], totals[12], totals[13], totals[14])
```

```python
import functools

import jax
import jax.numpy as jnp
from jax import lax
from jax.sharding import PartitionSpec as P

HEADS = 12
SEQ = 512
LAYERS = 3


norm_epsilon = 1e-05


def product(left, right):
    return jnp.dot(left, right, preferred_element_type=jnp.float32)


def product_tn(left, right):
    return lax.dot_general(
        left, right, (((0,), (0,)), ((), ())), preferred_element_type=jnp.float32
    )


def product_nt(left, right):
    return lax.dot_general(
        left, right, (((1,), (1,)), ((), ())), preferred_element_type=jnp.float32
    )


def column_sums(values):
    return jnp.sum(values.astype(jnp.float32), axis=0)


def gelu_tanh(values):
    return jax.nn.gelu(values, approximate=True)


def layer_norm(summed, gain, shift):
    centre = summed - jnp.mean(summed, axis=-1, keepdims=True)
    inverse = lax.rsqrt(jnp.mean(centre * centre, axis=-1, keepdims=True) + norm_epsilon)
    normed = centre * inverse
    return (normed * gain.astype(jnp.float32) + shift.astype(jnp.float32), normed, inverse)


def norm_backward(upstream, normed, inverse, gain):
    scaled = upstream * gain.astype(jnp.float32)
    return inverse * (
        scaled
        - jnp.mean(scaled, axis=-1, keepdims=True)
        - normed * jnp.mean(scaled * normed, axis=-1, keepdims=True)
    )


def by_heads(rows):
    return rows.reshape(rows.shape[0], HEADS, rows.shape[1] // HEADS)


def by_sequence(rows):
    return rows.reshape(rows.shape[0] // SEQ, SEQ, rows.shape[1])


def flatten_rows(blocks):
    return blocks.reshape(-1, blocks.shape[-1])


def attend_forward(triple):
    query_rows, key_rows, value_rows = triple
    query_heads = by_heads(query_rows)
    key_heads = by_heads(key_rows)
    value_heads = by_heads(value_rows)
    scale = query_heads.shape[-1] ** (-0.5)
    scores = (
        jnp.einsum("qhd,khd->hqk", query_heads, key_heads, preferred_element_type=jnp.float32)
        * scale
    )
    top_score = jnp.max(scores, axis=-1, keepdims=True)
    weights = jnp.exp(scores - top_score)
    totals = jnp.sum(weights, axis=-1, keepdims=True)
    probs = (weights / totals).astype(jnp.bfloat16)
    context = jnp.einsum("hqk,khd->qhd", probs, value_heads, preferred_element_type=jnp.float32)
    return (context.reshape(query_rows.shape), (top_score + jnp.log(totals))[..., 0])


def attend_backward(packed):
    query_rows, key_rows, value_rows, log_total, context_grad = packed
    query_heads = by_heads(query_rows)
    key_heads = by_heads(key_rows)
    value_heads = by_heads(value_rows)
    grad_heads = by_heads(context_grad)
    scale = query_heads.shape[-1] ** (-0.5)
    scores = (
        jnp.einsum("qhd,khd->hqk", query_heads, key_heads, preferred_element_type=jnp.float32)
        * scale
    )
    probs = jnp.exp(scores - log_total[..., None])
    prob_grad = jnp.einsum(
        "qhd,khd->hqk", grad_heads, value_heads, preferred_element_type=jnp.float32
    )
    value_grad = jnp.einsum(
        "hqk,qhd->khd", probs.astype(jnp.bfloat16), grad_heads, preferred_element_type=jnp.float32
    )
    score_grad = (probs * (prob_grad - jnp.sum(probs * prob_grad, axis=-1, keepdims=True))).astype(
        jnp.bfloat16
    )
    query_grad = (
        jnp.einsum("hqk,khd->qhd", score_grad, key_heads, preferred_element_type=jnp.float32)
        * scale
    )
    key_grad = (
        jnp.einsum("hqk,qhd->khd", score_grad, query_heads, preferred_element_type=jnp.float32)
        * scale
    )
    row_shape = query_rows.shape
    return (
        query_grad.reshape(row_shape).astype(jnp.bfloat16),
        key_grad.reshape(row_shape).astype(jnp.bfloat16),
        value_grad.reshape(row_shape).astype(jnp.bfloat16),
    )


def layer_forward(weights, hidden_state):
    (
        query_weight,
        query_bias,
        key_weight,
        value_weight,
        value_bias,
        output_weight,
        output_bias,
        first_gain,
        first_shift,
        inner_weight,
        inner_bias,
        outer_weight,
        outer_bias,
        second_gain,
        second_shift,
    ) = weights
    rows_low = hidden_state.astype(jnp.bfloat16)
    query_rows = (product(rows_low, query_weight) + query_bias.astype(jnp.float32)).astype(
        jnp.bfloat16
    )
    key_rows = product(rows_low, key_weight).astype(jnp.bfloat16)
    value_rows = (product(rows_low, value_weight) + value_bias.astype(jnp.float32)).astype(
        jnp.bfloat16
    )
    context, log_total = jax.vmap(attend_forward)(
        (by_sequence(query_rows), by_sequence(key_rows), by_sequence(value_rows))
    )
    context_low = flatten_rows(context).astype(jnp.bfloat16)
    attended = product(context_low, output_weight) + output_bias.astype(jnp.float32)
    first_out, first_normed, first_inverse = layer_norm(
        hidden_state + attended, first_gain, first_shift
    )
    first_low = first_out.astype(jnp.bfloat16)
    inner_pre = product(first_low, inner_weight) + inner_bias.astype(jnp.float32)
    inner_low = gelu_tanh(inner_pre).astype(jnp.bfloat16)
    outer_out = product(inner_low, outer_weight) + outer_bias.astype(jnp.float32)
    result, second_normed, second_inverse = layer_norm(
        first_out + outer_out, second_gain, second_shift
    )
    kept_values = (
        rows_low,
        query_rows,
        key_rows,
        value_rows,
        log_total,
        context_low,
        first_normed,
        first_inverse,
        first_low,
        inner_pre,
        inner_low,
        second_normed,
        second_inverse,
    )
    return (result, kept_values)


def layer_backward(weights, kept_values, upstream):
    (
        query_weight,
        query_bias,
        key_weight,
        value_weight,
        value_bias,
        output_weight,
        output_bias,
        first_gain,
        first_shift,
        inner_weight,
        inner_bias,
        outer_weight,
        outer_bias,
        second_gain,
        second_shift,
    ) = weights
    (
        rows_low,
        query_rows,
        key_rows,
        value_rows,
        log_total,
        context_low,
        first_normed,
        first_inverse,
        first_low,
        inner_pre,
        inner_low,
        second_normed,
        second_inverse,
    ) = kept_values
    second_gain_grad = jnp.sum(upstream * second_normed, axis=0)
    second_shift_grad = jnp.sum(upstream, axis=0)
    second_grad = norm_backward(upstream, second_normed, second_inverse, second_gain)
    outer_low = second_grad.astype(jnp.bfloat16)
    outer_bias_grad = column_sums(outer_low)
    outer_weight_grad = product_tn(inner_low, outer_low)
    active_grad = product_nt(outer_low, outer_weight)
    gelu_pull = jax.vjp(gelu_tanh, inner_pre)[1]
    inner_grad = gelu_pull(active_grad)[0].astype(jnp.bfloat16)
    inner_bias_grad = column_sums(inner_grad)
    inner_weight_grad = product_tn(first_low, inner_grad)
    first_grad = second_grad + product_nt(inner_grad, inner_weight)
    first_gain_grad = jnp.sum(first_grad * first_normed, axis=0)
    first_shift_grad = jnp.sum(first_grad, axis=0)
    attended_grad = norm_backward(first_grad, first_normed, first_inverse, first_gain)
    attended_low = attended_grad.astype(jnp.bfloat16)
    output_bias_grad = column_sums(attended_low)
    output_weight_grad = product_tn(context_low, attended_low)
    context_grad = product_nt(attended_low, output_weight).astype(jnp.bfloat16)
    query_grad, key_grad, value_grad = jax.vmap(attend_backward)(
        (
            by_sequence(query_rows),
            by_sequence(key_rows),
            by_sequence(value_rows),
            log_total,
            by_sequence(context_grad),
        ),
    )
    query_grad = flatten_rows(query_grad)
    key_grad = flatten_rows(key_grad)
    value_grad = flatten_rows(value_grad)
    below_grad = (
        attended_grad
        + product_nt(query_grad, query_weight)
        + product_nt(key_grad, key_weight)
        + product_nt(value_grad, value_weight)
    )
    weight_grads = (
        product_tn(rows_low, query_grad),
        column_sums(query_grad),
        product_tn(rows_low, key_grad),
        product_tn(rows_low, value_grad),
        column_sums(value_grad),
        output_weight_grad,
        output_bias_grad,
        first_gain_grad,
        first_shift_grad,
        inner_weight_grad,
        inner_bias_grad,
        outer_weight_grad,
        outer_bias_grad,
        second_gain_grad,
        second_shift_grad,
    )
    return (below_grad, weight_grads)


AXES = ("dp", "fsdp")


def pack_weights(weights):
    (
        query_weight,
        query_bias,
        key_weight,
        value_weight,
        value_bias,
        output_weight,
        output_bias,
        first_gain,
        first_shift,
        inner_weight,
        inner_bias,
        outer_weight,
        outer_bias,
        second_gain,
        second_shift,
    ) = weights
    width = query_weight.shape[1]
    rows = query_weight.shape[0]
    vectors = jnp.concatenate(
        [
            query_bias,
            value_bias,
            output_bias,
            first_gain,
            first_shift,
            outer_bias,
            second_gain,
            second_shift,
            inner_bias,
        ]
    )
    vectors = jnp.pad(vectors, (0, width - vectors.shape[0]))[None, :]
    return jnp.concatenate(
        [
            query_weight,
            key_weight,
            value_weight,
            output_weight,
            inner_weight.reshape(-1, width),
            outer_weight,
            vectors,
        ],
        axis=0,
    )


def unpack_rows(packed, rows, ff_rows):
    width = packed.shape[-1]
    at = 0
    pieces = []
    for count in (rows, rows, rows, rows, ff_rows, ff_rows):
        pieces.append(packed[..., at : at + count, :])
        at += count
    vectors = packed[..., at, :]
    return pieces, vectors


def gather_weights(weights):
    rows = weights[0].shape[0]
    ff_rows = weights[11].shape[0]
    width = weights[0].shape[1]
    packed = lax.all_gather(pack_weights(weights), AXES, axis=0, tiled=False)
    shards = packed.shape[0]
    (qw, kw, vw, ow, iw, uw), vectors = unpack_rows(packed, rows, ff_rows)
    full_rows = shards * rows

    def square(piece):
        return piece.reshape(full_rows, width)

    inner_weight = iw.reshape(shards, rows, -1).reshape(full_rows, -1)
    outer_weight = uw.reshape(shards * ff_rows, width)
    at = 0
    found = []
    for count in (rows,) * 8 + (ff_rows,):
        found.append(vectors[:, at : at + count].reshape(-1))
        at += count
    (qb, vb, ob, g1, s1, ub, g2, s2, ib) = found
    return (
        square(qw),
        qb,
        square(kw),
        square(vw),
        vb,
        square(ow),
        ob,
        g1,
        s1,
        inner_weight,
        ib,
        outer_weight,
        ub,
        g2,
        s2,
    )


def scatter_grads(grads, shards):
    (
        query_weight_grad,
        query_bias_grad,
        key_weight_grad,
        value_weight_grad,
        value_bias_grad,
        output_weight_grad,
        output_bias_grad,
        first_gain_grad,
        first_shift_grad,
        inner_weight_grad,
        inner_bias_grad,
        outer_weight_grad,
        outer_bias_grad,
        second_gain_grad,
        second_shift_grad,
    ) = grads
    width = query_weight_grad.shape[1]
    rows = query_weight_grad.shape[0] // shards
    ff_rows = outer_weight_grad.shape[0] // shards

    def blocks(grad):
        return grad.reshape(shards, -1, width)

    vectors = jnp.concatenate(
        [
            v.reshape(shards, -1)
            for v in (
                query_bias_grad,
                value_bias_grad,
                output_bias_grad,
                first_gain_grad,
                first_shift_grad,
                outer_bias_grad,
                second_gain_grad,
                second_shift_grad,
                inner_bias_grad,
            )
        ],
        axis=1,
    )
    vectors = jnp.pad(vectors, ((0, 0), (0, width - vectors.shape[1])))[:, None, :]
    packed = jnp.concatenate(
        [
            blocks(query_weight_grad),
            blocks(key_weight_grad),
            blocks(value_weight_grad),
            blocks(output_weight_grad),
            blocks(inner_weight_grad.reshape(shards, rows, -1)),
            blocks(outer_weight_grad),
            vectors,
        ],
        axis=1,
    )
    mine = lax.psum_scatter(packed, AXES, scatter_dimension=0, tiled=True)[0]
    (qw, kw, vw, ow, iw, uw), vec = unpack_rows(mine, rows, ff_rows)
    at = 0
    found = []
    for count in (rows,) * 8 + (ff_rows,):
        found.append(vec[at : at + count])
        at += count
    (qb, vb, ob, g1, s1, ub, g2, s2, ib) = found
    return (
        qw,
        qb,
        kw,
        vw,
        vb,
        ow,
        ob,
        g1,
        s1,
        iw.reshape(rows, -1),
        ib,
        uw,
        ub,
        g2,
        s2,
    )


def per_device(
    shards,
    inputs,
    cotangent,
    masked,
    *weights,
):
    resident = gather_weights(weights)
    hidden_state = inputs.astype(jnp.float32)
    kept = []
    for applied in range(LAYERS):
        hidden_state, kept_values = layer_forward(resident, hidden_state)
        kept.append(kept_values)
    outputs = hidden_state.astype(jnp.bfloat16)
    upstream = cotangent.astype(jnp.float32) * masked.reshape(-1, 1).astype(jnp.float32)
    collected = None
    for applied in range(LAYERS - 1, -1, -1):
        upstream, weight_grads = layer_backward(resident, kept[applied], upstream)
        collected = (
            weight_grads
            if collected is None
            else tuple((earlier + later for earlier, later in zip(collected, weight_grads)))
        )
    collected = scatter_grads(collected, shards)
    return (outputs, upstream.astype(jnp.bfloat16)) + tuple(collected)


def solution(mesh):
    in_specs = (
        P(("dp", "fsdp"), None),
        P(("dp", "fsdp"), None),
        P(("dp", "fsdp"), None),
        P(("dp", "fsdp"), None),
        P(("dp", "fsdp")),
        P(("dp", "fsdp"), None),
        P(("dp", "fsdp"), None),
        P(("dp", "fsdp")),
        P(("dp", "fsdp"), None),
        P(("dp", "fsdp")),
        P(("dp", "fsdp")),
        P(("dp", "fsdp")),
        P(("dp", "fsdp"), None),
        P(("dp", "fsdp")),
        P(("dp", "fsdp"), None),
        P(("dp", "fsdp")),
        P(("dp", "fsdp")),
        P(("dp", "fsdp")),
    )
    out_specs = (
        P(("dp", "fsdp"), None),
        P(("dp", "fsdp"), None),
        P(("dp", "fsdp"), None),
        P(("dp", "fsdp")),
        P(("dp", "fsdp"), None),
        P(("dp", "fsdp"), None),
        P(("dp", "fsdp")),
        P(("dp", "fsdp"), None),
        P(("dp", "fsdp")),
        P(("dp", "fsdp")),
        P(("dp", "fsdp")),
        P(("dp", "fsdp"), None),
        P(("dp", "fsdp")),
        P(("dp", "fsdp"), None),
        P(("dp", "fsdp")),
        P(("dp", "fsdp")),
        P(("dp", "fsdp")),
    )
    shards = mesh.shape["dp"] * mesh.shape["fsdp"]
    return jax.shard_map(
        functools.partial(per_device, shards), mesh=mesh, in_specs=in_specs, out_specs=out_specs, check_vma=False
    )
```

```python
import functools

import jax
import jax.numpy as jnp
from jax import lax
from jax.sharding import PartitionSpec as P

HEADS = 12
SEQ = 512
LAYERS = 3


norm_epsilon = 1e-05


def product(left, right):
    return jnp.dot(left, right, preferred_element_type=jnp.float32)


def product_tn(left, right):
    return lax.dot_general(
        left, right, (((0,), (0,)), ((), ())), preferred_element_type=jnp.float32
    )


def product_nt(left, right):
    return lax.dot_general(
        left, right, (((1,), (1,)), ((), ())), preferred_element_type=jnp.float32
    )


def column_sums(values):
    return jnp.sum(values.astype(jnp.float32), axis=0)


def gelu_tanh(values):
    return jax.nn.gelu(values, approximate=True)


def layer_norm(summed, gain, shift):
    centre = summed - jnp.mean(summed, axis=-1, keepdims=True)
    inverse = lax.rsqrt(jnp.mean(centre * centre, axis=-1, keepdims=True) + norm_epsilon)
    normed = centre * inverse
    return (normed * gain.astype(jnp.float32) + shift.astype(jnp.float32), normed, inverse)


def norm_backward(upstream, normed, inverse, gain):
    scaled = upstream * gain.astype(jnp.float32)
    return inverse * (
        scaled
        - jnp.mean(scaled, axis=-1, keepdims=True)
        - normed * jnp.mean(scaled * normed, axis=-1, keepdims=True)
    )


def by_heads(rows):
    return rows.reshape(rows.shape[0], HEADS, rows.shape[1] // HEADS)


def by_sequence(rows):
    return rows.reshape(rows.shape[0] // SEQ, SEQ, rows.shape[1])


def flatten_rows(blocks):
    return blocks.reshape(-1, blocks.shape[-1])


def attend_forward(triple):
    query_rows, key_rows, value_rows = triple
    query_heads = by_heads(query_rows)
    key_heads = by_heads(key_rows)
    value_heads = by_heads(value_rows)
    scale = query_heads.shape[-1] ** (-0.5)
    scores = (
        jnp.einsum("qhd,khd->hqk", query_heads, key_heads, preferred_element_type=jnp.float32)
        * scale
    )
    top_score = jnp.max(scores, axis=-1, keepdims=True)
    weights = jnp.exp(scores - top_score)
    totals = jnp.sum(weights, axis=-1, keepdims=True)
    probs = (weights / totals).astype(jnp.bfloat16)
    context = jnp.einsum("hqk,khd->qhd", probs, value_heads, preferred_element_type=jnp.float32)
    return (context.reshape(query_rows.shape), (top_score + jnp.log(totals))[..., 0])


def attend_backward(packed):
    query_rows, key_rows, value_rows, log_total, context_grad = packed
    query_heads = by_heads(query_rows)
    key_heads = by_heads(key_rows)
    value_heads = by_heads(value_rows)
    grad_heads = by_heads(context_grad)
    scale = query_heads.shape[-1] ** (-0.5)
    scores = (
        jnp.einsum("qhd,khd->hqk", query_heads, key_heads, preferred_element_type=jnp.float32)
        * scale
    )
    probs = jnp.exp(scores - log_total[..., None])
    prob_grad = jnp.einsum(
        "qhd,khd->hqk", grad_heads, value_heads, preferred_element_type=jnp.float32
    )
    value_grad = jnp.einsum(
        "hqk,qhd->khd", probs.astype(jnp.bfloat16), grad_heads, preferred_element_type=jnp.float32
    )
    score_grad = (probs * (prob_grad - jnp.sum(probs * prob_grad, axis=-1, keepdims=True))).astype(
        jnp.bfloat16
    )
    query_grad = (
        jnp.einsum("hqk,khd->qhd", score_grad, key_heads, preferred_element_type=jnp.float32)
        * scale
    )
    key_grad = (
        jnp.einsum("hqk,qhd->khd", score_grad, query_heads, preferred_element_type=jnp.float32)
        * scale
    )
    row_shape = query_rows.shape
    return (
        query_grad.reshape(row_shape).astype(jnp.bfloat16),
        key_grad.reshape(row_shape).astype(jnp.bfloat16),
        value_grad.reshape(row_shape).astype(jnp.bfloat16),
    )


def layer_forward(weights, hidden_state):
    (
        query_weight,
        query_bias,
        key_weight,
        value_weight,
        value_bias,
        output_weight,
        output_bias,
        first_gain,
        first_shift,
        inner_weight,
        inner_bias,
        outer_weight,
        outer_bias,
        second_gain,
        second_shift,
    ) = weights
    rows_low = hidden_state.astype(jnp.bfloat16)
    query_rows = (product(rows_low, query_weight) + query_bias.astype(jnp.float32)).astype(
        jnp.bfloat16
    )
    key_rows = product(rows_low, key_weight).astype(jnp.bfloat16)
    value_rows = (product(rows_low, value_weight) + value_bias.astype(jnp.float32)).astype(
        jnp.bfloat16
    )
    context, log_total = jax.vmap(attend_forward)(
        (by_sequence(query_rows), by_sequence(key_rows), by_sequence(value_rows))
    )
    context_low = flatten_rows(context).astype(jnp.bfloat16)
    attended = product(context_low, output_weight) + output_bias.astype(jnp.float32)
    first_out, first_normed, first_inverse = layer_norm(
        hidden_state + attended, first_gain, first_shift
    )
    first_low = first_out.astype(jnp.bfloat16)
    inner_pre = product(first_low, inner_weight) + inner_bias.astype(jnp.float32)
    inner_low = gelu_tanh(inner_pre).astype(jnp.bfloat16)
    outer_out = product(inner_low, outer_weight) + outer_bias.astype(jnp.float32)
    result, second_normed, second_inverse = layer_norm(
        first_out + outer_out, second_gain, second_shift
    )
    kept_values = (
        rows_low,
        query_rows,
        key_rows,
        value_rows,
        log_total,
        context_low,
        first_normed,
        first_inverse,
        first_low,
        inner_pre,
        inner_low,
        second_normed,
        second_inverse,
    )
    return (result, kept_values)


def layer_backward(weights, kept_values, upstream):
    (
        query_weight,
        query_bias,
        key_weight,
        value_weight,
        value_bias,
        output_weight,
        output_bias,
        first_gain,
        first_shift,
        inner_weight,
        inner_bias,
        outer_weight,
        outer_bias,
        second_gain,
        second_shift,
    ) = weights
    (
        rows_low,
        query_rows,
        key_rows,
        value_rows,
        log_total,
        context_low,
        first_normed,
        first_inverse,
        first_low,
        inner_pre,
        inner_low,
        second_normed,
        second_inverse,
    ) = kept_values
    second_gain_grad = jnp.sum(upstream * second_normed, axis=0)
    second_shift_grad = jnp.sum(upstream, axis=0)
    second_grad = norm_backward(upstream, second_normed, second_inverse, second_gain)
    outer_low = second_grad.astype(jnp.bfloat16)
    outer_bias_grad = column_sums(outer_low)
    outer_weight_grad = product_tn(inner_low, outer_low)
    active_grad = product_nt(outer_low, outer_weight)
    gelu_pull = jax.vjp(gelu_tanh, inner_pre)[1]
    inner_grad = gelu_pull(active_grad)[0].astype(jnp.bfloat16)
    inner_bias_grad = column_sums(inner_grad)
    inner_weight_grad = product_tn(first_low, inner_grad)
    first_grad = second_grad + product_nt(inner_grad, inner_weight)
    first_gain_grad = jnp.sum(first_grad * first_normed, axis=0)
    first_shift_grad = jnp.sum(first_grad, axis=0)
    attended_grad = norm_backward(first_grad, first_normed, first_inverse, first_gain)
    attended_low = attended_grad.astype(jnp.bfloat16)
    output_bias_grad = column_sums(attended_low)
    output_weight_grad = product_tn(context_low, attended_low)
    context_grad = product_nt(attended_low, output_weight).astype(jnp.bfloat16)
    query_grad, key_grad, value_grad = jax.vmap(attend_backward)(
        (
            by_sequence(query_rows),
            by_sequence(key_rows),
            by_sequence(value_rows),
            log_total,
            by_sequence(context_grad),
        ),
    )
    query_grad = flatten_rows(query_grad)
    key_grad = flatten_rows(key_grad)
    value_grad = flatten_rows(value_grad)
    below_grad = (
        attended_grad
        + product_nt(query_grad, query_weight)
        + product_nt(key_grad, key_weight)
        + product_nt(value_grad, value_weight)
    )
    weight_grads = (
        product_tn(rows_low, query_grad),
        column_sums(query_grad),
        product_tn(rows_low, key_grad),
        product_tn(rows_low, value_grad),
        column_sums(value_grad),
        output_weight_grad,
        output_bias_grad,
        first_gain_grad,
        first_shift_grad,
        inner_weight_grad,
        inner_bias_grad,
        outer_weight_grad,
        outer_bias_grad,
        second_gain_grad,
        second_shift_grad,
    )
    return (below_grad, weight_grads)


AXES = ("dp", "fsdp")


def pack_weights(weights):
    (
        query_weight,
        query_bias,
        key_weight,
        value_weight,
        value_bias,
        output_weight,
        output_bias,
        first_gain,
        first_shift,
        inner_weight,
        inner_bias,
        outer_weight,
        outer_bias,
        second_gain,
        second_shift,
    ) = weights
    width = query_weight.shape[1]
    rows = query_weight.shape[0]
    vectors = jnp.concatenate(
        [
            query_bias,
            value_bias,
            output_bias,
            first_gain,
            first_shift,
            outer_bias,
            second_gain,
            second_shift,
            inner_bias,
        ]
    )
    vectors = jnp.pad(vectors, (0, width - vectors.shape[0]))[None, :]
    return jnp.concatenate(
        [
            query_weight,
            key_weight,
            value_weight,
            output_weight,
            inner_weight.reshape(-1, width),
            outer_weight,
            vectors,
        ],
        axis=0,
    )


def unpack_rows(packed, rows, ff_rows):
    width = packed.shape[-1]
    at = 0
    pieces = []
    for count in (rows, rows, rows, rows, ff_rows, ff_rows):
        pieces.append(packed[..., at : at + count, :])
        at += count
    vectors = packed[..., at, :]
    return pieces, vectors


def gather_weights(weights):
    rows = weights[0].shape[0]
    ff_rows = weights[11].shape[0]
    width = weights[0].shape[1]
    packed = lax.all_gather(pack_weights(weights), AXES, axis=0, tiled=False)
    shards = packed.shape[0]
    (qw, kw, vw, ow, iw, uw), vectors = unpack_rows(packed, rows, ff_rows)
    full_rows = shards * rows

    def square(piece):
        return piece.reshape(full_rows, width)

    inner_weight = iw.reshape(shards, rows, -1).reshape(full_rows, -1)
    outer_weight = uw.reshape(shards * ff_rows, width)
    at = 0
    found = []
    for count in (rows,) * 8 + (ff_rows,):
        found.append(vectors[:, at : at + count].reshape(-1))
        at += count
    (qb, vb, ob, g1, s1, ub, g2, s2, ib) = found
    return (
        square(qw),
        qb,
        square(kw),
        square(vw),
        vb,
        square(ow),
        ob,
        g1,
        s1,
        inner_weight,
        ib,
        outer_weight,
        ub,
        g2,
        s2,
    )


def scatter_grads(grads, shards):
    (
        query_weight_grad,
        query_bias_grad,
        key_weight_grad,
        value_weight_grad,
        value_bias_grad,
        output_weight_grad,
        output_bias_grad,
        first_gain_grad,
        first_shift_grad,
        inner_weight_grad,
        inner_bias_grad,
        outer_weight_grad,
        outer_bias_grad,
        second_gain_grad,
        second_shift_grad,
    ) = grads
    width = query_weight_grad.shape[1]
    rows = query_weight_grad.shape[0] // shards
    ff_rows = outer_weight_grad.shape[0] // shards

    def blocks(grad):
        return grad.reshape(shards, -1, width)

    vectors = jnp.concatenate(
        [
            v.reshape(shards, -1)
            for v in (
                query_bias_grad,
                value_bias_grad,
                output_bias_grad,
                first_gain_grad,
                first_shift_grad,
                outer_bias_grad,
                second_gain_grad,
                second_shift_grad,
                inner_bias_grad,
            )
        ],
        axis=1,
    )
    vectors = jnp.pad(vectors, ((0, 0), (0, width - vectors.shape[1])))[:, None, :]
    packed = jnp.concatenate(
        [
            blocks(query_weight_grad),
            blocks(key_weight_grad),
            blocks(value_weight_grad),
            blocks(output_weight_grad),
            blocks(inner_weight_grad.reshape(shards, rows, -1)),
            blocks(outer_weight_grad),
            vectors,
        ],
        axis=1,
    )
    mine = lax.psum_scatter(
        packed.astype(jnp.bfloat16), AXES, scatter_dimension=0, tiled=True
    )[0].astype(jnp.float32)
    (qw, kw, vw, ow, iw, uw), vec = unpack_rows(mine, rows, ff_rows)
    at = 0
    found = []
    for count in (rows,) * 8 + (ff_rows,):
        found.append(vec[at : at + count])
        at += count
    (qb, vb, ob, g1, s1, ub, g2, s2, ib) = found
    return (
        qw,
        qb,
        kw,
        vw,
        vb,
        ow,
        ob,
        g1,
        s1,
        iw.reshape(rows, -1),
        ib,
        uw,
        ub,
        g2,
        s2,
    )


def per_device(
    shards,
    inputs,
    cotangent,
    masked,
    *weights,
):
    resident = gather_weights(weights)
    hidden_state = inputs.astype(jnp.float32)
    kept = []
    for applied in range(LAYERS):
        hidden_state, kept_values = layer_forward(resident, hidden_state)
        kept.append(kept_values)
    outputs = hidden_state.astype(jnp.bfloat16)
    upstream = cotangent.astype(jnp.float32) * masked.reshape(-1, 1).astype(jnp.float32)
    collected = None
    for applied in range(LAYERS - 1, -1, -1):
        upstream, weight_grads = layer_backward(resident, kept[applied], upstream)
        collected = (
            weight_grads
            if collected is None
            else tuple((earlier + later for earlier, later in zip(collected, weight_grads)))
        )
    collected = scatter_grads(collected, shards)
    return (outputs, upstream.astype(jnp.bfloat16)) + tuple(collected)


def solution(mesh):
    in_specs = (
        P(("dp", "fsdp"), None),
        P(("dp", "fsdp"), None),
        P(("dp", "fsdp"), None),
        P(("dp", "fsdp"), None),
        P(("dp", "fsdp")),
        P(("dp", "fsdp"), None),
        P(("dp", "fsdp"), None),
        P(("dp", "fsdp")),
        P(("dp", "fsdp"), None),
        P(("dp", "fsdp")),
        P(("dp", "fsdp")),
        P(("dp", "fsdp")),
        P(("dp", "fsdp"), None),
        P(("dp", "fsdp")),
        P(("dp", "fsdp"), None),
        P(("dp", "fsdp")),
        P(("dp", "fsdp")),
        P(("dp", "fsdp")),
    )
    out_specs = (
        P(("dp", "fsdp"), None),
        P(("dp", "fsdp"), None),
        P(("dp", "fsdp"), None),
        P(("dp", "fsdp")),
        P(("dp", "fsdp"), None),
        P(("dp", "fsdp"), None),
        P(("dp", "fsdp")),
        P(("dp", "fsdp"), None),
        P(("dp", "fsdp")),
        P(("dp", "fsdp")),
        P(("dp", "fsdp")),
        P(("dp", "fsdp"), None),
        P(("dp", "fsdp")),
        P(("dp", "fsdp"), None),
        P(("dp", "fsdp")),
        P(("dp", "fsdp")),
        P(("dp", "fsdp")),
    )
    shards = mesh.shape["dp"] * mesh.shape["fsdp"]
    return jax.shard_map(
        functools.partial(per_device, shards), mesh=mesh, in_specs=in_specs, out_specs=out_specs, check_vma=False
    )
```

```python
import functools

import jax
import jax.numpy as jnp
from jax import lax
from jax.sharding import PartitionSpec as P

from jax.experimental import pallas as pl
from jax.experimental.pallas import tpu as pltpu

HEADS = 12
SEQ = 512
LAYERS = 3


norm_epsilon = 1e-05


def product(left, right):
    return jnp.dot(left, right, preferred_element_type=jnp.float32)


def product_tn(left, right):
    return lax.dot_general(
        left, right, (((0,), (0,)), ((), ())), preferred_element_type=jnp.float32
    )


def product_nt(left, right):
    return lax.dot_general(
        left, right, (((1,), (1,)), ((), ())), preferred_element_type=jnp.float32
    )


def column_sums(values):
    return jnp.sum(values.astype(jnp.float32), axis=0)


def gelu_tanh(values):
    return jax.nn.gelu(values, approximate=True)


def layer_norm(summed, gain, shift):
    centre = summed - jnp.mean(summed, axis=-1, keepdims=True)
    inverse = lax.rsqrt(jnp.mean(centre * centre, axis=-1, keepdims=True) + norm_epsilon)
    normed = centre * inverse
    return (normed * gain.astype(jnp.float32) + shift.astype(jnp.float32), normed, inverse)


def norm_backward(upstream, normed, inverse, gain):
    scaled = upstream * gain.astype(jnp.float32)
    return inverse * (
        scaled
        - jnp.mean(scaled, axis=-1, keepdims=True)
        - normed * jnp.mean(scaled * normed, axis=-1, keepdims=True)
    )


def by_heads(rows):
    return rows.reshape(rows.shape[0], HEADS, rows.shape[1] // HEADS)


def by_sequence(rows):
    return rows.reshape(rows.shape[0] // SEQ, SEQ, rows.shape[1])


def flatten_rows(blocks):
    return blocks.reshape(-1, blocks.shape[-1])


HEAD = 64
PAIR = 128
NT = (((1,), (1,)), ((), ()))
TN = (((0,), (0,)), ((), ()))


def _head_masks(shape):
    lane = lax.broadcasted_iota(jnp.int32, shape, 1)
    first = lane < HEAD
    return first, jnp.logical_not(first)


def attention_forward_kernel(q_ref, k_ref, v_ref, ctx_ref, lt_ref):
    scale = HEAD ** (-0.5)
    q = q_ref[...]
    k = k_ref[...]
    v = v_ref[...]
    masks = _head_masks(q.shape)
    zero = jnp.zeros_like(q)
    context = None
    total = None
    for mask in masks:
        scores = lax.dot_general(
            jnp.where(mask, q, zero), k, NT, preferred_element_type=jnp.float32
        ) * scale
        top = jnp.max(scores, axis=-1, keepdims=True)
        weights = jnp.exp(scores - top)
        sums = jnp.sum(weights, axis=-1, keepdims=True)
        probs = (weights / sums).astype(jnp.bfloat16)
        part = jnp.dot(probs, v, preferred_element_type=jnp.float32)
        log_total = jnp.broadcast_to(top + jnp.log(sums), part.shape)
        context = part if context is None else jnp.where(mask, part, context)
        total = log_total if total is None else jnp.where(mask, log_total, total)
    ctx_ref[...] = context.astype(ctx_ref.dtype)
    lt_ref[...] = total


def attention_backward_kernel(q_ref, k_ref, v_ref, lt_ref, g_ref, dq_ref, dk_ref, dv_ref):
    scale = HEAD ** (-0.5)
    q = q_ref[...]
    k = k_ref[...]
    v = v_ref[...]
    g = g_ref[...]
    lt_all = lt_ref[...]
    masks = _head_masks(q.shape)
    zero = jnp.zeros_like(q)
    dq = dk = dv = None
    for mask in masks:
        scores = lax.dot_general(
            jnp.where(mask, q, zero), k, NT, preferred_element_type=jnp.float32
        ) * scale
        lt = jnp.max(jnp.where(mask, lt_all, -jnp.inf), axis=-1, keepdims=True)
        probs = jnp.exp(scores - lt)
        prob_grad = lax.dot_general(
            jnp.where(mask, g, zero), v, NT, preferred_element_type=jnp.float32
        )
        value_part = lax.dot_general(
            probs.astype(jnp.bfloat16), g, TN, preferred_element_type=jnp.float32
        )
        score_grad = (
            probs * (prob_grad - jnp.sum(probs * prob_grad, axis=-1, keepdims=True))
        ).astype(jnp.bfloat16)
        query_part = jnp.dot(score_grad, k, preferred_element_type=jnp.float32) * scale
        key_part = lax.dot_general(score_grad, q, TN, preferred_element_type=jnp.float32) * scale
        if dq is None:
            dq, dk, dv = query_part, key_part, value_part
        else:
            dq = jnp.where(mask, query_part, dq)
            dk = jnp.where(mask, key_part, dk)
            dv = jnp.where(mask, value_part, dv)
    dq_ref[...] = dq.astype(dq_ref.dtype)
    dk_ref[...] = dk.astype(dk_ref.dtype)
    dv_ref[...] = dv.astype(dv_ref.dtype)


def _grid(rows):
    tokens, width = rows.shape
    return (tokens // SEQ, width // PAIR)


def _spec():
    return pl.BlockSpec((SEQ, PAIR), lambda s, h: (s, h))


def attention_forward(query_rows, key_rows, value_rows):
    tokens, width = query_rows.shape
    grid = _grid(query_rows)
    steps = grid[0] * grid[1]
    flops = steps * 2 * (2 * 2 * SEQ * SEQ * PAIR)
    return pl.pallas_call(
        attention_forward_kernel,
        grid=grid,
        in_specs=[_spec(), _spec(), _spec()],
        out_specs=[_spec(), _spec()],
        out_shape=[
            jax.ShapeDtypeStruct((tokens, width), jnp.bfloat16),
            jax.ShapeDtypeStruct((tokens, width), jnp.float32),
        ],
        compiler_params=pltpu.CompilerParams(dimension_semantics=("parallel", "parallel")),
        cost_estimate=pl.CostEstimate(
            flops=flops, transcendentals=steps * 2 * SEQ * SEQ, bytes_accessed=tokens * width * 12
        ),
        name="attention_forward",
    )(query_rows, key_rows, value_rows)


def attention_backward(query_rows, key_rows, value_rows, log_total, context_grad):
    tokens, width = query_rows.shape
    grid = _grid(query_rows)
    steps = grid[0] * grid[1]
    flops = steps * 2 * (5 * 2 * SEQ * SEQ * PAIR)
    shape = jax.ShapeDtypeStruct((tokens, width), jnp.bfloat16)
    return pl.pallas_call(
        attention_backward_kernel,
        grid=grid,
        in_specs=[_spec()] * 5,
        out_specs=[_spec()] * 3,
        out_shape=[shape, shape, shape],
        compiler_params=pltpu.CompilerParams(dimension_semantics=("parallel", "parallel")),
        cost_estimate=pl.CostEstimate(
            flops=flops, transcendentals=steps * 2 * SEQ * SEQ, bytes_accessed=tokens * width * 18
        ),
        name="attention_backward",
    )(query_rows, key_rows, value_rows, log_total, context_grad)


def layer_forward(weights, hidden_state):
    (
        query_weight,
        query_bias,
        key_weight,
        value_weight,
        value_bias,
        output_weight,
        output_bias,
        first_gain,
        first_shift,
        inner_weight,
        inner_bias,
        outer_weight,
        outer_bias,
        second_gain,
        second_shift,
    ) = weights
    rows_low = hidden_state.astype(jnp.bfloat16)
    query_rows = (product(rows_low, query_weight) + query_bias.astype(jnp.float32)).astype(
        jnp.bfloat16
    )
    key_rows = product(rows_low, key_weight).astype(jnp.bfloat16)
    value_rows = (product(rows_low, value_weight) + value_bias.astype(jnp.float32)).astype(
        jnp.bfloat16
    )
    context_low, log_total = attention_forward(query_rows, key_rows, value_rows)
    attended = product(context_low, output_weight) + output_bias.astype(jnp.float32)
    first_out, first_normed, first_inverse = layer_norm(
        hidden_state + attended, first_gain, first_shift
    )
    first_low = first_out.astype(jnp.bfloat16)
    inner_pre = product(first_low, inner_weight) + inner_bias.astype(jnp.float32)
    inner_low = gelu_tanh(inner_pre).astype(jnp.bfloat16)
    outer_out = product(inner_low, outer_weight) + outer_bias.astype(jnp.float32)
    result, second_normed, second_inverse = layer_norm(
        first_out + outer_out, second_gain, second_shift
    )
    kept_values = (
        rows_low,
        query_rows,
        key_rows,
        value_rows,
        log_total,
        context_low,
        first_normed,
        first_inverse,
        first_low,
        inner_pre,
        inner_low,
        second_normed,
        second_inverse,
    )
    return (result, kept_values)


def layer_backward(weights, kept_values, upstream):
    (
        query_weight,
        query_bias,
        key_weight,
        value_weight,
        value_bias,
        output_weight,
        output_bias,
        first_gain,
        first_shift,
        inner_weight,
        inner_bias,
        outer_weight,
        outer_bias,
        second_gain,
        second_shift,
    ) = weights
    (
        rows_low,
        query_rows,
        key_rows,
        value_rows,
        log_total,
        context_low,
        first_normed,
        first_inverse,
        first_low,
        inner_pre,
        inner_low,
        second_normed,
        second_inverse,
    ) = kept_values
    second_gain_grad = jnp.sum(upstream * second_normed, axis=0)
    second_shift_grad = jnp.sum(upstream, axis=0)
    second_grad = norm_backward(upstream, second_normed, second_inverse, second_gain)
    outer_low = second_grad.astype(jnp.bfloat16)
    outer_bias_grad = column_sums(outer_low)
    outer_weight_grad = product_tn(inner_low, outer_low)
    active_grad = product_nt(outer_low, outer_weight)
    gelu_pull = jax.vjp(gelu_tanh, inner_pre)[1]
    inner_grad = gelu_pull(active_grad)[0].astype(jnp.bfloat16)
    inner_bias_grad = column_sums(inner_grad)
    inner_weight_grad = product_tn(first_low, inner_grad)
    first_grad = second_grad + product_nt(inner_grad, inner_weight)
    first_gain_grad = jnp.sum(first_grad * first_normed, axis=0)
    first_shift_grad = jnp.sum(first_grad, axis=0)
    attended_grad = norm_backward(first_grad, first_normed, first_inverse, first_gain)
    attended_low = attended_grad.astype(jnp.bfloat16)
    output_bias_grad = column_sums(attended_low)
    output_weight_grad = product_tn(context_low, attended_low)
    context_grad = product_nt(attended_low, output_weight).astype(jnp.bfloat16)
    query_grad, key_grad, value_grad = attention_backward(
        query_rows, key_rows, value_rows, log_total, context_grad
    )
    below_grad = (
        attended_grad
        + product_nt(query_grad, query_weight)
        + product_nt(key_grad, key_weight)
        + product_nt(value_grad, value_weight)
    )
    weight_grads = (
        product_tn(rows_low, query_grad),
        column_sums(query_grad),
        product_tn(rows_low, key_grad),
        product_tn(rows_low, value_grad),
        column_sums(value_grad),
        output_weight_grad,
        output_bias_grad,
        first_gain_grad,
        first_shift_grad,
        inner_weight_grad,
        inner_bias_grad,
        outer_weight_grad,
        outer_bias_grad,
        second_gain_grad,
        second_shift_grad,
    )
    return (below_grad, weight_grads)


AXES = ("dp", "fsdp")


def pack_weights(weights):
    (
        query_weight,
        query_bias,
        key_weight,
        value_weight,
        value_bias,
        output_weight,
        output_bias,
        first_gain,
        first_shift,
        inner_weight,
        inner_bias,
        outer_weight,
        outer_bias,
        second_gain,
        second_shift,
    ) = weights
    width = query_weight.shape[1]
    rows = query_weight.shape[0]
    vectors = jnp.concatenate(
        [
            query_bias,
            value_bias,
            output_bias,
            first_gain,
            first_shift,
            outer_bias,
            second_gain,
            second_shift,
            inner_bias,
        ]
    )
    vectors = jnp.pad(vectors, (0, width - vectors.shape[0]))[None, :]
    return jnp.concatenate(
        [
            query_weight,
            key_weight,
            value_weight,
            output_weight,
            inner_weight.reshape(-1, width),
            outer_weight,
            vectors,
        ],
        axis=0,
    )


def unpack_rows(packed, rows, ff_rows):
    width = packed.shape[-1]
    at = 0
    pieces = []
    for count in (rows, rows, rows, rows, ff_rows, ff_rows):
        pieces.append(packed[..., at : at + count, :])
        at += count
    vectors = packed[..., at, :]
    return pieces, vectors


def gather_weights(weights):
    rows = weights[0].shape[0]
    ff_rows = weights[11].shape[0]
    width = weights[0].shape[1]
    packed = lax.all_gather(pack_weights(weights), AXES, axis=0, tiled=False)
    shards = packed.shape[0]
    (qw, kw, vw, ow, iw, uw), vectors = unpack_rows(packed, rows, ff_rows)
    full_rows = shards * rows

    def square(piece):
        return piece.reshape(full_rows, width)

    inner_weight = iw.reshape(shards, rows, -1).reshape(full_rows, -1)
    outer_weight = uw.reshape(shards * ff_rows, width)
    at = 0
    found = []
    for count in (rows,) * 8 + (ff_rows,):
        found.append(vectors[:, at : at + count].reshape(-1))
        at += count
    (qb, vb, ob, g1, s1, ub, g2, s2, ib) = found
    return (
        square(qw),
        qb,
        square(kw),
        square(vw),
        vb,
        square(ow),
        ob,
        g1,
        s1,
        inner_weight,
        ib,
        outer_weight,
        ub,
        g2,
        s2,
    )


def scatter_grads(grads, shards):
    (
        query_weight_grad,
        query_bias_grad,
        key_weight_grad,
        value_weight_grad,
        value_bias_grad,
        output_weight_grad,
        output_bias_grad,
        first_gain_grad,
        first_shift_grad,
        inner_weight_grad,
        inner_bias_grad,
        outer_weight_grad,
        outer_bias_grad,
        second_gain_grad,
        second_shift_grad,
    ) = grads
    width = query_weight_grad.shape[1]
    rows = query_weight_grad.shape[0] // shards
    ff_rows = outer_weight_grad.shape[0] // shards

    def blocks(grad):
        return grad.reshape(shards, -1, width)

    vectors = jnp.concatenate(
        [
            v.reshape(shards, -1)
            for v in (
                query_bias_grad,
                value_bias_grad,
                output_bias_grad,
                first_gain_grad,
                first_shift_grad,
                outer_bias_grad,
                second_gain_grad,
                second_shift_grad,
                inner_bias_grad,
            )
        ],
        axis=1,
    )
    vectors = jnp.pad(vectors, ((0, 0), (0, width - vectors.shape[1])))[:, None, :]
    packed = jnp.concatenate(
        [
            blocks(query_weight_grad),
            blocks(key_weight_grad),
            blocks(value_weight_grad),
            blocks(output_weight_grad),
            blocks(inner_weight_grad.reshape(shards, rows, -1)),
            blocks(outer_weight_grad),
            vectors,
        ],
        axis=1,
    )
    mine = lax.psum_scatter(
        packed.astype(jnp.bfloat16), AXES, scatter_dimension=0, tiled=True
    )[0].astype(jnp.float32)
    (qw, kw, vw, ow, iw, uw), vec = unpack_rows(mine, rows, ff_rows)
    at = 0
    found = []
    for count in (rows,) * 8 + (ff_rows,):
        found.append(vec[at : at + count])
        at += count
    (qb, vb, ob, g1, s1, ub, g2, s2, ib) = found
    return (
        qw,
        qb,
        kw,
        vw,
        vb,
        ow,
        ob,
        g1,
        s1,
        iw.reshape(rows, -1),
        ib,
        uw,
        ub,
        g2,
        s2,
    )


def per_device(
    shards,
    inputs,
    cotangent,
    masked,
    *weights,
):
    resident = gather_weights(weights)
    hidden_state = inputs.astype(jnp.float32)
    kept = []
    for applied in range(LAYERS):
        hidden_state, kept_values = layer_forward(resident, hidden_state)
        kept.append(kept_values)
    outputs = hidden_state.astype(jnp.bfloat16)
    upstream = cotangent.astype(jnp.float32) * masked.reshape(-1, 1).astype(jnp.float32)
    collected = None
    for applied in range(LAYERS - 1, -1, -1):
        upstream, weight_grads = layer_backward(resident, kept[applied], upstream)
        collected = (
            weight_grads
            if collected is None
            else tuple((earlier + later for earlier, later in zip(collected, weight_grads)))
        )
    collected = scatter_grads(collected, shards)
    return (outputs, upstream.astype(jnp.bfloat16)) + tuple(collected)


def solution(mesh):
    in_specs = (
        P(("dp", "fsdp"), None),
        P(("dp", "fsdp"), None),
        P(("dp", "fsdp"), None),
        P(("dp", "fsdp"), None),
        P(("dp", "fsdp")),
        P(("dp", "fsdp"), None),
        P(("dp", "fsdp"), None),
        P(("dp", "fsdp")),
        P(("dp", "fsdp"), None),
        P(("dp", "fsdp")),
        P(("dp", "fsdp")),
        P(("dp", "fsdp")),
        P(("dp", "fsdp"), None),
        P(("dp", "fsdp")),
        P(("dp", "fsdp"), None),
        P(("dp", "fsdp")),
        P(("dp", "fsdp")),
        P(("dp", "fsdp")),
    )
    out_specs = (
        P(("dp", "fsdp"), None),
        P(("dp", "fsdp"), None),
        P(("dp", "fsdp"), None),
        P(("dp", "fsdp")),
        P(("dp", "fsdp"), None),
        P(("dp", "fsdp"), None),
        P(("dp", "fsdp")),
        P(("dp", "fsdp"), None),
        P(("dp", "fsdp")),
        P(("dp", "fsdp")),
        P(("dp", "fsdp")),
        P(("dp", "fsdp"), None),
        P(("dp", "fsdp")),
        P(("dp", "fsdp"), None),
        P(("dp", "fsdp")),
        P(("dp", "fsdp")),
        P(("dp", "fsdp")),
    )
    shards = mesh.shape["dp"] * mesh.shape["fsdp"]
    return jax.shard_map(
        functools.partial(per_device, shards), mesh=mesh, in_specs=in_specs, out_specs=out_specs, check_vma=False
    )
```

```python
import functools

import jax
import jax.numpy as jnp
from jax import lax
from jax.experimental import pallas as pl
from jax.experimental.pallas import tpu as pltpu
from jax.sharding import PartitionSpec as P

SEQ = 512
HEAD = 64
PAIR = 128
LAYERS = 3
AXES = ("dp", "fsdp")
NT = (((1,), (1,)), ((), ()))
TN = (((0,), (0,)), ((), ()))
norm_epsilon = 1e-05


def product(left, right):
    return jnp.dot(left, right, preferred_element_type=jnp.float32)


def product_nt(left, right):
    return lax.dot_general(left, right, NT, preferred_element_type=jnp.float32)


def gelu_tanh(values):
    return jax.nn.gelu(values, approximate=True)


def layer_norm(summed, gain, shift):
    centre = summed - jnp.mean(summed, axis=-1, keepdims=True)
    inverse = lax.rsqrt(jnp.mean(centre * centre, axis=-1, keepdims=True) + norm_epsilon)
    normed = centre * inverse
    return (normed * gain + shift, normed, inverse)


def norm_backward(upstream, normed, inverse, gain):
    scaled = upstream * gain
    return inverse * (
        scaled
        - jnp.mean(scaled, axis=-1, keepdims=True)
        - normed * jnp.mean(scaled * normed, axis=-1, keepdims=True)
    )


def _head_masks(shape):
    lane = lax.broadcasted_iota(jnp.int32, shape, 1)
    first = lane < HEAD
    return first, jnp.logical_not(first)


def attention_forward_kernel(qkv_ref, ctx_ref, lt_ref):
    scale = HEAD ** (-0.5)
    q = qkv_ref[:, 0:PAIR]
    k = qkv_ref[:, PAIR : 2 * PAIR]
    v = qkv_ref[:, 2 * PAIR : 3 * PAIR]
    masks = _head_masks(q.shape)
    zero = jnp.zeros_like(q)
    context = None
    total = None
    for mask in masks:
        scores = product_nt(jnp.where(mask, q, zero), k) * scale
        top = jnp.max(scores, axis=-1, keepdims=True)
        weights = jnp.exp(scores - top)
        sums = jnp.sum(weights, axis=-1, keepdims=True)
        probs = (weights / sums).astype(jnp.bfloat16)
        part = jnp.dot(probs, v, preferred_element_type=jnp.float32)
        log_total = jnp.broadcast_to(top + jnp.log(sums), part.shape)
        context = part if context is None else jnp.where(mask, part, context)
        total = log_total if total is None else jnp.where(mask, log_total, total)
    ctx_ref[...] = context.astype(ctx_ref.dtype)
    lt_ref[...] = total


def attention_backward_kernel(qkv_ref, lt_ref, g_ref, out_ref):
    scale = HEAD ** (-0.5)
    q = qkv_ref[:, 0:PAIR]
    k = qkv_ref[:, PAIR : 2 * PAIR]
    v = qkv_ref[:, 2 * PAIR : 3 * PAIR]
    g = g_ref[...]
    lt_all = lt_ref[...]
    masks = _head_masks(q.shape)
    zero = jnp.zeros_like(q)
    dq = dk = dv = None
    for mask in masks:
        scores = product_nt(jnp.where(mask, q, zero), k) * scale
        lt = jnp.max(jnp.where(mask, lt_all, -jnp.inf), axis=-1, keepdims=True)
        probs = jnp.exp(scores - lt)
        prob_grad = product_nt(jnp.where(mask, g, zero), v)
        value_part = lax.dot_general(
            probs.astype(jnp.bfloat16), g, TN, preferred_element_type=jnp.float32
        )
        score_grad = (
            probs * (prob_grad - jnp.sum(probs * prob_grad, axis=-1, keepdims=True))
        ).astype(jnp.bfloat16)
        query_part = jnp.dot(score_grad, k, preferred_element_type=jnp.float32) * scale
        key_part = lax.dot_general(score_grad, q, TN, preferred_element_type=jnp.float32) * scale
        if dq is None:
            dq, dk, dv = query_part, key_part, value_part
        else:
            dq = jnp.where(mask, query_part, dq)
            dk = jnp.where(mask, key_part, dk)
            dv = jnp.where(mask, value_part, dv)
    out_ref[:, 0:PAIR] = dq.astype(out_ref.dtype)
    out_ref[:, PAIR : 2 * PAIR] = dk.astype(out_ref.dtype)
    out_ref[:, 2 * PAIR : 3 * PAIR] = dv.astype(out_ref.dtype)


def attention_forward(qkv):
    tokens, width = qkv.shape
    grid = (tokens // SEQ, width // (3 * PAIR))
    steps = grid[0] * grid[1]
    pair = pl.BlockSpec((SEQ, PAIR), lambda s, h: (s, h))
    return pl.pallas_call(
        attention_forward_kernel,
        grid=grid,
        in_specs=[pl.BlockSpec((SEQ, 3 * PAIR), lambda s, h: (s, h))],
        out_specs=[pair, pair],
        out_shape=[
            jax.ShapeDtypeStruct((tokens, width // 3), jnp.bfloat16),
            jax.ShapeDtypeStruct((tokens, width // 3), jnp.float32),
        ],
        compiler_params=pltpu.CompilerParams(dimension_semantics=("parallel", "parallel")),
        cost_estimate=pl.CostEstimate(
            flops=steps * 8 * SEQ * SEQ * PAIR,
            transcendentals=steps * 2 * SEQ * SEQ,
            bytes_accessed=tokens * width * 4,
        ),
        name="attention_forward",
    )(qkv)


def attention_backward(qkv, log_total, context_grad):
    tokens, width = qkv.shape
    grid = (tokens // SEQ, width // (3 * PAIR))
    steps = grid[0] * grid[1]
    pair = pl.BlockSpec((SEQ, PAIR), lambda s, h: (s, h))
    triple = pl.BlockSpec((SEQ, 3 * PAIR), lambda s, h: (s, h))
    return pl.pallas_call(
        attention_backward_kernel,
        grid=grid,
        in_specs=[triple, pair, pair],
        out_specs=triple,
        out_shape=jax.ShapeDtypeStruct((tokens, width), jnp.bfloat16),
        compiler_params=pltpu.CompilerParams(dimension_semantics=("parallel", "parallel")),
        cost_estimate=pl.CostEstimate(
            flops=steps * 20 * SEQ * SEQ * PAIR,
            transcendentals=steps * 2 * SEQ * SEQ,
            bytes_accessed=tokens * width * 6,
        ),
        name="attention_backward",
    )(qkv, log_total, context_grad)


def weight_grad_kernel(*refs):
    count = (len(refs) - 2) // 2
    xs, gs = refs[:count], refs[count : 2 * count]
    out_ref, sum_ref = refs[-2], refs[-1]
    acc = None
    sums = None
    for x_ref, g_ref in zip(xs, gs):
        g = g_ref[...]
        part = lax.dot_general(x_ref[...], g, TN, preferred_element_type=jnp.float32)
        col = jnp.sum(g.astype(jnp.float32), axis=0, keepdims=True)
        acc = part if acc is None else acc + part
        sums = col if sums is None else sums + col
    out_ref[...] = acc.astype(out_ref.dtype)
    sum_ref[...] = sums


def weight_grad(xs, gs, block=768):
    tokens, depth = xs[0].shape
    width = gs[0].shape[1]
    bk = min(block, depth)
    bn = min(block, width)
    grid = (depth // bk, width // bn)
    count = len(xs)
    in_specs = [pl.BlockSpec((tokens, bk), lambda i, j: (0, i))] * count + [
        pl.BlockSpec((tokens, bn), lambda i, j: (0, j))
    ] * count
    return pl.pallas_call(
        weight_grad_kernel,
        grid=grid,
        in_specs=in_specs,
        out_specs=[
            pl.BlockSpec((bk, bn), lambda i, j: (i, j)),
            pl.BlockSpec((1, bn), lambda i, j: (0, j)),
        ],
        out_shape=[
            jax.ShapeDtypeStruct((depth, width), jnp.bfloat16),
            jax.ShapeDtypeStruct((1, width), jnp.float32),
        ],
        compiler_params=pltpu.CompilerParams(
            dimension_semantics=("arbitrary", "arbitrary"), vmem_limit_bytes=48 * 1024 * 1024
        ),
        cost_estimate=pl.CostEstimate(
            flops=2 * count * tokens * depth * width,
            transcendentals=0,
            bytes_accessed=2 * count * tokens * (depth + width) + 2 * depth * width,
        ),
        name="weight_grad",
    )(*xs, *gs)


def interleave_qkv(q, k, v):
    pieces = []
    for h in range(q.shape[-1] // PAIR):
        cols = slice(h * PAIR, (h + 1) * PAIR)
        pieces += [q[..., cols], k[..., cols], v[..., cols]]
    return jnp.concatenate(pieces, axis=-1)


def split_qkv(packed):
    pairs = packed.shape[-1] // (3 * PAIR)
    parts = [[], [], []]
    for h in range(pairs):
        for which in range(3):
            start = (3 * h + which) * PAIR
            parts[which].append(packed[..., start : start + PAIR])
    return [jnp.concatenate(p, axis=-1) for p in parts]


def pack_weights(weights):
    (qw, qb, kw, vw, vb, ow, ob, g1, s1, iw, ib, uw, ub, g2, s2) = weights
    rows, width = qw.shape
    wide = iw.shape[1]
    vectors = jnp.concatenate([qb, vb, ob, g1, s1, ub, g2, s2, ib])
    vectors = jnp.pad(vectors, (0, wide - vectors.shape[0]))[None, :]
    return jnp.concatenate(
        [
            jnp.concatenate([interleave_qkv(qw, kw, vw), ow], axis=1),
            iw,
            uw.reshape(rows, wide),
            vectors,
        ],
        axis=0,
    )


def gather_weights(weights):
    rows, width = weights[0].shape
    ff_rows, wide = weights[11].shape[0], weights[9].shape[1]
    packed = lax.all_gather(pack_weights(weights), AXES, axis=0, tiled=False)
    shards = packed.shape[0]
    attn = packed[:, 0:rows].reshape(shards * rows, wide)
    inner = packed[:, rows : 2 * rows].reshape(shards * rows, wide)
    outer = packed[:, 2 * rows : 3 * rows].reshape(shards * ff_rows, width)
    vectors = packed[:, 3 * rows, :].astype(jnp.float32)
    found = []
    at = 0
    for count in (rows,) * 8 + (ff_rows,):
        found.append(vectors[:, at : at + count].reshape(-1))
        at += count
    (qb, vb, ob, g1, s1, ub, g2, s2, ib) = found
    return dict(
        qkv=attn[:, : 3 * width],
        qkv_bias=interleave_qkv(qb, jnp.zeros_like(qb), vb),
        out=attn[:, 3 * width :],
        out_bias=ob,
        g1=g1,
        s1=s1,
        inner=inner,
        inner_bias=ib,
        outer=outer,
        outer_bias=ub,
        g2=g2,
        s2=s2,
    )


def layer_forward(w, hidden_state):
    rows_low = hidden_state.astype(jnp.bfloat16)
    qkv = (product(rows_low, w["qkv"]) + w["qkv_bias"]).astype(jnp.bfloat16)
    context_low, log_total = attention_forward(qkv)
    attended = product(context_low, w["out"]) + w["out_bias"]
    first_out, first_normed, first_inverse = layer_norm(hidden_state + attended, w["g1"], w["s1"])
    first_low = first_out.astype(jnp.bfloat16)
    inner_pre = product(first_low, w["inner"]) + w["inner_bias"]
    inner_low = gelu_tanh(inner_pre).astype(jnp.bfloat16)
    outer_out = product(inner_low, w["outer"]) + w["outer_bias"]
    result, second_normed, second_inverse = layer_norm(first_out + outer_out, w["g2"], w["s2"])
    kept = dict(
        rows_low=rows_low,
        qkv=qkv,
        log_total=log_total,
        context_low=context_low,
        first_normed=first_normed,
        first_inverse=first_inverse,
        first_low=first_low,
        inner_pre=inner_pre,
        inner_low=inner_low,
        second_normed=second_normed,
        second_inverse=second_inverse,
    )
    return result, kept


def layer_backward(w, kept, upstream):
    second_gain_grad = jnp.sum(upstream * kept["second_normed"], axis=0)
    second_shift_grad = jnp.sum(upstream, axis=0)
    second_grad = norm_backward(upstream, kept["second_normed"], kept["second_inverse"], w["g2"])
    outer_low = second_grad.astype(jnp.bfloat16)
    active_grad = product_nt(outer_low, w["outer"])
    gelu_pull = jax.vjp(gelu_tanh, kept["inner_pre"])[1]
    inner_grad = gelu_pull(active_grad)[0].astype(jnp.bfloat16)
    first_grad = second_grad + product_nt(inner_grad, w["inner"])
    first_gain_grad = jnp.sum(first_grad * kept["first_normed"], axis=0)
    first_shift_grad = jnp.sum(first_grad, axis=0)
    attended_grad = norm_backward(first_grad, kept["first_normed"], kept["first_inverse"], w["g1"])
    attended_low = attended_grad.astype(jnp.bfloat16)
    context_grad = product_nt(attended_low, w["out"]).astype(jnp.bfloat16)
    qkv_grad = attention_backward(kept["qkv"], kept["log_total"], context_grad)
    below_grad = attended_grad + product_nt(qkv_grad, w["qkv"])
    saved = dict(
        outer_low=outer_low,
        inner_grad=inner_grad,
        attended_low=attended_low,
        qkv_grad=qkv_grad,
    )
    norms = (second_gain_grad, second_shift_grad, first_gain_grad, first_shift_grad)
    return below_grad, saved, norms


def scatter_grads(kept, saved, norms, shards):
    def across(source, name):
        return [item[name] for item in source]

    qkv_w, qkv_b = weight_grad(across(kept, "rows_low"), across(saved, "qkv_grad"))
    out_w, out_b = weight_grad(across(kept, "context_low"), across(saved, "attended_low"))
    inner_w, inner_b = weight_grad(across(kept, "first_low"), across(saved, "inner_grad"))
    outer_w, outer_b = weight_grad(across(kept, "inner_low"), across(saved, "outer_low"))
    rows, wide = inner_w.shape
    q_b, _, v_b = split_qkv(qkv_b[0])
    s2g, s2s, s1g, s1s = [sum(parts) for parts in zip(*norms)]
    columns = jnp.stack(
        [q_b, v_b, out_b[0], s1g, s1s, outer_b[0], s2g, s2s], axis=1
    )
    columns = jnp.concatenate([columns, inner_b[0].reshape(rows, -1)], axis=1)
    columns = jnp.pad(columns, ((0, 0), (0, PAIR - columns.shape[1]))).astype(jnp.bfloat16)
    packed = jnp.concatenate(
        [qkv_w, out_w, inner_w, outer_w.reshape(rows, wide), columns], axis=1
    )
    mine = lax.psum_scatter(packed, AXES, scatter_dimension=0, tiled=True).astype(jnp.float32)
    width = out_w.shape[1]
    at = 0
    pieces = []
    for count in (3 * width, width, wide, wide, PAIR):
        pieces.append(mine[:, at : at + count])
        at += count
    qkv_mine, out_mine, inner_mine, outer_mine, col_mine = pieces
    q_w, k_w, v_w = split_qkv(qkv_mine)
    c = [col_mine[:, i] for i in range(8)]
    ib_mine = col_mine[:, 8:12].reshape(-1)
    return (
        q_w,
        c[0],
        k_w,
        v_w,
        c[1],
        out_mine,
        c[2],
        c[3],
        c[4],
        inner_mine,
        ib_mine,
        outer_mine.reshape(-1, width),
        c[5],
        c[6],
        c[7],
    )


def per_device(shards, inputs, cotangent, masked, *weights):
    w = gather_weights(weights)
    hidden_state = inputs.astype(jnp.float32)
    kept = []
    for applied in range(LAYERS):
        hidden_state, kept_values = layer_forward(w, hidden_state)
        kept.append(kept_values)
    outputs = hidden_state.astype(jnp.bfloat16)
    upstream = cotangent.astype(jnp.float32) * masked.reshape(-1, 1).astype(jnp.float32)
    saved = [None] * LAYERS
    norms = [None] * LAYERS
    for applied in range(LAYERS - 1, -1, -1):
        upstream, saved[applied], norms[applied] = layer_backward(w, kept[applied], upstream)
    collected = scatter_grads(kept, saved, norms, shards)
    return (outputs, upstream.astype(jnp.bfloat16)) + tuple(collected)


def solution(mesh):
    rows = P(AXES, None)
    vec = P(AXES)
    in_specs = (rows, rows, rows, rows, vec, rows, rows, vec, rows, vec, vec, vec, rows, vec, rows, vec, vec, vec)
    out_specs = (rows, rows, rows, vec, rows, rows, vec, rows, vec, vec, vec, rows, vec, rows, vec, vec, vec)
    shards = mesh.shape["dp"] * mesh.shape["fsdp"]
    return jax.shard_map(
        functools.partial(per_device, shards),
        mesh=mesh,
        in_specs=in_specs,
        out_specs=out_specs,
        check_vma=False,
    )
```

```python
import functools

import jax
import jax.numpy as jnp
from jax import lax
from jax.experimental import pallas as pl
from jax.experimental.pallas import tpu as pltpu
from jax.sharding import PartitionSpec as P

SEQ = 512
HEAD = 64
PAIR = 128
LAYERS = 3
AXES = ("dp", "fsdp")
NT = (((1,), (1,)), ((), ()))
TN = (((0,), (0,)), ((), ()))
norm_epsilon = 1e-05


def product(left, right):
    return jnp.dot(left, right, preferred_element_type=jnp.float32)


def product_nt(left, right):
    return lax.dot_general(left, right, NT, preferred_element_type=jnp.float32)


def gelu_tanh(values):
    return jax.nn.gelu(values, approximate=True)


def layer_norm(summed, gain, shift):
    centre = summed - jnp.mean(summed, axis=-1, keepdims=True)
    inverse = lax.rsqrt(jnp.mean(centre * centre, axis=-1, keepdims=True) + norm_epsilon)
    normed = centre * inverse
    return (normed * gain + shift, normed, inverse)


def norm_backward(upstream, normed, inverse, gain):
    scaled = upstream * gain
    return inverse * (
        scaled
        - jnp.mean(scaled, axis=-1, keepdims=True)
        - normed * jnp.mean(scaled * normed, axis=-1, keepdims=True)
    )


def _head_masks(shape):
    lane = lax.broadcasted_iota(jnp.int32, shape, 1)
    first = lane < HEAD
    return first, jnp.logical_not(first)


def attention_forward_kernel(qkv_ref, ctx_ref, lt_ref):
    scale = HEAD ** (-0.5)
    q = qkv_ref[:, 0:PAIR]
    k = qkv_ref[:, PAIR : 2 * PAIR]
    v = qkv_ref[:, 2 * PAIR : 3 * PAIR]
    masks = _head_masks(q.shape)
    zero = jnp.zeros_like(q)
    context = None
    total = None
    for mask in masks:
        scores = product_nt(jnp.where(mask, q, zero), k) * scale
        top = jnp.max(scores, axis=-1, keepdims=True)
        weights = jnp.exp(scores - top)
        sums = jnp.sum(weights, axis=-1, keepdims=True)
        probs = (weights / sums).astype(jnp.bfloat16)
        part = jnp.dot(probs, v, preferred_element_type=jnp.float32)
        log_total = jnp.broadcast_to(top + jnp.log(sums), part.shape)
        context = part if context is None else jnp.where(mask, part, context)
        total = log_total if total is None else jnp.where(mask, log_total, total)
    ctx_ref[...] = context.astype(ctx_ref.dtype)
    lt_ref[...] = total


def attention_backward_kernel(qkv_ref, lt_ref, g_ref, out_ref):
    scale = HEAD ** (-0.5)
    q = qkv_ref[:, 0:PAIR]
    k = qkv_ref[:, PAIR : 2 * PAIR]
    v = qkv_ref[:, 2 * PAIR : 3 * PAIR]
    g = g_ref[...]
    lt_all = lt_ref[...]
    masks = _head_masks(q.shape)
    zero = jnp.zeros_like(q)
    dq = dk = dv = None
    for mask in masks:
        scores = product_nt(jnp.where(mask, q, zero), k) * scale
        lt = jnp.max(jnp.where(mask, lt_all, -jnp.inf), axis=-1, keepdims=True)
        probs = jnp.exp(scores - lt)
        prob_grad = product_nt(jnp.where(mask, g, zero), v)
        value_part = lax.dot_general(
            probs.astype(jnp.bfloat16), g, TN, preferred_element_type=jnp.float32
        )
        score_grad = (
            probs * (prob_grad - jnp.sum(probs * prob_grad, axis=-1, keepdims=True))
        ).astype(jnp.bfloat16)
        query_part = jnp.dot(score_grad, k, preferred_element_type=jnp.float32) * scale
        key_part = lax.dot_general(score_grad, q, TN, preferred_element_type=jnp.float32) * scale
        if dq is None:
            dq, dk, dv = query_part, key_part, value_part
        else:
            dq = jnp.where(mask, query_part, dq)
            dk = jnp.where(mask, key_part, dk)
            dv = jnp.where(mask, value_part, dv)
    out_ref[:, 0:PAIR] = dq.astype(out_ref.dtype)
    out_ref[:, PAIR : 2 * PAIR] = dk.astype(out_ref.dtype)
    out_ref[:, 2 * PAIR : 3 * PAIR] = dv.astype(out_ref.dtype)


def attention_forward(qkv):
    tokens, width = qkv.shape
    grid = (tokens // SEQ, width // (3 * PAIR))
    steps = grid[0] * grid[1]
    pair = pl.BlockSpec((SEQ, PAIR), lambda s, h: (s, h))
    return pl.pallas_call(
        attention_forward_kernel,
        grid=grid,
        in_specs=[pl.BlockSpec((SEQ, 3 * PAIR), lambda s, h: (s, h))],
        out_specs=[pair, pair],
        out_shape=[
            jax.ShapeDtypeStruct((tokens, width // 3), jnp.bfloat16),
            jax.ShapeDtypeStruct((tokens, width // 3), jnp.float32),
        ],
        compiler_params=pltpu.CompilerParams(dimension_semantics=("parallel", "parallel")),
        cost_estimate=pl.CostEstimate(
            flops=steps * 8 * SEQ * SEQ * PAIR,
            transcendentals=steps * 2 * SEQ * SEQ,
            bytes_accessed=tokens * width * 4,
        ),
        name="attention_forward",
    )(qkv)


def attention_backward(qkv, log_total, context_grad):
    tokens, width = qkv.shape
    grid = (tokens // SEQ, width // (3 * PAIR))
    steps = grid[0] * grid[1]
    pair = pl.BlockSpec((SEQ, PAIR), lambda s, h: (s, h))
    triple = pl.BlockSpec((SEQ, 3 * PAIR), lambda s, h: (s, h))
    return pl.pallas_call(
        attention_backward_kernel,
        grid=grid,
        in_specs=[triple, pair, pair],
        out_specs=triple,
        out_shape=jax.ShapeDtypeStruct((tokens, width), jnp.bfloat16),
        compiler_params=pltpu.CompilerParams(dimension_semantics=("parallel", "parallel")),
        cost_estimate=pl.CostEstimate(
            flops=steps * 20 * SEQ * SEQ * PAIR,
            transcendentals=steps * 2 * SEQ * SEQ,
            bytes_accessed=tokens * width * 6,
        ),
        name="attention_backward",
    )(qkv, log_total, context_grad)


def weight_grad_kernel(*refs):
    count = (len(refs) - 2) // 2
    xs, gs = refs[:count], refs[count : 2 * count]
    out_ref, sum_ref = refs[-2], refs[-1]
    acc = None
    sums = None
    for x_ref, g_ref in zip(xs, gs):
        g = g_ref[...]
        part = lax.dot_general(x_ref[...], g, TN, preferred_element_type=jnp.float32)
        col = jnp.sum(g.astype(jnp.float32), axis=0, keepdims=True)
        acc = part if acc is None else acc + part
        sums = col if sums is None else sums + col
    out_ref[...] = acc.astype(out_ref.dtype)
    sum_ref[...] = sums


def weight_grad(xs, gs, into=None, at=0, stack=False, columns=None, block=768):
    tokens, depth = xs[0].shape
    width = gs[0].shape[1]
    bk = min(block, depth)
    bn = min(block, width)
    grid = (depth // bk, width // bn)
    count = len(xs)
    if stack:
        place = lambda i, j: (0, at + i * grid[1] + j)
        shape = (bk, depth // bk * width)
    else:
        place = lambda i, j: (i, at + j)
        shape = (depth, width)
    if into is not None:
        target = into.shape
    elif columns is not None:
        target = (shape[0], columns)
    else:
        target = shape
    in_specs = [pl.BlockSpec((tokens, bk), lambda i, j: (0, i))] * count + [
        pl.BlockSpec((tokens, bn), lambda i, j: (0, j))
    ] * count
    args = list(xs) + list(gs)
    aliases = {}
    kernel = weight_grad_kernel
    if into is not None:
        in_specs.append(pl.BlockSpec(memory_space=pl.ANY))
        args.append(into)
        aliases = {len(args) - 1: 0}
        kernel = lambda *refs: weight_grad_kernel(*refs[: 2 * count], *refs[2 * count + 1 :])
    return pl.pallas_call(
        kernel,
        grid=grid,
        in_specs=in_specs,
        out_specs=[
            pl.BlockSpec((bk, bn), place),
            pl.BlockSpec((1, bn), lambda i, j: (0, j)),
        ],
        out_shape=[
            jax.ShapeDtypeStruct(target, jnp.bfloat16),
            jax.ShapeDtypeStruct((1, width), jnp.float32),
        ],
        input_output_aliases=aliases,
        compiler_params=pltpu.CompilerParams(
            dimension_semantics=("arbitrary", "arbitrary"), vmem_limit_bytes=48 * 1024 * 1024
        ),
        cost_estimate=pl.CostEstimate(
            flops=2 * count * tokens * depth * width,
            transcendentals=0,
            bytes_accessed=2 * count * tokens * (depth + width) + 2 * depth * width,
        ),
        name="weight_grad",
    )(*args)


def interleave_qkv(q, k, v):
    lead = q.shape[:-1]
    pairs = q.shape[-1] // PAIR
    stacked = jnp.stack([q, k, v], axis=-2).reshape(lead + (3, pairs, PAIR))
    return jnp.swapaxes(stacked, -3, -2).reshape(lead + (3 * pairs * PAIR,))


def split_qkv(packed):
    pairs = packed.shape[-1] // (3 * PAIR)
    parts = [[], [], []]
    for h in range(pairs):
        for which in range(3):
            start = (3 * h + which) * PAIR
            parts[which].append(packed[..., start : start + PAIR])
    return [jnp.concatenate(p, axis=-1) for p in parts]


def to_hidden_order(values, groups=4):
    lead, n = values.shape[:-1], values.shape[-1]
    return jnp.swapaxes(values.reshape(lead + (n // groups, groups)), -1, -2).reshape(lead + (n,))


def from_hidden_order(values, groups=4):
    lead, n = values.shape[:-1], values.shape[-1]
    return jnp.swapaxes(values.reshape(lead + (groups, n // groups)), -1, -2).reshape(lead + (n,))


def pack_weights(weights):
    (qw, qb, kw, vw, vb, ow, ob, g1, s1, iw, ib, uw, ub, g2, s2) = weights
    rows, width = qw.shape
    wide = iw.shape[1]
    vectors = None
    at = 0
    for piece in (qb, vb, ob, g1, s1, ub, g2, s2, ib):
        placed = jnp.pad(piece, (at, wide - at - piece.shape[0]))
        vectors = placed if vectors is None else vectors + placed
        at += piece.shape[0]
    vectors = vectors[None, :]
    return jnp.concatenate(
        [
            jnp.concatenate([interleave_qkv(qw, kw, vw), ow], axis=1),
            to_hidden_order(iw),
            uw.reshape(rows, wide),
            vectors,
        ],
        axis=0,
    )


def gather_weights(weights):
    rows, width = weights[0].shape
    ff_rows, wide = weights[11].shape[0], weights[9].shape[1]
    packed = lax.all_gather(pack_weights(weights), AXES, axis=0, tiled=False)
    shards = packed.shape[0]
    attn = packed[:, 0:rows].reshape(shards * rows, wide)
    inner = packed[:, rows : 2 * rows].reshape(shards * rows, wide)
    outer_rows = packed[:, 2 * rows : 3 * rows].reshape(shards * rows, wide)
    groups = wide // width
    outer = jnp.concatenate(
        [outer_rows[:, c * width : (c + 1) * width] for c in range(groups)], axis=0
    )
    vectors = packed[:, 3 * rows, :].astype(jnp.float32)
    found = []
    at = 0
    for count in (rows,) * 8 + (ff_rows,):
        found.append(vectors[:, at : at + count].reshape(-1))
        at += count
    (qb, vb, ob, g1, s1, ub, g2, s2, ib) = found
    return dict(
        qkv=attn[:, : 3 * width],
        qkv_bias=interleave_qkv(qb, jnp.zeros_like(qb), vb),
        out=attn[:, 3 * width :],
        out_bias=ob,
        g1=g1,
        s1=s1,
        inner=inner,
        inner_bias=ib.reshape(shards, rows, groups).transpose(2, 0, 1).reshape(-1),
        outer=outer,
        outer_bias=ub,
        g2=g2,
        s2=s2,
    )


def layer_forward(w, hidden_state):
    rows_low = hidden_state.astype(jnp.bfloat16)
    qkv = (product(rows_low, w["qkv"]) + w["qkv_bias"]).astype(jnp.bfloat16)
    context_low, log_total = attention_forward(qkv)
    attended = product(context_low, w["out"]) + w["out_bias"]
    first_out, first_normed, first_inverse = layer_norm(hidden_state + attended, w["g1"], w["s1"])
    first_low = first_out.astype(jnp.bfloat16)
    inner_pre = product(first_low, w["inner"]) + w["inner_bias"]
    inner_low = gelu_tanh(inner_pre).astype(jnp.bfloat16)
    outer_out = product(inner_low, w["outer"]) + w["outer_bias"]
    result, second_normed, second_inverse = layer_norm(first_out + outer_out, w["g2"], w["s2"])
    kept = dict(
        rows_low=rows_low,
        qkv=qkv,
        log_total=log_total,
        context_low=context_low,
        first_normed=first_normed,
        first_inverse=first_inverse,
        first_low=first_low,
        inner_pre=inner_pre,
        inner_low=inner_low,
        second_normed=second_normed,
        second_inverse=second_inverse,
    )
    return result, kept


def layer_backward(w, kept, upstream):
    second_gain_grad = jnp.sum(upstream * kept["second_normed"], axis=0)
    second_shift_grad = jnp.sum(upstream, axis=0)
    second_grad = norm_backward(upstream, kept["second_normed"], kept["second_inverse"], w["g2"])
    outer_low = second_grad.astype(jnp.bfloat16)
    active_grad = product_nt(outer_low, w["outer"])
    gelu_pull = jax.vjp(gelu_tanh, kept["inner_pre"])[1]
    inner_grad = gelu_pull(active_grad)[0].astype(jnp.bfloat16)
    first_grad = second_grad + product_nt(inner_grad, w["inner"])
    first_gain_grad = jnp.sum(first_grad * kept["first_normed"], axis=0)
    first_shift_grad = jnp.sum(first_grad, axis=0)
    attended_grad = norm_backward(first_grad, kept["first_normed"], kept["first_inverse"], w["g1"])
    attended_low = attended_grad.astype(jnp.bfloat16)
    context_grad = product_nt(attended_low, w["out"]).astype(jnp.bfloat16)
    qkv_grad = attention_backward(kept["qkv"], kept["log_total"], context_grad)
    below_grad = attended_grad + product_nt(qkv_grad, w["qkv"])
    saved = dict(
        outer_low=outer_low,
        inner_grad=inner_grad,
        attended_low=attended_low,
        qkv_grad=qkv_grad,
    )
    norms = (second_gain_grad, second_shift_grad, first_gain_grad, first_shift_grad)
    return below_grad, saved, norms


def scatter_grads(kept, saved, norms, shards):
    def across(source, name):
        return [item[name] for item in source]

    width = kept[0]["context_low"].shape[1]
    three = kept[0]["qkv"].shape[1]
    wide = kept[0]["inner_low"].shape[1]
    blocks = (three + width + 2 * wide) // width
    packed, qkv_b = weight_grad(
        across(kept, "rows_low"), across(saved, "qkv_grad"), columns=blocks * width + PAIR
    )
    at = three // width
    packed, out_b = weight_grad(
        across(kept, "context_low"), across(saved, "attended_low"), into=packed, at=at
    )
    at += 1
    packed, inner_b = weight_grad(
        across(kept, "first_low"), across(saved, "inner_grad"), into=packed, at=at
    )
    at += wide // width
    packed, outer_b = weight_grad(
        across(kept, "inner_low"), across(saved, "outer_low"), into=packed, at=at, stack=True
    )
    rows = width
    q_b, _, v_b = split_qkv(qkv_b[0])
    s2g, s2s, s1g, s1s = [sum(parts) for parts in zip(*norms)]
    columns = jnp.stack([q_b, v_b, out_b[0], s1g, s1s, outer_b[0], s2g, s2s], axis=1)
    inner_cols = inner_b[0].reshape(wide // rows, rows).T
    columns = jnp.concatenate([columns, inner_cols], axis=1)
    columns = jnp.pad(columns, ((0, 0), (0, PAIR - columns.shape[1]))).astype(jnp.bfloat16)
    packed = lax.dynamic_update_slice(packed, columns, (0, blocks * width))
    mine = lax.psum_scatter(packed, AXES, scatter_dimension=0, tiled=True).astype(jnp.float32)
    at = 0
    pieces = []
    for count in (three, width, wide, wide, PAIR):
        pieces.append(mine[:, at : at + count])
        at += count
    qkv_mine, out_mine, inner_mine, outer_mine, col_mine = pieces
    q_w, k_w, v_w = split_qkv(qkv_mine)
    c = [col_mine[:, i] for i in range(8)]
    ib_mine = col_mine[:, 8:12].reshape(-1)
    return (
        q_w,
        c[0],
        k_w,
        v_w,
        c[1],
        out_mine,
        c[2],
        c[3],
        c[4],
        from_hidden_order(inner_mine),
        ib_mine,
        outer_mine.reshape(-1, width),
        c[5],
        c[6],
        c[7],
    )


def per_device(shards, inputs, cotangent, masked, *weights):
    w = gather_weights(weights)
    hidden_state = inputs.astype(jnp.float32)
    kept = []
    for applied in range(LAYERS):
        hidden_state, kept_values = layer_forward(w, hidden_state)
        kept.append(kept_values)
    outputs = hidden_state.astype(jnp.bfloat16)
    upstream = cotangent.astype(jnp.float32) * masked.reshape(-1, 1).astype(jnp.float32)
    saved = [None] * LAYERS
    norms = [None] * LAYERS
    for applied in range(LAYERS - 1, -1, -1):
        upstream, saved[applied], norms[applied] = layer_backward(w, kept[applied], upstream)
    collected = scatter_grads(kept, saved, norms, shards)
    return (outputs, upstream.astype(jnp.bfloat16)) + tuple(collected)


def solution(mesh):
    rows = P(AXES, None)
    vec = P(AXES)
    in_specs = (rows, rows, rows, rows, vec, rows, rows, vec, rows, vec, vec, vec, rows, vec, rows, vec, vec, vec)
    out_specs = (rows, rows, rows, vec, rows, rows, vec, rows, vec, vec, vec, rows, vec, rows, vec, vec, vec)
    shards = mesh.shape["dp"] * mesh.shape["fsdp"]
    return jax.shard_map(
        functools.partial(per_device, shards),
        mesh=mesh,
        in_specs=in_specs,
        out_specs=out_specs,
        check_vma=False,
    )
```

```python
import functools

import jax
import jax.numpy as jnp
from jax import lax
from jax.experimental import pallas as pl
from jax.experimental.pallas import tpu as pltpu
from jax.sharding import PartitionSpec as P

SEQ = 512
HEAD = 64
PAIR = 128
LAYERS = 3
AXES = ("dp", "fsdp")
NT = (((1,), (1,)), ((), ()))
TN = (((0,), (0,)), ((), ()))
norm_epsilon = 1e-05


def product(left, right):
    return jnp.dot(left, right, preferred_element_type=jnp.float32)


def product_nt(left, right):
    return lax.dot_general(left, right, NT, preferred_element_type=jnp.float32)


def gelu_tanh(values):
    return jax.nn.gelu(values, approximate=True)


def layer_norm(summed, gain, shift):
    centre = summed - jnp.mean(summed, axis=-1, keepdims=True)
    inverse = lax.rsqrt(jnp.mean(centre * centre, axis=-1, keepdims=True) + norm_epsilon)
    normed = centre * inverse
    return (normed * gain + shift, normed, inverse)


def norm_backward(upstream, normed, inverse, gain):
    scaled = upstream * gain
    return inverse * (
        scaled
        - jnp.mean(scaled, axis=-1, keepdims=True)
        - normed * jnp.mean(scaled * normed, axis=-1, keepdims=True)
    )


def _head_masks(shape):
    lane = lax.broadcasted_iota(jnp.int32, shape, 1)
    first = lane < HEAD
    return first, jnp.logical_not(first)


def attention_forward_kernel(qkv_ref, ctx_ref, lt_ref):
    scale = HEAD ** (-0.5)
    q = qkv_ref[:, 0:PAIR]
    k = qkv_ref[:, PAIR : 2 * PAIR]
    v = qkv_ref[:, 2 * PAIR : 3 * PAIR]
    masks = _head_masks(q.shape)
    zero = jnp.zeros_like(q)
    context = None
    total = None
    for mask in masks:
        scores = product_nt(jnp.where(mask, q, zero), k) * scale
        top = jnp.max(scores, axis=-1, keepdims=True)
        weights = jnp.exp(scores - top)
        sums = jnp.sum(weights, axis=-1, keepdims=True)
        probs = (weights / sums).astype(jnp.bfloat16)
        part = jnp.dot(probs, v, preferred_element_type=jnp.float32)
        log_total = jnp.broadcast_to(top + jnp.log(sums), part.shape)
        context = part if context is None else jnp.where(mask, part, context)
        total = log_total if total is None else jnp.where(mask, log_total, total)
    ctx_ref[...] = context.astype(ctx_ref.dtype)
    lt_ref[...] = total


def attention_backward_kernel(qkv_ref, lt_ref, g_ref, out_ref):
    scale = HEAD ** (-0.5)
    q = qkv_ref[:, 0:PAIR]
    k = qkv_ref[:, PAIR : 2 * PAIR]
    v = qkv_ref[:, 2 * PAIR : 3 * PAIR]
    g = g_ref[...]
    lt_all = lt_ref[...]
    masks = _head_masks(q.shape)
    zero = jnp.zeros_like(q)
    dq = dk = dv = None
    for mask in masks:
        scores = product_nt(jnp.where(mask, q, zero), k) * scale
        lt = jnp.max(jnp.where(mask, lt_all, -jnp.inf), axis=-1, keepdims=True)
        probs = jnp.exp(scores - lt)
        prob_grad = product_nt(jnp.where(mask, g, zero), v)
        value_part = lax.dot_general(
            probs.astype(jnp.bfloat16), g, TN, preferred_element_type=jnp.float32
        )
        score_grad = (
            probs * (prob_grad - jnp.sum(probs * prob_grad, axis=-1, keepdims=True))
        ).astype(jnp.bfloat16)
        query_part = jnp.dot(score_grad, k, preferred_element_type=jnp.float32) * scale
        key_part = lax.dot_general(score_grad, q, TN, preferred_element_type=jnp.float32) * scale
        if dq is None:
            dq, dk, dv = query_part, key_part, value_part
        else:
            dq = jnp.where(mask, query_part, dq)
            dk = jnp.where(mask, key_part, dk)
            dv = jnp.where(mask, value_part, dv)
    out_ref[:, 0:PAIR] = dq.astype(out_ref.dtype)
    out_ref[:, PAIR : 2 * PAIR] = dk.astype(out_ref.dtype)
    out_ref[:, 2 * PAIR : 3 * PAIR] = dv.astype(out_ref.dtype)


def attention_forward(qkv):
    tokens, width = qkv.shape
    grid = (tokens // SEQ, width // (3 * PAIR))
    steps = grid[0] * grid[1]
    pair = pl.BlockSpec((SEQ, PAIR), lambda s, h: (s, h))
    return pl.pallas_call(
        attention_forward_kernel,
        grid=grid,
        in_specs=[pl.BlockSpec((SEQ, 3 * PAIR), lambda s, h: (s, h))],
        out_specs=[pair, pair],
        out_shape=[
            jax.ShapeDtypeStruct((tokens, width // 3), jnp.bfloat16),
            jax.ShapeDtypeStruct((tokens, width // 3), jnp.float32),
        ],
        compiler_params=pltpu.CompilerParams(dimension_semantics=("parallel", "parallel")),
        cost_estimate=pl.CostEstimate(
            flops=steps * 8 * SEQ * SEQ * PAIR,
            transcendentals=steps * 2 * SEQ * SEQ,
            bytes_accessed=tokens * width * 4,
        ),
        name="attention_forward",
    )(qkv)


def attention_backward(qkv, log_total, context_grad):
    tokens, width = qkv.shape
    grid = (tokens // SEQ, width // (3 * PAIR))
    steps = grid[0] * grid[1]
    pair = pl.BlockSpec((SEQ, PAIR), lambda s, h: (s, h))
    triple = pl.BlockSpec((SEQ, 3 * PAIR), lambda s, h: (s, h))
    return pl.pallas_call(
        attention_backward_kernel,
        grid=grid,
        in_specs=[triple, pair, pair],
        out_specs=triple,
        out_shape=jax.ShapeDtypeStruct((tokens, width), jnp.bfloat16),
        compiler_params=pltpu.CompilerParams(dimension_semantics=("parallel", "parallel")),
        cost_estimate=pl.CostEstimate(
            flops=steps * 20 * SEQ * SEQ * PAIR,
            transcendentals=steps * 2 * SEQ * SEQ,
            bytes_accessed=tokens * width * 6,
        ),
        name="attention_backward",
    )(qkv, log_total, context_grad)


def weight_grad_kernel(*refs):
    count = (len(refs) - 2) // 2
    xs, gs = refs[:count], refs[count : 2 * count]
    out_ref, sum_ref = refs[-2], refs[-1]
    acc = None
    sums = None
    for x_ref, g_ref in zip(xs, gs):
        g = g_ref[...]
        part = lax.dot_general(x_ref[...], g, TN, preferred_element_type=jnp.float32)
        col = jnp.sum(g.astype(jnp.float32), axis=0, keepdims=True)
        acc = part if acc is None else acc + part
        sums = col if sums is None else sums + col
    out_ref[...] = acc.astype(out_ref.dtype)
    sum_ref[...] = sums


def weight_grad(xs, gs, into=None, at=0, stack=False, columns=None, block=768):
    tokens, depth = xs[0].shape
    width = gs[0].shape[1]
    bk = min(block, depth)
    bn = min(block, width)
    grid = (depth // bk, width // bn)
    count = len(xs)
    if stack:
        place = lambda i, j: (0, at + i * grid[1] + j)
        shape = (bk, depth // bk * width)
    else:
        place = lambda i, j: (i, at + j)
        shape = (depth, width)
    if into is not None:
        target = into.shape
    elif columns is not None:
        target = (shape[0], columns)
    else:
        target = shape
    in_specs = [pl.BlockSpec((tokens, bk), lambda i, j: (0, i))] * count + [
        pl.BlockSpec((tokens, bn), lambda i, j: (0, j))
    ] * count
    args = list(xs) + list(gs)
    aliases = {}
    kernel = weight_grad_kernel
    if into is not None:
        in_specs.append(pl.BlockSpec(memory_space=pl.ANY))
        args.append(into)
        aliases = {len(args) - 1: 0}
        kernel = lambda *refs: weight_grad_kernel(*refs[: 2 * count], *refs[2 * count + 1 :])
    return pl.pallas_call(
        kernel,
        grid=grid,
        in_specs=in_specs,
        out_specs=[
            pl.BlockSpec((bk, bn), place),
            pl.BlockSpec((1, bn), lambda i, j: (0, j)),
        ],
        out_shape=[
            jax.ShapeDtypeStruct(target, jnp.bfloat16),
            jax.ShapeDtypeStruct((1, width), jnp.float32),
        ],
        input_output_aliases=aliases,
        compiler_params=pltpu.CompilerParams(
            dimension_semantics=("arbitrary", "arbitrary"), vmem_limit_bytes=48 * 1024 * 1024
        ),
        cost_estimate=pl.CostEstimate(
            flops=2 * count * tokens * depth * width,
            transcendentals=0,
            bytes_accessed=2 * count * tokens * (depth + width) + 2 * depth * width,
        ),
        name="weight_grad",
    )(*args)


def interleave_qkv(q, k, v):
    lead = q.shape[:-1]
    pairs = q.shape[-1] // PAIR
    stacked = jnp.stack([q, k, v], axis=-2).reshape(lead + (3, pairs, PAIR))
    return jnp.swapaxes(stacked, -3, -2).reshape(lead + (3 * pairs * PAIR,))


def split_qkv(packed):
    pairs = packed.shape[-1] // (3 * PAIR)
    parts = [[], [], []]
    for h in range(pairs):
        for which in range(3):
            start = (3 * h + which) * PAIR
            parts[which].append(packed[..., start : start + PAIR])
    return [jnp.concatenate(p, axis=-1) for p in parts]


def to_hidden_order(values, groups=4):
    lead, n = values.shape[:-1], values.shape[-1]
    return jnp.swapaxes(values.reshape(lead + (n // groups, groups)), -1, -2).reshape(lead + (n,))


def from_hidden_order(values, groups=4):
    lead, n = values.shape[:-1], values.shape[-1]
    return jnp.swapaxes(values.reshape(lead + (groups, n // groups)), -1, -2).reshape(lead + (n,))


def pack_weights(weights):
    (qw, qb, kw, vw, vb, ow, ob, g1, s1, iw, ib, uw, ub, g2, s2) = weights
    rows, width = qw.shape
    wide = iw.shape[1]
    vectors = None
    at = 0
    for piece in (qb, vb, ob, g1, s1, ub, g2, s2, ib):
        placed = jnp.pad(piece, (at, wide - at - piece.shape[0]))
        vectors = placed if vectors is None else vectors + placed
        at += piece.shape[0]
    vectors = vectors[None, :]
    return jnp.concatenate(
        [
            jnp.concatenate([interleave_qkv(qw, kw, vw), ow], axis=1),
            to_hidden_order(iw),
            uw.reshape(rows, wide),
            vectors,
        ],
        axis=0,
    )


def gather_weights(weights):
    rows, width = weights[0].shape
    ff_rows, wide = weights[11].shape[0], weights[9].shape[1]
    packed = lax.all_gather(pack_weights(weights), AXES, axis=0, tiled=False)
    shards = packed.shape[0]
    attn = packed[:, 0:rows].reshape(shards * rows, wide)
    inner = packed[:, rows : 2 * rows].reshape(shards * rows, wide)
    outer_rows = packed[:, 2 * rows : 3 * rows].reshape(shards * rows, wide)
    groups = wide // width
    outer = jnp.concatenate(
        [outer_rows[:, c * width : (c + 1) * width] for c in range(groups)], axis=0
    )
    vectors = packed[:, 3 * rows, :].astype(jnp.float32)
    found = []
    at = 0
    for count in (rows,) * 8 + (ff_rows,):
        found.append(vectors[:, at : at + count].reshape(-1))
        at += count
    (qb, vb, ob, g1, s1, ub, g2, s2, ib) = found
    found = dict(
        qkv=attn[:, : 3 * width],
        qkv_bias=interleave_qkv(qb, jnp.zeros_like(qb), vb),
        out=attn[:, 3 * width :],
        out_bias=ob,
        g1=g1,
        s1=s1,
        inner=inner,
        inner_bias=ib.reshape(shards, rows, groups).transpose(2, 0, 1).reshape(-1),
        outer=outer,
        outer_bias=ub,
        g2=g2,
        s2=s2,
    )
    return lax.optimization_barrier(found)


def layer_forward(w, hidden_state):
    rows_low = hidden_state.astype(jnp.bfloat16)
    qkv = (product(rows_low, w["qkv"]) + w["qkv_bias"]).astype(jnp.bfloat16)
    context_low, log_total = attention_forward(qkv)
    attended = product(context_low, w["out"]) + w["out_bias"]
    first_out, first_normed, first_inverse = layer_norm(hidden_state + attended, w["g1"], w["s1"])
    first_low = first_out.astype(jnp.bfloat16)
    inner_pre = product(first_low, w["inner"]) + w["inner_bias"]
    inner_low = gelu_tanh(inner_pre).astype(jnp.bfloat16)
    outer_out = product(inner_low, w["outer"]) + w["outer_bias"]
    result, second_normed, second_inverse = layer_norm(first_out + outer_out, w["g2"], w["s2"])
    kept = dict(
        rows_low=rows_low,
        qkv=qkv,
        log_total=log_total,
        context_low=context_low,
        first_normed=first_normed,
        first_inverse=first_inverse,
        first_low=first_low,
        inner_pre=inner_pre,
        inner_low=inner_low,
        second_normed=second_normed,
        second_inverse=second_inverse,
    )
    return result, kept


def layer_backward(w, kept, upstream):
    second_gain_grad = jnp.sum(upstream * kept["second_normed"], axis=0)
    second_shift_grad = jnp.sum(upstream, axis=0)
    second_grad = norm_backward(upstream, kept["second_normed"], kept["second_inverse"], w["g2"])
    outer_low = second_grad.astype(jnp.bfloat16)
    active_grad = product_nt(outer_low, w["outer"])
    gelu_pull = jax.vjp(gelu_tanh, kept["inner_pre"])[1]
    inner_grad = gelu_pull(active_grad)[0].astype(jnp.bfloat16)
    first_grad = second_grad + product_nt(inner_grad, w["inner"])
    first_gain_grad = jnp.sum(first_grad * kept["first_normed"], axis=0)
    first_shift_grad = jnp.sum(first_grad, axis=0)
    attended_grad = norm_backward(first_grad, kept["first_normed"], kept["first_inverse"], w["g1"])
    attended_low = attended_grad.astype(jnp.bfloat16)
    context_grad = product_nt(attended_low, w["out"]).astype(jnp.bfloat16)
    qkv_grad = attention_backward(kept["qkv"], kept["log_total"], context_grad)
    below_grad = attended_grad + product_nt(qkv_grad, w["qkv"])
    saved = dict(
        outer_low=outer_low,
        inner_grad=inner_grad,
        attended_low=attended_low,
        qkv_grad=qkv_grad,
    )
    norms = (second_gain_grad, second_shift_grad, first_gain_grad, first_shift_grad)
    return below_grad, saved, norms


def scatter_grads(kept, saved, norms, shards):
    def across(source, name):
        return [item[name] for item in source]

    width = kept[0]["context_low"].shape[1]
    three = kept[0]["qkv"].shape[1]
    wide = kept[0]["inner_low"].shape[1]
    blocks = (three + width + 2 * wide) // width
    packed, qkv_b = weight_grad(
        across(kept, "rows_low"), across(saved, "qkv_grad"), columns=blocks * width + PAIR
    )
    at = three // width
    packed, out_b = weight_grad(
        across(kept, "context_low"), across(saved, "attended_low"), into=packed, at=at
    )
    at += 1
    packed, inner_b = weight_grad(
        across(kept, "first_low"), across(saved, "inner_grad"), into=packed, at=at
    )
    at += wide // width
    packed, outer_b = weight_grad(
        across(kept, "inner_low"), across(saved, "outer_low"), into=packed, at=at, stack=True
    )
    rows = width
    q_b, _, v_b = split_qkv(qkv_b[0])
    s2g, s2s, s1g, s1s = [sum(parts) for parts in zip(*norms)]
    columns = jnp.stack([q_b, v_b, out_b[0], s1g, s1s, outer_b[0], s2g, s2s], axis=1)
    inner_cols = inner_b[0].reshape(wide // rows, rows).T
    columns = jnp.concatenate([columns, inner_cols], axis=1)
    columns = jnp.pad(columns, ((0, 0), (0, PAIR - columns.shape[1]))).astype(jnp.bfloat16)
    packed = lax.dynamic_update_slice(packed, columns, (0, blocks * width))
    mine = lax.psum_scatter(packed, AXES, scatter_dimension=0, tiled=True).astype(jnp.float32)
    at = 0
    pieces = []
    for count in (three, width, wide, wide, PAIR):
        pieces.append(mine[:, at : at + count])
        at += count
    qkv_mine, out_mine, inner_mine, outer_mine, col_mine = pieces
    q_w, k_w, v_w = split_qkv(qkv_mine)
    c = [col_mine[:, i] for i in range(8)]
    ib_mine = col_mine[:, 8:12].reshape(-1)
    return (
        q_w,
        c[0],
        k_w,
        v_w,
        c[1],
        out_mine,
        c[2],
        c[3],
        c[4],
        from_hidden_order(inner_mine),
        ib_mine,
        outer_mine.reshape(-1, width),
        c[5],
        c[6],
        c[7],
    )


def per_device(shards, inputs, cotangent, masked, *weights):
    w = gather_weights(weights)
    hidden_state = inputs.astype(jnp.float32)
    kept = []
    for applied in range(LAYERS):
        hidden_state, kept_values = layer_forward(w, hidden_state)
        kept.append(kept_values)
    outputs = hidden_state.astype(jnp.bfloat16)
    upstream = cotangent.astype(jnp.float32) * masked.reshape(-1, 1).astype(jnp.float32)
    saved = [None] * LAYERS
    norms = [None] * LAYERS
    for applied in range(LAYERS - 1, -1, -1):
        upstream, saved[applied], norms[applied] = layer_backward(w, kept[applied], upstream)
    collected = scatter_grads(kept, saved, norms, shards)
    return (outputs, upstream.astype(jnp.bfloat16)) + tuple(collected)


def solution(mesh):
    rows = P(AXES, None)
    vec = P(AXES)
    in_specs = (rows, rows, rows, rows, vec, rows, rows, vec, rows, vec, vec, vec, rows, vec, rows, vec, vec, vec)
    out_specs = (rows, rows, rows, vec, rows, rows, vec, rows, vec, vec, vec, rows, vec, rows, vec, vec, vec)
    shards = mesh.shape["dp"] * mesh.shape["fsdp"]
    return jax.shard_map(
        functools.partial(per_device, shards),
        mesh=mesh,
        in_specs=in_specs,
        out_specs=out_specs,
        check_vma=False,
    )
```

```python
import functools

import jax
import jax.numpy as jnp
from jax import lax
from jax.experimental import pallas as pl
from jax.experimental.pallas import tpu as pltpu
from jax.sharding import PartitionSpec as P

SEQ = 512
HEAD = 64
PAIR = 128
LAYERS = 3
AXES = ("dp", "fsdp")
NT = (((1,), (1,)), ((), ()))
TN = (((0,), (0,)), ((), ()))
norm_epsilon = 1e-05


def product(left, right):
    return jnp.dot(left, right, preferred_element_type=jnp.float32)


def product_nt(left, right):
    return lax.dot_general(left, right, NT, preferred_element_type=jnp.float32)


def gelu_tanh(values):
    return jax.nn.gelu(values, approximate=True)


def layer_norm(summed, gain, shift):
    centre = summed - jnp.mean(summed, axis=-1, keepdims=True)
    inverse = lax.rsqrt(jnp.mean(centre * centre, axis=-1, keepdims=True) + norm_epsilon)
    normed = centre * inverse
    return (normed * gain + shift, normed, inverse)


def norm_backward(upstream, normed, inverse, gain):
    scaled = upstream * gain
    return inverse * (
        scaled
        - jnp.mean(scaled, axis=-1, keepdims=True)
        - normed * jnp.mean(scaled * normed, axis=-1, keepdims=True)
    )


def _head_masks(shape):
    lane = lax.broadcasted_iota(jnp.int32, shape, 1)
    first = lane < HEAD
    return first, jnp.logical_not(first)


def attention_forward_kernel(qkv_ref, ctx_ref, lt_ref):
    scale = HEAD ** (-0.5)
    q = qkv_ref[:, 0:PAIR]
    k = qkv_ref[:, PAIR : 2 * PAIR]
    v = qkv_ref[:, 2 * PAIR : 3 * PAIR]
    masks = _head_masks(q.shape)
    zero = jnp.zeros_like(q)
    context = None
    total = None
    for mask in masks:
        scores = product_nt(jnp.where(mask, q, zero), k) * scale
        top = jnp.max(scores, axis=-1, keepdims=True)
        weights = jnp.exp(scores - top)
        sums = jnp.sum(weights, axis=-1, keepdims=True)
        probs = (weights / sums).astype(jnp.bfloat16)
        part = jnp.dot(probs, v, preferred_element_type=jnp.float32)
        log_total = jnp.broadcast_to(top + jnp.log(sums), part.shape)
        context = part if context is None else jnp.where(mask, part, context)
        total = log_total if total is None else jnp.where(mask, log_total, total)
    ctx_ref[...] = context.astype(ctx_ref.dtype)
    lt_ref[...] = total


def attention_backward_kernel(qkv_ref, lt_ref, g_ref, out_ref):
    scale = HEAD ** (-0.5)
    q = qkv_ref[:, 0:PAIR]
    k = qkv_ref[:, PAIR : 2 * PAIR]
    v = qkv_ref[:, 2 * PAIR : 3 * PAIR]
    g = g_ref[...]
    lt_all = lt_ref[...]
    masks = _head_masks(q.shape)
    zero = jnp.zeros_like(q)
    dq = dk = dv = None
    for mask in masks:
        scores = product_nt(jnp.where(mask, q, zero), k) * scale
        lt = jnp.max(jnp.where(mask, lt_all, -jnp.inf), axis=-1, keepdims=True)
        probs = jnp.exp(scores - lt)
        prob_grad = product_nt(jnp.where(mask, g, zero), v)
        value_part = lax.dot_general(
            probs.astype(jnp.bfloat16), g, TN, preferred_element_type=jnp.float32
        )
        score_grad = (
            probs * (prob_grad - jnp.sum(probs * prob_grad, axis=-1, keepdims=True))
        ).astype(jnp.bfloat16)
        query_part = jnp.dot(score_grad, k, preferred_element_type=jnp.float32) * scale
        key_part = lax.dot_general(score_grad, q, TN, preferred_element_type=jnp.float32) * scale
        if dq is None:
            dq, dk, dv = query_part, key_part, value_part
        else:
            dq = jnp.where(mask, query_part, dq)
            dk = jnp.where(mask, key_part, dk)
            dv = jnp.where(mask, value_part, dv)
    out_ref[:, 0:PAIR] = dq.astype(out_ref.dtype)
    out_ref[:, PAIR : 2 * PAIR] = dk.astype(out_ref.dtype)
    out_ref[:, 2 * PAIR : 3 * PAIR] = dv.astype(out_ref.dtype)


def attention_forward(qkv):
    tokens, width = qkv.shape
    grid = (tokens // SEQ, width // (3 * PAIR))
    steps = grid[0] * grid[1]
    pair = pl.BlockSpec((SEQ, PAIR), lambda s, h: (s, h))
    return pl.pallas_call(
        attention_forward_kernel,
        grid=grid,
        in_specs=[pl.BlockSpec((SEQ, 3 * PAIR), lambda s, h: (s, h))],
        out_specs=[pair, pair],
        out_shape=[
            jax.ShapeDtypeStruct((tokens, width // 3), jnp.bfloat16),
            jax.ShapeDtypeStruct((tokens, width // 3), jnp.float32),
        ],
        compiler_params=pltpu.CompilerParams(dimension_semantics=("parallel", "parallel")),
        cost_estimate=pl.CostEstimate(
            flops=steps * 8 * SEQ * SEQ * PAIR,
            transcendentals=steps * 2 * SEQ * SEQ,
            bytes_accessed=tokens * width * 4,
        ),
        name="attention_forward",
    )(qkv)


def attention_backward(qkv, log_total, context_grad):
    tokens, width = qkv.shape
    grid = (tokens // SEQ, width // (3 * PAIR))
    steps = grid[0] * grid[1]
    pair = pl.BlockSpec((SEQ, PAIR), lambda s, h: (s, h))
    triple = pl.BlockSpec((SEQ, 3 * PAIR), lambda s, h: (s, h))
    return pl.pallas_call(
        attention_backward_kernel,
        grid=grid,
        in_specs=[triple, pair, pair],
        out_specs=triple,
        out_shape=jax.ShapeDtypeStruct((tokens, width), jnp.bfloat16),
        compiler_params=pltpu.CompilerParams(dimension_semantics=("parallel", "parallel")),
        cost_estimate=pl.CostEstimate(
            flops=steps * 20 * SEQ * SEQ * PAIR,
            transcendentals=steps * 2 * SEQ * SEQ,
            bytes_accessed=tokens * width * 6,
        ),
        name="attention_backward",
    )(qkv, log_total, context_grad)


def weight_grad_kernel(*refs):
    count = (len(refs) - 2) // 2
    xs, gs = refs[:count], refs[count : 2 * count]
    out_ref, sum_ref = refs[-2], refs[-1]
    acc = None
    sums = None
    for x_ref, g_ref in zip(xs, gs):
        g = g_ref[...]
        part = lax.dot_general(x_ref[...], g, TN, preferred_element_type=jnp.float32)
        col = jnp.sum(g.astype(jnp.float32), axis=0, keepdims=True)
        acc = part if acc is None else acc + part
        sums = col if sums is None else sums + col
    out_ref[...] = acc.astype(out_ref.dtype)
    sum_ref[...] = sums


def weight_grad(xs, gs, into=None, at=0, stack=False, columns=None, block=768):
    tokens, depth = xs[0].shape
    width = gs[0].shape[1]
    bk = min(block, depth)
    bn = min(block, width)
    grid = (depth // bk, width // bn)
    count = len(xs)
    if stack:
        place = lambda i, j: (0, at + i * grid[1] + j)
        shape = (bk, depth // bk * width)
    else:
        place = lambda i, j: (i, at + j)
        shape = (depth, width)
    if into is not None:
        target = into.shape
    elif columns is not None:
        target = (shape[0], columns)
    else:
        target = shape
    in_specs = [pl.BlockSpec((tokens, bk), lambda i, j: (0, i))] * count + [
        pl.BlockSpec((tokens, bn), lambda i, j: (0, j))
    ] * count
    args = list(xs) + list(gs)
    aliases = {}
    kernel = weight_grad_kernel
    if into is not None:
        in_specs.append(pl.BlockSpec(memory_space=pl.ANY))
        args.append(into)
        aliases = {len(args) - 1: 0}
        kernel = lambda *refs: weight_grad_kernel(*refs[: 2 * count], *refs[2 * count + 1 :])
    return pl.pallas_call(
        kernel,
        grid=grid,
        in_specs=in_specs,
        out_specs=[
            pl.BlockSpec((bk, bn), place),
            pl.BlockSpec((1, bn), lambda i, j: (0, j)),
        ],
        out_shape=[
            jax.ShapeDtypeStruct(target, jnp.bfloat16),
            jax.ShapeDtypeStruct((1, width), jnp.float32),
        ],
        input_output_aliases=aliases,
        compiler_params=pltpu.CompilerParams(
            dimension_semantics=("arbitrary", "arbitrary"), vmem_limit_bytes=48 * 1024 * 1024
        ),
        cost_estimate=pl.CostEstimate(
            flops=2 * count * tokens * depth * width,
            transcendentals=0,
            bytes_accessed=2 * count * tokens * (depth + width) + 2 * depth * width,
        ),
        name="weight_grad",
    )(*args)


def interleave_qkv(q, k, v):
    lead = q.shape[:-1]
    pairs = q.shape[-1] // PAIR
    stacked = jnp.stack([q, k, v], axis=-2).reshape(lead + (3, pairs, PAIR))
    return jnp.swapaxes(stacked, -3, -2).reshape(lead + (3 * pairs * PAIR,))


def split_qkv(packed):
    pairs = packed.shape[-1] // (3 * PAIR)
    parts = [[], [], []]
    for h in range(pairs):
        for which in range(3):
            start = (3 * h + which) * PAIR
            parts[which].append(packed[..., start : start + PAIR])
    return [jnp.concatenate(p, axis=-1) for p in parts]


def to_hidden_order(values, groups=4):
    lead, n = values.shape[:-1], values.shape[-1]
    return jnp.swapaxes(values.reshape(lead + (n // groups, groups)), -1, -2).reshape(lead + (n,))


def from_hidden_order(values, groups=4):
    lead, n = values.shape[:-1], values.shape[-1]
    return jnp.swapaxes(values.reshape(lead + (groups, n // groups)), -1, -2).reshape(lead + (n,))


def pack_weights(weights):
    (qw, qb, kw, vw, vb, ow, ob, g1, s1, iw, ib, uw, ub, g2, s2) = weights
    rows, width = qw.shape
    wide = iw.shape[1]
    columns = jnp.stack([qb, vb, ob, g1, s1, ub, g2, s2], axis=1)
    columns = jnp.concatenate([columns, ib.reshape(rows, -1)], axis=1)
    columns = jnp.pad(columns, ((0, 0), (0, PAIR - columns.shape[1])))
    return jnp.concatenate(
        [interleave_qkv(qw, kw, vw), ow, to_hidden_order(iw), uw.reshape(rows, wide), columns],
        axis=1,
    )


def gather_weights(weights):
    rows, width = weights[0].shape
    wide = weights[9].shape[1]
    packed = lax.all_gather(pack_weights(weights), AXES, axis=0, tiled=True)
    full = packed.shape[0]
    shards = full // rows
    three = 3 * width
    at = 0
    pieces = []
    for count in (three, width, wide, wide, PAIR):
        pieces.append(packed[:, at : at + count])
        at += count
    qkv, out, inner, outer_rows, cols = pieces
    groups = wide // width
    outer = jnp.concatenate(
        [outer_rows[:, c * width : (c + 1) * width] for c in range(groups)], axis=0
    )
    outer = lax.optimization_barrier(outer)
    cols = cols.astype(jnp.float32)
    (qb, vb, ob, g1, s1, ub, g2, s2) = [cols[:, i] for i in range(8)]
    ib = cols[:, 8 : 8 + groups].reshape(shards, rows, groups)
    return dict(
        qkv=qkv,
        qkv_bias=interleave_qkv(qb, jnp.zeros_like(qb), vb),
        out=out,
        out_bias=ob,
        g1=g1,
        s1=s1,
        inner=inner,
        inner_bias=ib.transpose(2, 0, 1).reshape(-1),
        outer=outer,
        outer_bias=ub,
        g2=g2,
        s2=s2,
    )


def layer_forward(w, hidden_state):
    rows_low = hidden_state.astype(jnp.bfloat16)
    qkv = (product(rows_low, w["qkv"]) + w["qkv_bias"]).astype(jnp.bfloat16)
    context_low, log_total = attention_forward(qkv)
    attended = product(context_low, w["out"]) + w["out_bias"]
    first_out, first_normed, first_inverse = layer_norm(hidden_state + attended, w["g1"], w["s1"])
    first_low = first_out.astype(jnp.bfloat16)
    inner_pre = product(first_low, w["inner"]) + w["inner_bias"]
    inner_low = gelu_tanh(inner_pre).astype(jnp.bfloat16)
    outer_out = product(inner_low, w["outer"]) + w["outer_bias"]
    result, second_normed, second_inverse = layer_norm(first_out + outer_out, w["g2"], w["s2"])
    kept = dict(
        rows_low=rows_low,
        qkv=qkv,
        log_total=log_total,
        context_low=context_low,
        first_normed=first_normed,
        first_inverse=first_inverse,
        first_low=first_low,
        inner_pre=inner_pre,
        inner_low=inner_low,
        second_normed=second_normed,
        second_inverse=second_inverse,
    )
    return result, kept


def layer_backward(w, kept, upstream):
    second_gain_grad = jnp.sum(upstream * kept["second_normed"], axis=0)
    second_shift_grad = jnp.sum(upstream, axis=0)
    second_grad = norm_backward(upstream, kept["second_normed"], kept["second_inverse"], w["g2"])
    outer_low = second_grad.astype(jnp.bfloat16)
    active_grad = product_nt(outer_low, w["outer"])
    gelu_pull = jax.vjp(gelu_tanh, kept["inner_pre"])[1]
    inner_grad = gelu_pull(active_grad)[0].astype(jnp.bfloat16)
    first_grad = second_grad + product_nt(inner_grad, w["inner"])
    first_gain_grad = jnp.sum(first_grad * kept["first_normed"], axis=0)
    first_shift_grad = jnp.sum(first_grad, axis=0)
    attended_grad = norm_backward(first_grad, kept["first_normed"], kept["first_inverse"], w["g1"])
    attended_low = attended_grad.astype(jnp.bfloat16)
    context_grad = product_nt(attended_low, w["out"]).astype(jnp.bfloat16)
    qkv_grad = attention_backward(kept["qkv"], kept["log_total"], context_grad)
    below_grad = attended_grad + product_nt(qkv_grad, w["qkv"])
    saved = dict(
        outer_low=outer_low,
        inner_grad=inner_grad,
        attended_low=attended_low,
        qkv_grad=qkv_grad,
    )
    norms = (second_gain_grad, second_shift_grad, first_gain_grad, first_shift_grad)
    return below_grad, saved, norms


def scatter_grads(kept, saved, norms, shards):
    def across(source, name):
        return [item[name] for item in source]

    width = kept[0]["context_low"].shape[1]
    three = kept[0]["qkv"].shape[1]
    wide = kept[0]["inner_low"].shape[1]
    blocks = (three + width + 2 * wide) // width
    packed, qkv_b = weight_grad(
        across(kept, "rows_low"), across(saved, "qkv_grad"), columns=blocks * width + PAIR
    )
    at = three // width
    packed, out_b = weight_grad(
        across(kept, "context_low"), across(saved, "attended_low"), into=packed, at=at
    )
    at += 1
    packed, inner_b = weight_grad(
        across(kept, "first_low"), across(saved, "inner_grad"), into=packed, at=at
    )
    at += wide // width
    packed, outer_b = weight_grad(
        across(kept, "inner_low"), across(saved, "outer_low"), into=packed, at=at, stack=True
    )
    rows = width
    q_b, _, v_b = split_qkv(qkv_b[0])
    s2g, s2s, s1g, s1s = [sum(parts) for parts in zip(*norms)]
    columns = jnp.stack([q_b, v_b, out_b[0], s1g, s1s, outer_b[0], s2g, s2s], axis=1)
    inner_cols = inner_b[0].reshape(wide // rows, rows).T
    columns = jnp.concatenate([columns, inner_cols], axis=1)
    columns = jnp.pad(columns, ((0, 0), (0, PAIR - columns.shape[1]))).astype(jnp.bfloat16)
    packed = lax.dynamic_update_slice(packed, columns, (0, blocks * width))
    mine = lax.psum_scatter(packed, AXES, scatter_dimension=0, tiled=True).astype(jnp.float32)
    at = 0
    pieces = []
    for count in (three, width, wide, wide, PAIR):
        pieces.append(mine[:, at : at + count])
        at += count
    qkv_mine, out_mine, inner_mine, outer_mine, col_mine = pieces
    q_w, k_w, v_w = split_qkv(qkv_mine)
    c = [col_mine[:, i] for i in range(8)]
    ib_mine = col_mine[:, 8:12].reshape(-1)
    return (
        q_w,
        c[0],
        k_w,
        v_w,
        c[1],
        out_mine,
        c[2],
        c[3],
        c[4],
        from_hidden_order(inner_mine),
        ib_mine,
        outer_mine.reshape(-1, width),
        c[5],
        c[6],
        c[7],
    )


def per_device(shards, inputs, cotangent, masked, *weights):
    w = gather_weights(weights)
    hidden_state = inputs.astype(jnp.float32)
    kept = []
    for applied in range(LAYERS):
        hidden_state, kept_values = layer_forward(w, hidden_state)
        kept.append(kept_values)
    outputs = hidden_state.astype(jnp.bfloat16)
    upstream = cotangent.astype(jnp.float32) * masked.reshape(-1, 1).astype(jnp.float32)
    saved = [None] * LAYERS
    norms = [None] * LAYERS
    for applied in range(LAYERS - 1, -1, -1):
        upstream, saved[applied], norms[applied] = layer_backward(w, kept[applied], upstream)
    collected = scatter_grads(kept, saved, norms, shards)
    return (outputs, upstream.astype(jnp.bfloat16)) + tuple(collected)


def solution(mesh):
    rows = P(AXES, None)
    vec = P(AXES)
    in_specs = (rows, rows, rows, rows, vec, rows, rows, vec, rows, vec, vec, vec, rows, vec, rows, vec, vec, vec)
    out_specs = (rows, rows, rows, vec, rows, rows, vec, rows, vec, vec, vec, rows, vec, rows, vec, vec, vec)
    shards = mesh.shape["dp"] * mesh.shape["fsdp"]
    return jax.shard_map(
        functools.partial(per_device, shards),
        mesh=mesh,
        in_specs=in_specs,
        out_specs=out_specs,
        check_vma=False,
    )
```

```python
import functools

import jax
import jax.numpy as jnp
from jax import lax
from jax.experimental import pallas as pl
from jax.experimental.pallas import tpu as pltpu
from jax.sharding import PartitionSpec as P

SEQ = 512
HEAD = 64
PAIR = 128
LAYERS = 3
AXES = ("dp", "fsdp")
NT = (((1,), (1,)), ((), ()))
TN = (((0,), (0,)), ((), ()))
norm_epsilon = 1e-05


def product(left, right):
    return jnp.dot(left, right, preferred_element_type=jnp.float32)


def product_nt(left, right):
    return lax.dot_general(left, right, NT, preferred_element_type=jnp.float32)


def gelu_tanh(values):
    return jax.nn.gelu(values, approximate=True)


def layer_norm(summed, gain, shift):
    centre = summed - jnp.mean(summed, axis=-1, keepdims=True)
    inverse = lax.rsqrt(jnp.mean(centre * centre, axis=-1, keepdims=True) + norm_epsilon)
    normed = centre * inverse
    return (normed * gain + shift, normed, inverse)


def norm_backward(upstream, normed, inverse, gain):
    scaled = upstream * gain
    return inverse * (
        scaled
        - jnp.mean(scaled, axis=-1, keepdims=True)
        - normed * jnp.mean(scaled * normed, axis=-1, keepdims=True)
    )


def _head_masks(shape):
    lane = lax.broadcasted_iota(jnp.int32, shape, 1)
    first = lane < HEAD
    return first, jnp.logical_not(first)


def attention_forward_kernel(qkv_ref, ctx_ref, lt_ref):
    scale = HEAD ** (-0.5)
    q = qkv_ref[:, 0:PAIR]
    k = qkv_ref[:, PAIR : 2 * PAIR]
    v = qkv_ref[:, 2 * PAIR : 3 * PAIR]
    masks = _head_masks(q.shape)
    zero = jnp.zeros_like(q)
    context = None
    total = None
    for mask in masks:
        scores = product_nt(jnp.where(mask, q, zero), k) * scale
        top = jnp.max(scores, axis=-1, keepdims=True)
        weights = jnp.exp(scores - top)
        sums = jnp.sum(weights, axis=-1, keepdims=True)
        probs = (weights / sums).astype(jnp.bfloat16)
        part = jnp.dot(probs, v, preferred_element_type=jnp.float32)
        log_total = jnp.broadcast_to(top + jnp.log(sums), part.shape)
        context = part if context is None else jnp.where(mask, part, context)
        total = log_total if total is None else jnp.where(mask, log_total, total)
    ctx_ref[...] = context.astype(ctx_ref.dtype)
    lt_ref[...] = total


def attention_backward_kernel(qkv_ref, lt_ref, g_ref, out_ref):
    scale = HEAD ** (-0.5)
    q = qkv_ref[:, 0:PAIR]
    k = qkv_ref[:, PAIR : 2 * PAIR]
    v = qkv_ref[:, 2 * PAIR : 3 * PAIR]
    g = g_ref[...]
    lt_t = lt_ref[...].T
    masks = _head_masks(q.shape)
    zero = jnp.zeros_like(q)
    dq = dk = dv = None
    for h, mask in enumerate(masks):
        lt_row = lt_t[h * HEAD : h * HEAD + 1, :]
        scores_t = product_nt(jnp.where(mask, k, zero), q) * scale
        probs_t = jnp.exp(scores_t - lt_row)
        prob_grad_t = product_nt(jnp.where(mask, v, zero), g)
        value_part = jnp.dot(probs_t.astype(jnp.bfloat16), g, preferred_element_type=jnp.float32)
        row_sums = jnp.sum(probs_t * prob_grad_t, axis=0, keepdims=True)
        score_grad_t = (probs_t * (prob_grad_t - row_sums)).astype(jnp.bfloat16)
        key_part = jnp.dot(score_grad_t, q, preferred_element_type=jnp.float32) * scale
        query_part = lax.dot_general(score_grad_t, k, TN, preferred_element_type=jnp.float32) * scale
        if dq is None:
            dq, dk, dv = query_part, key_part, value_part
        else:
            dq = jnp.where(mask, query_part, dq)
            dk = jnp.where(mask, key_part, dk)
            dv = jnp.where(mask, value_part, dv)
    out_ref[:, 0:PAIR] = dq.astype(out_ref.dtype)
    out_ref[:, PAIR : 2 * PAIR] = dk.astype(out_ref.dtype)
    out_ref[:, 2 * PAIR : 3 * PAIR] = dv.astype(out_ref.dtype)


def attention_forward(qkv):
    tokens, width = qkv.shape
    grid = (tokens // SEQ, width // (3 * PAIR))
    steps = grid[0] * grid[1]
    pair = pl.BlockSpec((SEQ, PAIR), lambda s, h: (s, h))
    return pl.pallas_call(
        attention_forward_kernel,
        grid=grid,
        in_specs=[pl.BlockSpec((SEQ, 3 * PAIR), lambda s, h: (s, h))],
        out_specs=[pair, pair],
        out_shape=[
            jax.ShapeDtypeStruct((tokens, width // 3), jnp.bfloat16),
            jax.ShapeDtypeStruct((tokens, width // 3), jnp.float32),
        ],
        compiler_params=pltpu.CompilerParams(dimension_semantics=("parallel", "parallel")),
        cost_estimate=pl.CostEstimate(
            flops=steps * 8 * SEQ * SEQ * PAIR,
            transcendentals=steps * 2 * SEQ * SEQ,
            bytes_accessed=tokens * width * 4,
        ),
        name="attention_forward",
    )(qkv)


def attention_backward(qkv, log_total, context_grad):
    tokens, width = qkv.shape
    grid = (tokens // SEQ, width // (3 * PAIR))
    steps = grid[0] * grid[1]
    pair = pl.BlockSpec((SEQ, PAIR), lambda s, h: (s, h))
    triple = pl.BlockSpec((SEQ, 3 * PAIR), lambda s, h: (s, h))
    return pl.pallas_call(
        attention_backward_kernel,
        grid=grid,
        in_specs=[triple, pair, pair],
        out_specs=triple,
        out_shape=jax.ShapeDtypeStruct((tokens, width), jnp.bfloat16),
        compiler_params=pltpu.CompilerParams(dimension_semantics=("parallel", "parallel")),
        cost_estimate=pl.CostEstimate(
            flops=steps * 20 * SEQ * SEQ * PAIR,
            transcendentals=steps * 2 * SEQ * SEQ,
            bytes_accessed=tokens * width * 6,
        ),
        name="attention_backward",
    )(qkv, log_total, context_grad)


def weight_grad_kernel(*refs):
    count = (len(refs) - 2) // 2
    xs, gs = refs[:count], refs[count : 2 * count]
    out_ref, sum_ref = refs[-2], refs[-1]
    acc = None
    sums = None
    for x_ref, g_ref in zip(xs, gs):
        g = g_ref[...]
        part = lax.dot_general(x_ref[...], g, TN, preferred_element_type=jnp.float32)
        col = jnp.sum(g.astype(jnp.float32), axis=0, keepdims=True)
        acc = part if acc is None else acc + part
        sums = col if sums is None else sums + col
    out_ref[...] = acc.astype(out_ref.dtype)
    sum_ref[...] = sums


def weight_grad(xs, gs, into=None, at=0, stack=False, columns=None, block=768):
    tokens, depth = xs[0].shape
    width = gs[0].shape[1]
    bk = min(block, depth)
    bn = min(block, width)
    grid = (depth // bk, width // bn)
    count = len(xs)
    if stack:
        place = lambda i, j: (0, at + i * grid[1] + j)
        shape = (bk, depth // bk * width)
    else:
        place = lambda i, j: (i, at + j)
        shape = (depth, width)
    if into is not None:
        target = into.shape
    elif columns is not None:
        target = (shape[0], columns)
    else:
        target = shape
    in_specs = [pl.BlockSpec((tokens, bk), lambda i, j: (0, i))] * count + [
        pl.BlockSpec((tokens, bn), lambda i, j: (0, j))
    ] * count
    args = list(xs) + list(gs)
    aliases = {}
    kernel = weight_grad_kernel
    if into is not None:
        in_specs.append(pl.BlockSpec(memory_space=pl.ANY))
        args.append(into)
        aliases = {len(args) - 1: 0}
        kernel = lambda *refs: weight_grad_kernel(*refs[: 2 * count], *refs[2 * count + 1 :])
    return pl.pallas_call(
        kernel,
        grid=grid,
        in_specs=in_specs,
        out_specs=[
            pl.BlockSpec((bk, bn), place),
            pl.BlockSpec((1, bn), lambda i, j: (0, j)),
        ],
        out_shape=[
            jax.ShapeDtypeStruct(target, jnp.bfloat16),
            jax.ShapeDtypeStruct((1, width), jnp.float32),
        ],
        input_output_aliases=aliases,
        compiler_params=pltpu.CompilerParams(
            dimension_semantics=("arbitrary", "arbitrary"), vmem_limit_bytes=48 * 1024 * 1024
        ),
        cost_estimate=pl.CostEstimate(
            flops=2 * count * tokens * depth * width,
            transcendentals=0,
            bytes_accessed=2 * count * tokens * (depth + width) + 2 * depth * width,
        ),
        name="weight_grad",
    )(*args)


def interleave_qkv(q, k, v):
    lead = q.shape[:-1]
    pairs = q.shape[-1] // PAIR
    stacked = jnp.stack([q, k, v], axis=-2).reshape(lead + (3, pairs, PAIR))
    return jnp.swapaxes(stacked, -3, -2).reshape(lead + (3 * pairs * PAIR,))


def split_qkv(packed):
    pairs = packed.shape[-1] // (3 * PAIR)
    parts = [[], [], []]
    for h in range(pairs):
        for which in range(3):
            start = (3 * h + which) * PAIR
            parts[which].append(packed[..., start : start + PAIR])
    return [jnp.concatenate(p, axis=-1) for p in parts]


def to_hidden_order(values, groups=4):
    lead, n = values.shape[:-1], values.shape[-1]
    return jnp.swapaxes(values.reshape(lead + (n // groups, groups)), -1, -2).reshape(lead + (n,))


def from_hidden_order(values, groups=4):
    lead, n = values.shape[:-1], values.shape[-1]
    return jnp.swapaxes(values.reshape(lead + (groups, n // groups)), -1, -2).reshape(lead + (n,))


def pack_weights(weights):
    (qw, qb, kw, vw, vb, ow, ob, g1, s1, iw, ib, uw, ub, g2, s2) = weights
    rows, width = qw.shape
    wide = iw.shape[1]
    columns = jnp.stack([qb, vb, ob, g1, s1, ub, g2, s2], axis=1)
    columns = jnp.concatenate([columns, ib.reshape(rows, -1)], axis=1)
    columns = jnp.pad(columns, ((0, 0), (0, PAIR - columns.shape[1])))
    return jnp.concatenate(
        [interleave_qkv(qw, kw, vw), ow, to_hidden_order(iw), uw.reshape(rows, wide), columns],
        axis=1,
    )


def gather_weights(weights):
    rows, width = weights[0].shape
    wide = weights[9].shape[1]
    packed = lax.all_gather(pack_weights(weights), AXES, axis=0, tiled=True)
    full = packed.shape[0]
    shards = full // rows
    three = 3 * width
    at = 0
    pieces = []
    for count in (three, width, wide, wide, PAIR):
        pieces.append(packed[:, at : at + count])
        at += count
    qkv, out, inner, outer_rows, cols = pieces
    groups = wide // width
    outer = jnp.concatenate(
        [outer_rows[:, c * width : (c + 1) * width] for c in range(groups)], axis=0
    )
    outer = lax.optimization_barrier(outer)
    cols = cols.astype(jnp.float32)
    (qb, vb, ob, g1, s1, ub, g2, s2) = [cols[:, i] for i in range(8)]
    ib = cols[:, 8 : 8 + groups].reshape(shards, rows, groups)
    return dict(
        qkv=qkv,
        qkv_bias=interleave_qkv(qb, jnp.zeros_like(qb), vb),
        out=out,
        out_bias=ob,
        g1=g1,
        s1=s1,
        inner=inner,
        inner_bias=ib.transpose(2, 0, 1).reshape(-1),
        outer=outer,
        outer_bias=ub,
        g2=g2,
        s2=s2,
    )


def layer_forward(w, hidden_state):
    rows_low = hidden_state.astype(jnp.bfloat16)
    qkv = (product(rows_low, w["qkv"]) + w["qkv_bias"]).astype(jnp.bfloat16)
    context_low, log_total = attention_forward(qkv)
    attended = product(context_low, w["out"]) + w["out_bias"]
    first_out, first_normed, first_inverse = layer_norm(hidden_state + attended, w["g1"], w["s1"])
    first_low = first_out.astype(jnp.bfloat16)
    inner_pre = product(first_low, w["inner"]) + w["inner_bias"]
    inner_low = gelu_tanh(inner_pre).astype(jnp.bfloat16)
    outer_out = product(inner_low, w["outer"]) + w["outer_bias"]
    result, second_normed, second_inverse = layer_norm(first_out + outer_out, w["g2"], w["s2"])
    kept = dict(
        rows_low=rows_low,
        qkv=qkv,
        log_total=log_total,
        context_low=context_low,
        first_normed=first_normed,
        first_inverse=first_inverse,
        first_low=first_low,
        inner_pre=inner_pre,
        inner_low=inner_low,
        second_normed=second_normed,
        second_inverse=second_inverse,
    )
    return result, kept


def layer_backward(w, kept, upstream):
    second_gain_grad = jnp.sum(upstream * kept["second_normed"], axis=0)
    second_shift_grad = jnp.sum(upstream, axis=0)
    second_grad = norm_backward(upstream, kept["second_normed"], kept["second_inverse"], w["g2"])
    outer_low = second_grad.astype(jnp.bfloat16)
    active_grad = product_nt(outer_low, w["outer"])
    gelu_pull = jax.vjp(gelu_tanh, kept["inner_pre"])[1]
    inner_grad = gelu_pull(active_grad)[0].astype(jnp.bfloat16)
    first_grad = second_grad + product_nt(inner_grad, w["inner"])
    first_gain_grad = jnp.sum(first_grad * kept["first_normed"], axis=0)
    first_shift_grad = jnp.sum(first_grad, axis=0)
    attended_grad = norm_backward(first_grad, kept["first_normed"], kept["first_inverse"], w["g1"])
    attended_low = attended_grad.astype(jnp.bfloat16)
    context_grad = product_nt(attended_low, w["out"]).astype(jnp.bfloat16)
    qkv_grad = attention_backward(kept["qkv"], kept["log_total"], context_grad)
    below_grad = attended_grad + product_nt(qkv_grad, w["qkv"])
    saved = dict(
        outer_low=outer_low,
        inner_grad=inner_grad,
        attended_low=attended_low,
        qkv_grad=qkv_grad,
    )
    norms = (second_gain_grad, second_shift_grad, first_gain_grad, first_shift_grad)
    return below_grad, saved, norms


def scatter_grads(kept, saved, norms, shards):
    def across(source, name):
        return [item[name] for item in source]

    width = kept[0]["context_low"].shape[1]
    three = kept[0]["qkv"].shape[1]
    wide = kept[0]["inner_low"].shape[1]
    blocks = (three + width + 2 * wide) // width
    packed, qkv_b = weight_grad(
        across(kept, "rows_low"), across(saved, "qkv_grad"), columns=blocks * width + PAIR
    )
    at = three // width
    packed, out_b = weight_grad(
        across(kept, "context_low"), across(saved, "attended_low"), into=packed, at=at
    )
    at += 1
    packed, inner_b = weight_grad(
        across(kept, "first_low"), across(saved, "inner_grad"), into=packed, at=at
    )
    at += wide // width
    packed, outer_b = weight_grad(
        across(kept, "inner_low"), across(saved, "outer_low"), into=packed, at=at, stack=True
    )
    rows = width
    q_b, _, v_b = split_qkv(qkv_b[0])
    s2g, s2s, s1g, s1s = [sum(parts) for parts in zip(*norms)]
    columns = jnp.stack([q_b, v_b, out_b[0], s1g, s1s, outer_b[0], s2g, s2s], axis=1)
    inner_cols = inner_b[0].reshape(wide // rows, rows).T
    columns = jnp.concatenate([columns, inner_cols], axis=1)
    columns = jnp.pad(columns, ((0, 0), (0, PAIR - columns.shape[1]))).astype(jnp.bfloat16)
    packed = lax.dynamic_update_slice(packed, columns, (0, blocks * width))
    mine = lax.psum_scatter(packed, AXES, scatter_dimension=0, tiled=True).astype(jnp.float32)
    at = 0
    pieces = []
    for count in (three, width, wide, wide, PAIR):
        pieces.append(mine[:, at : at + count])
        at += count
    qkv_mine, out_mine, inner_mine, outer_mine, col_mine = pieces
    q_w, k_w, v_w = split_qkv(qkv_mine)
    c = [col_mine[:, i] for i in range(8)]
    ib_mine = col_mine[:, 8:12].reshape(-1)
    return (
        q_w,
        c[0],
        k_w,
        v_w,
        c[1],
        out_mine,
        c[2],
        c[3],
        c[4],
        from_hidden_order(inner_mine),
        ib_mine,
        outer_mine.reshape(-1, width),
        c[5],
        c[6],
        c[7],
    )


def per_device(shards, inputs, cotangent, masked, *weights):
    w = gather_weights(weights)
    hidden_state = inputs.astype(jnp.float32)
    kept = []
    for applied in range(LAYERS):
        hidden_state, kept_values = layer_forward(w, hidden_state)
        kept.append(kept_values)
    outputs = hidden_state.astype(jnp.bfloat16)
    upstream = cotangent.astype(jnp.float32) * masked.reshape(-1, 1).astype(jnp.float32)
    saved = [None] * LAYERS
    norms = [None] * LAYERS
    for applied in range(LAYERS - 1, -1, -1):
        upstream, saved[applied], norms[applied] = layer_backward(w, kept[applied], upstream)
    collected = scatter_grads(kept, saved, norms, shards)
    return (outputs, upstream.astype(jnp.bfloat16)) + tuple(collected)


def solution(mesh):
    rows = P(AXES, None)
    vec = P(AXES)
    in_specs = (rows, rows, rows, rows, vec, rows, rows, vec, rows, vec, vec, vec, rows, vec, rows, vec, vec, vec)
    out_specs = (rows, rows, rows, vec, rows, rows, vec, rows, vec, vec, vec, rows, vec, rows, vec, vec, vec)
    shards = mesh.shape["dp"] * mesh.shape["fsdp"]
    return jax.shard_map(
        functools.partial(per_device, shards),
        mesh=mesh,
        in_specs=in_specs,
        out_specs=out_specs,
        check_vma=False,
    )
```

```python
import functools

import jax
import jax.numpy as jnp
import numpy as np
from jax import lax
from jax.experimental import pallas as pl
from jax.experimental.pallas import tpu as pltpu
from jax.sharding import PartitionSpec as P

SEQ = 512
HEAD = 64
PAIR = 128
LAYERS = 3
AXES = ("dp", "fsdp")
NT = (((1,), (1,)), ((), ()))
TN = (((0,), (0,)), ((), ()))
norm_epsilon = 1e-05


def product(left, right):
    return jnp.dot(left, right, preferred_element_type=jnp.float32)


def product_nt(left, right):
    return lax.dot_general(left, right, NT, preferred_element_type=jnp.float32)


def gelu_tanh(values):
    root = np.sqrt(2 / np.pi).astype(np.float32)
    cube = values * values * values
    bent = jnp.tanh(root * (values + 0.044715 * cube))
    cdf = 0.5 * (1.0 + bent)
    slope = cdf + values * (0.5 * (1.0 - bent * bent) * root * (1.0 + 3 * 0.044715 * values * values))
    return values * cdf, slope


def layer_norm(summed, gain, shift):
    centre = summed - jnp.mean(summed, axis=-1, keepdims=True)
    inverse = lax.rsqrt(jnp.mean(centre * centre, axis=-1, keepdims=True) + norm_epsilon)
    normed = centre * inverse
    return (normed * gain + shift, normed, inverse)


def norm_backward(upstream, normed, inverse, gain):
    scaled = upstream * gain
    return inverse * (
        scaled
        - jnp.mean(scaled, axis=-1, keepdims=True)
        - normed * jnp.mean(scaled * normed, axis=-1, keepdims=True)
    )


def _head_masks(shape):
    lane = lax.broadcasted_iota(jnp.int32, shape, 1)
    first = lane < HEAD
    return first, jnp.logical_not(first)


def attention_forward_kernel(qkv_ref, ctx_ref, lt_ref):
    scale = HEAD ** (-0.5)
    q = qkv_ref[:, 0:PAIR]
    k = qkv_ref[:, PAIR : 2 * PAIR]
    v = qkv_ref[:, 2 * PAIR : 3 * PAIR]
    masks = _head_masks(q.shape)
    zero = jnp.zeros_like(q)
    context = None
    total = None
    for mask in masks:
        scores = product_nt(jnp.where(mask, q, zero), k) * scale
        top = jnp.max(scores, axis=-1, keepdims=True)
        weights = jnp.exp(scores - top)
        sums = jnp.sum(weights, axis=-1, keepdims=True)
        probs = (weights / sums).astype(jnp.bfloat16)
        part = jnp.dot(probs, v, preferred_element_type=jnp.float32)
        log_total = jnp.broadcast_to(top + jnp.log(sums), part.shape)
        context = part if context is None else jnp.where(mask, part, context)
        total = log_total if total is None else jnp.where(mask, log_total, total)
    ctx_ref[...] = context.astype(ctx_ref.dtype)
    lt_ref[...] = total


def attention_backward_kernel(qkv_ref, lt_ref, g_ref, out_ref):
    scale = HEAD ** (-0.5)
    q = qkv_ref[:, 0:PAIR]
    k = qkv_ref[:, PAIR : 2 * PAIR]
    v = qkv_ref[:, 2 * PAIR : 3 * PAIR]
    g = g_ref[...]
    lt_t = lt_ref[...].T
    masks = _head_masks(q.shape)
    zero = jnp.zeros_like(q)
    dq = dk = dv = None
    for h, mask in enumerate(masks):
        lt_row = lt_t[h * HEAD : h * HEAD + 1, :]
        scores_t = product_nt(jnp.where(mask, k, zero), q) * scale
        probs_t = jnp.exp(scores_t - lt_row)
        prob_grad_t = product_nt(jnp.where(mask, v, zero), g)
        value_part = jnp.dot(probs_t.astype(jnp.bfloat16), g, preferred_element_type=jnp.float32)
        row_sums = jnp.sum(probs_t * prob_grad_t, axis=0, keepdims=True)
        score_grad_t = (probs_t * (prob_grad_t - row_sums)).astype(jnp.bfloat16)
        key_part = jnp.dot(score_grad_t, q, preferred_element_type=jnp.float32) * scale
        query_part = lax.dot_general(score_grad_t, k, TN, preferred_element_type=jnp.float32) * scale
        if dq is None:
            dq, dk, dv = query_part, key_part, value_part
        else:
            dq = jnp.where(mask, query_part, dq)
            dk = jnp.where(mask, key_part, dk)
            dv = jnp.where(mask, value_part, dv)
    out_ref[:, 0:PAIR] = dq.astype(out_ref.dtype)
    out_ref[:, PAIR : 2 * PAIR] = dk.astype(out_ref.dtype)
    out_ref[:, 2 * PAIR : 3 * PAIR] = dv.astype(out_ref.dtype)


def attention_forward(qkv):
    tokens, width = qkv.shape
    grid = (tokens // SEQ, width // (3 * PAIR))
    steps = grid[0] * grid[1]
    pair = pl.BlockSpec((SEQ, PAIR), lambda s, h: (s, h))
    return pl.pallas_call(
        attention_forward_kernel,
        grid=grid,
        in_specs=[pl.BlockSpec((SEQ, 3 * PAIR), lambda s, h: (s, h))],
        out_specs=[pair, pair],
        out_shape=[
            jax.ShapeDtypeStruct((tokens, width // 3), jnp.bfloat16),
            jax.ShapeDtypeStruct((tokens, width // 3), jnp.float32),
        ],
        compiler_params=pltpu.CompilerParams(dimension_semantics=("parallel", "parallel")),
        cost_estimate=pl.CostEstimate(
            flops=steps * 8 * SEQ * SEQ * PAIR,
            transcendentals=steps * 2 * SEQ * SEQ,
            bytes_accessed=tokens * width * 4,
        ),
        name="attention_forward",
    )(qkv)


def attention_backward(qkv, log_total, context_grad):
    tokens, width = qkv.shape
    grid = (tokens // SEQ, width // (3 * PAIR))
    steps = grid[0] * grid[1]
    pair = pl.BlockSpec((SEQ, PAIR), lambda s, h: (s, h))
    triple = pl.BlockSpec((SEQ, 3 * PAIR), lambda s, h: (s, h))
    return pl.pallas_call(
        attention_backward_kernel,
        grid=grid,
        in_specs=[triple, pair, pair],
        out_specs=triple,
        out_shape=jax.ShapeDtypeStruct((tokens, width), jnp.bfloat16),
        compiler_params=pltpu.CompilerParams(dimension_semantics=("parallel", "parallel")),
        cost_estimate=pl.CostEstimate(
            flops=steps * 20 * SEQ * SEQ * PAIR,
            transcendentals=steps * 2 * SEQ * SEQ,
            bytes_accessed=tokens * width * 6,
        ),
        name="attention_backward",
    )(qkv, log_total, context_grad)


def weight_grad_kernel(*refs):
    count = (len(refs) - 2) // 2
    xs, gs = refs[:count], refs[count : 2 * count]
    out_ref, sum_ref = refs[-2], refs[-1]
    acc = None
    sums = None
    for x_ref, g_ref in zip(xs, gs):
        g = g_ref[...]
        part = lax.dot_general(x_ref[...], g, TN, preferred_element_type=jnp.float32)
        col = jnp.sum(g.astype(jnp.float32), axis=0, keepdims=True)
        acc = part if acc is None else acc + part
        sums = col if sums is None else sums + col
    out_ref[...] = acc.astype(out_ref.dtype)
    sum_ref[...] = sums


def weight_grad(xs, gs, into=None, at=0, stack=False, columns=None, block=768):
    tokens, depth = xs[0].shape
    width = gs[0].shape[1]
    bk = min(block, depth)
    bn = min(block, width)
    grid = (depth // bk, width // bn)
    count = len(xs)
    if stack:
        place = lambda i, j: (0, at + i * grid[1] + j)
        shape = (bk, depth // bk * width)
    else:
        place = lambda i, j: (i, at + j)
        shape = (depth, width)
    if into is not None:
        target = into.shape
    elif columns is not None:
        target = (shape[0], columns)
    else:
        target = shape
    in_specs = [pl.BlockSpec((tokens, bk), lambda i, j: (0, i))] * count + [
        pl.BlockSpec((tokens, bn), lambda i, j: (0, j))
    ] * count
    args = list(xs) + list(gs)
    aliases = {}
    kernel = weight_grad_kernel
    if into is not None:
        in_specs.append(pl.BlockSpec(memory_space=pl.ANY))
        args.append(into)
        aliases = {len(args) - 1: 0}
        kernel = lambda *refs: weight_grad_kernel(*refs[: 2 * count], *refs[2 * count + 1 :])
    return pl.pallas_call(
        kernel,
        grid=grid,
        in_specs=in_specs,
        out_specs=[
            pl.BlockSpec((bk, bn), place),
            pl.BlockSpec((1, bn), lambda i, j: (0, j)),
        ],
        out_shape=[
            jax.ShapeDtypeStruct(target, jnp.bfloat16),
            jax.ShapeDtypeStruct((1, width), jnp.float32),
        ],
        input_output_aliases=aliases,
        compiler_params=pltpu.CompilerParams(
            dimension_semantics=("arbitrary", "arbitrary"), vmem_limit_bytes=48 * 1024 * 1024
        ),
        cost_estimate=pl.CostEstimate(
            flops=2 * count * tokens * depth * width,
            transcendentals=0,
            bytes_accessed=2 * count * tokens * (depth + width) + 2 * depth * width,
        ),
        name="weight_grad",
    )(*args)


def interleave_qkv(q, k, v):
    lead = q.shape[:-1]
    pairs = q.shape[-1] // PAIR
    stacked = jnp.stack([q, k, v], axis=-2).reshape(lead + (3, pairs, PAIR))
    return jnp.swapaxes(stacked, -3, -2).reshape(lead + (3 * pairs * PAIR,))


def split_qkv(packed):
    pairs = packed.shape[-1] // (3 * PAIR)
    parts = [[], [], []]
    for h in range(pairs):
        for which in range(3):
            start = (3 * h + which) * PAIR
            parts[which].append(packed[..., start : start + PAIR])
    return [jnp.concatenate(p, axis=-1) for p in parts]


def to_hidden_order(values, groups=4):
    lead, n = values.shape[:-1], values.shape[-1]
    return jnp.swapaxes(values.reshape(lead + (n // groups, groups)), -1, -2).reshape(lead + (n,))


def from_hidden_order(values, groups=4):
    lead, n = values.shape[:-1], values.shape[-1]
    return jnp.swapaxes(values.reshape(lead + (groups, n // groups)), -1, -2).reshape(lead + (n,))


def pack_weights(weights):
    (qw, qb, kw, vw, vb, ow, ob, g1, s1, iw, ib, uw, ub, g2, s2) = weights
    rows, width = qw.shape
    wide = iw.shape[1]
    columns = jnp.stack([qb, vb, ob, g1, s1, ub, g2, s2], axis=1)
    columns = jnp.concatenate([columns, ib.reshape(rows, -1)], axis=1)
    columns = jnp.pad(columns, ((0, 0), (0, PAIR - columns.shape[1])))
    return jnp.concatenate(
        [interleave_qkv(qw, kw, vw), ow, to_hidden_order(iw), uw.reshape(rows, wide), columns],
        axis=1,
    )


def gather_weights(weights):
    rows, width = weights[0].shape
    wide = weights[9].shape[1]
    packed = lax.all_gather(pack_weights(weights), AXES, axis=0, tiled=True)
    full = packed.shape[0]
    shards = full // rows
    three = 3 * width
    at = 0
    pieces = []
    for count in (three, width, wide, wide, PAIR):
        pieces.append(packed[:, at : at + count])
        at += count
    qkv, out, inner, outer_rows, cols = pieces
    groups = wide // width
    outer = jnp.concatenate(
        [outer_rows[:, c * width : (c + 1) * width] for c in range(groups)], axis=0
    )
    outer = lax.optimization_barrier(outer)
    cols = cols.astype(jnp.float32)
    (qb, vb, ob, g1, s1, ub, g2, s2) = [cols[:, i] for i in range(8)]
    ib = cols[:, 8 : 8 + groups].reshape(shards, rows, groups)
    return dict(
        qkv=qkv,
        qkv_bias=interleave_qkv(qb, jnp.zeros_like(qb), vb),
        out=out,
        out_bias=ob,
        g1=g1,
        s1=s1,
        inner=inner,
        inner_bias=ib.transpose(2, 0, 1).reshape(-1),
        outer=outer,
        outer_bias=ub,
        g2=g2,
        s2=s2,
    )


def layer_forward(w, hidden_state):
    rows_low = hidden_state.astype(jnp.bfloat16)
    qkv = (product(rows_low, w["qkv"]) + w["qkv_bias"]).astype(jnp.bfloat16)
    context_low, log_total = attention_forward(qkv)
    attended = product(context_low, w["out"]) + w["out_bias"]
    first_out, first_normed, first_inverse = layer_norm(hidden_state + attended, w["g1"], w["s1"])
    first_low = first_out.astype(jnp.bfloat16)
    inner_pre = product(first_low, w["inner"]) + w["inner_bias"]
    inner_act, inner_slope = gelu_tanh(inner_pre)
    inner_low = inner_act.astype(jnp.bfloat16)
    outer_out = product(inner_low, w["outer"]) + w["outer_bias"]
    result, second_normed, second_inverse = layer_norm(first_out + outer_out, w["g2"], w["s2"])
    kept = dict(
        rows_low=rows_low,
        qkv=qkv,
        log_total=log_total,
        context_low=context_low,
        first_normed=first_normed,
        first_inverse=first_inverse,
        first_low=first_low,
        inner_slope=inner_slope,
        inner_low=inner_low,
        second_normed=second_normed,
        second_inverse=second_inverse,
    )
    return result, kept


def layer_backward(w, kept, upstream):
    second_gain_grad = jnp.sum(upstream * kept["second_normed"], axis=0)
    second_shift_grad = jnp.sum(upstream, axis=0)
    second_grad = norm_backward(upstream, kept["second_normed"], kept["second_inverse"], w["g2"])
    outer_low = second_grad.astype(jnp.bfloat16)
    active_grad = product_nt(outer_low, w["outer"])
    inner_grad = (active_grad * kept["inner_slope"]).astype(jnp.bfloat16)
    first_grad = second_grad + product_nt(inner_grad, w["inner"])
    first_gain_grad = jnp.sum(first_grad * kept["first_normed"], axis=0)
    first_shift_grad = jnp.sum(first_grad, axis=0)
    attended_grad = norm_backward(first_grad, kept["first_normed"], kept["first_inverse"], w["g1"])
    attended_low = attended_grad.astype(jnp.bfloat16)
    context_grad = product_nt(attended_low, w["out"]).astype(jnp.bfloat16)
    qkv_grad = attention_backward(kept["qkv"], kept["log_total"], context_grad)
    below_grad = attended_grad + product_nt(qkv_grad, w["qkv"])
    saved = dict(
        outer_low=outer_low,
        inner_grad=inner_grad,
        attended_low=attended_low,
        qkv_grad=qkv_grad,
    )
    norms = (second_gain_grad, second_shift_grad, first_gain_grad, first_shift_grad)
    return below_grad, saved, norms


def scatter_grads(kept, saved, norms, shards):
    def across(source, name):
        return [item[name] for item in source]

    width = kept[0]["context_low"].shape[1]
    three = kept[0]["qkv"].shape[1]
    wide = kept[0]["inner_low"].shape[1]
    blocks = (three + width + 2 * wide) // width
    packed, qkv_b = weight_grad(
        across(kept, "rows_low"), across(saved, "qkv_grad"), columns=blocks * width + PAIR
    )
    at = three // width
    packed, out_b = weight_grad(
        across(kept, "context_low"), across(saved, "attended_low"), into=packed, at=at
    )
    at += 1
    packed, inner_b = weight_grad(
        across(kept, "first_low"), across(saved, "inner_grad"), into=packed, at=at
    )
    at += wide // width
    packed, outer_b = weight_grad(
        across(kept, "inner_low"), across(saved, "outer_low"), into=packed, at=at, stack=True
    )
    rows = width
    q_b, _, v_b = split_qkv(qkv_b[0])
    s2g, s2s, s1g, s1s = [sum(parts) for parts in zip(*norms)]
    columns = jnp.stack([q_b, v_b, out_b[0], s1g, s1s, outer_b[0], s2g, s2s], axis=1)
    inner_cols = inner_b[0].reshape(wide // rows, rows).T
    columns = jnp.concatenate([columns, inner_cols], axis=1)
    columns = jnp.pad(columns, ((0, 0), (0, PAIR - columns.shape[1]))).astype(jnp.bfloat16)
    packed = lax.dynamic_update_slice(packed, columns, (0, blocks * width))
    mine = lax.psum_scatter(packed, AXES, scatter_dimension=0, tiled=True).astype(jnp.float32)
    at = 0
    pieces = []
    for count in (three, width, wide, wide, PAIR):
        pieces.append(mine[:, at : at + count])
        at += count
    qkv_mine, out_mine, inner_mine, outer_mine, col_mine = pieces
    q_w, k_w, v_w = split_qkv(qkv_mine)
    c = [col_mine[:, i] for i in range(8)]
    ib_mine = col_mine[:, 8:12].reshape(-1)
    return (
        q_w,
        c[0],
        k_w,
        v_w,
        c[1],
        out_mine,
        c[2],
        c[3],
        c[4],
        from_hidden_order(inner_mine),
        ib_mine,
        outer_mine.reshape(-1, width),
        c[5],
        c[6],
        c[7],
    )


def per_device(shards, inputs, cotangent, masked, *weights):
    w = gather_weights(weights)
    hidden_state = inputs.astype(jnp.float32)
    kept = []
    for applied in range(LAYERS):
        hidden_state, kept_values = layer_forward(w, hidden_state)
        kept.append(kept_values)
    outputs = hidden_state.astype(jnp.bfloat16)
    upstream = cotangent.astype(jnp.float32) * masked.reshape(-1, 1).astype(jnp.float32)
    saved = [None] * LAYERS
    norms = [None] * LAYERS
    for applied in range(LAYERS - 1, -1, -1):
        upstream, saved[applied], norms[applied] = layer_backward(w, kept[applied], upstream)
    collected = scatter_grads(kept, saved, norms, shards)
    return (outputs, upstream.astype(jnp.bfloat16)) + tuple(collected)


def solution(mesh):
    rows = P(AXES, None)
    vec = P(AXES)
    in_specs = (rows, rows, rows, rows, vec, rows, rows, vec, rows, vec, vec, vec, rows, vec, rows, vec, vec, vec)
    out_specs = (rows, rows, rows, vec, rows, rows, vec, rows, vec, vec, vec, rows, vec, rows, vec, vec, vec)
    shards = mesh.shape["dp"] * mesh.shape["fsdp"]
    return jax.shard_map(
        functools.partial(per_device, shards),
        mesh=mesh,
        in_specs=in_specs,
        out_specs=out_specs,
        check_vma=False,
    )
```

```python
import functools

import jax
import jax.numpy as jnp
import numpy as np
from jax import lax
from jax.experimental import pallas as pl
from jax.experimental.pallas import tpu as pltpu
from jax.sharding import PartitionSpec as P

SEQ = 512
HEAD = 64
PAIR = 128
LAYERS = 3
AXES = ("dp", "fsdp")
NT = (((1,), (1,)), ((), ()))
TN = (((0,), (0,)), ((), ()))
norm_epsilon = 1e-05


def product(left, right):
    return jnp.dot(left, right, preferred_element_type=jnp.float32)


def product_nt(left, right):
    return lax.dot_general(left, right, NT, preferred_element_type=jnp.float32)


def gelu_tanh(values):
    root = np.sqrt(2 / np.pi).astype(np.float32)
    cube = values * values * values
    bent = jnp.tanh(root * (values + 0.044715 * cube))
    cdf = 0.5 * (1.0 + bent)
    slope = cdf + values * (0.5 * (1.0 - bent * bent) * root * (1.0 + 3 * 0.044715 * values * values))
    return values * cdf, slope


def layer_norm(summed, gain, shift):
    centre = summed - jnp.mean(summed, axis=-1, keepdims=True)
    inverse = lax.rsqrt(jnp.mean(centre * centre, axis=-1, keepdims=True) + norm_epsilon)
    normed = centre * inverse
    return (normed * gain + shift, normed, inverse)


def norm_backward(upstream, normed, inverse, gain):
    scaled = upstream * gain
    return inverse * (
        scaled
        - jnp.mean(scaled, axis=-1, keepdims=True)
        - normed * jnp.mean(scaled * normed, axis=-1, keepdims=True)
    )


def _head_masks(shape):
    lane = lax.broadcasted_iota(jnp.int32, shape, 1)
    first = lane < HEAD
    return first, jnp.logical_not(first)


def attention_forward_kernel(qkv_ref, ctx_ref, lt_ref):
    scale = HEAD ** (-0.5)
    q = qkv_ref[:, 0:PAIR]
    k = qkv_ref[:, PAIR : 2 * PAIR]
    v = qkv_ref[:, 2 * PAIR : 3 * PAIR]
    masks = _head_masks(q.shape)
    zero = jnp.zeros_like(q)
    context = None
    total = None
    for mask in masks:
        scores = product_nt(jnp.where(mask, q, zero), k) * scale
        top = jnp.max(scores, axis=-1, keepdims=True)
        weights = jnp.exp(scores - top)
        sums = jnp.sum(weights, axis=-1, keepdims=True)
        probs = (weights / sums).astype(jnp.bfloat16)
        part = jnp.dot(probs, v, preferred_element_type=jnp.float32)
        log_total = jnp.broadcast_to(top + jnp.log(sums), part.shape)
        context = part if context is None else jnp.where(mask, part, context)
        total = log_total if total is None else jnp.where(mask, log_total, total)
    ctx_ref[...] = context.astype(ctx_ref.dtype)
    lt_ref[...] = total


def attention_backward_kernel(qkv_ref, lt_ref, g_ref, out_ref):
    scale = HEAD ** (-0.5)
    q = qkv_ref[:, 0:PAIR]
    k = qkv_ref[:, PAIR : 2 * PAIR]
    v = qkv_ref[:, 2 * PAIR : 3 * PAIR]
    g = g_ref[...]
    lt_t = lt_ref[...].T
    masks = _head_masks(q.shape)
    zero = jnp.zeros_like(q)
    dq = dk = dv = None
    for h, mask in enumerate(masks):
        lt_row = lt_t[h * HEAD : h * HEAD + 1, :]
        scores_t = product_nt(jnp.where(mask, k, zero), q) * scale
        probs_t = jnp.exp(scores_t - lt_row)
        prob_grad_t = product_nt(jnp.where(mask, v, zero), g)
        value_part = jnp.dot(probs_t.astype(jnp.bfloat16), g, preferred_element_type=jnp.float32)
        row_sums = jnp.sum(probs_t * prob_grad_t, axis=0, keepdims=True)
        score_grad_t = (probs_t * (prob_grad_t - row_sums)).astype(jnp.bfloat16)
        key_part = jnp.dot(score_grad_t, q, preferred_element_type=jnp.float32) * scale
        query_part = lax.dot_general(score_grad_t, k, TN, preferred_element_type=jnp.float32) * scale
        if dq is None:
            dq, dk, dv = query_part, key_part, value_part
        else:
            dq = jnp.where(mask, query_part, dq)
            dk = jnp.where(mask, key_part, dk)
            dv = jnp.where(mask, value_part, dv)
    out_ref[:, 0:PAIR] = dq.astype(out_ref.dtype)
    out_ref[:, PAIR : 2 * PAIR] = dk.astype(out_ref.dtype)
    out_ref[:, 2 * PAIR : 3 * PAIR] = dv.astype(out_ref.dtype)


def attention_forward(qkv):
    tokens, width = qkv.shape
    grid = (tokens // SEQ, width // (3 * PAIR))
    steps = grid[0] * grid[1]
    pair = pl.BlockSpec((SEQ, PAIR), lambda s, h: (s, h))
    return pl.pallas_call(
        attention_forward_kernel,
        grid=grid,
        in_specs=[pl.BlockSpec((SEQ, 3 * PAIR), lambda s, h: (s, h))],
        out_specs=[pair, pair],
        out_shape=[
            jax.ShapeDtypeStruct((tokens, width // 3), jnp.bfloat16),
            jax.ShapeDtypeStruct((tokens, width // 3), jnp.float32),
        ],
        compiler_params=pltpu.CompilerParams(dimension_semantics=("parallel", "parallel")),
        cost_estimate=pl.CostEstimate(
            flops=steps * 8 * SEQ * SEQ * PAIR,
            transcendentals=steps * 2 * SEQ * SEQ,
            bytes_accessed=tokens * width * 4,
        ),
        name="attention_forward",
    )(qkv)


def attention_backward(qkv, log_total, context_grad):
    tokens, width = qkv.shape
    grid = (tokens // SEQ, width // (3 * PAIR))
    steps = grid[0] * grid[1]
    pair = pl.BlockSpec((SEQ, PAIR), lambda s, h: (s, h))
    triple = pl.BlockSpec((SEQ, 3 * PAIR), lambda s, h: (s, h))
    return pl.pallas_call(
        attention_backward_kernel,
        grid=grid,
        in_specs=[triple, pair, pair],
        out_specs=triple,
        out_shape=jax.ShapeDtypeStruct((tokens, width), jnp.bfloat16),
        compiler_params=pltpu.CompilerParams(dimension_semantics=("parallel", "parallel")),
        cost_estimate=pl.CostEstimate(
            flops=steps * 20 * SEQ * SEQ * PAIR,
            transcendentals=steps * 2 * SEQ * SEQ,
            bytes_accessed=tokens * width * 6,
        ),
        name="attention_backward",
    )(qkv, log_total, context_grad)


def weight_grad_kernel(*refs):
    count = (len(refs) - 2) // 2
    xs, gs = refs[:count], refs[count : 2 * count]
    out_ref, sum_ref = refs[-2], refs[-1]
    acc = None
    sums = None
    for x_ref, g_ref in zip(xs, gs):
        g = g_ref[...]
        part = lax.dot_general(x_ref[...], g, TN, preferred_element_type=jnp.float32)
        col = jnp.sum(g.astype(jnp.float32), axis=0, keepdims=True)
        acc = part if acc is None else acc + part
        sums = col if sums is None else sums + col
    out_ref[...] = acc.astype(out_ref.dtype)
    sum_ref[...] = sums


def weight_grad(xs, gs, into=None, at=0, stack=False, columns=None, block=768):
    tokens, depth = xs[0].shape
    width = gs[0].shape[1]
    bk = min(block, depth)
    bn = min(block, width)
    grid = (depth // bk, width // bn)
    count = len(xs)
    if stack:
        place = lambda i, j: (0, at + i * grid[1] + j)
        shape = (bk, depth // bk * width)
    else:
        place = lambda i, j: (i, at + j)
        shape = (depth, width)
    if into is not None:
        target = into.shape
    elif columns is not None:
        target = (shape[0], columns)
    else:
        target = shape
    in_specs = [pl.BlockSpec((tokens, bk), lambda i, j: (0, i))] * count + [
        pl.BlockSpec((tokens, bn), lambda i, j: (0, j))
    ] * count
    args = list(xs) + list(gs)
    aliases = {}
    kernel = weight_grad_kernel
    if into is not None:
        in_specs.append(pl.BlockSpec(memory_space=pl.ANY))
        args.append(into)
        aliases = {len(args) - 1: 0}
        kernel = lambda *refs: weight_grad_kernel(*refs[: 2 * count], *refs[2 * count + 1 :])
    return pl.pallas_call(
        kernel,
        grid=grid,
        in_specs=in_specs,
        out_specs=[
            pl.BlockSpec((bk, bn), place),
            pl.BlockSpec((1, bn), lambda i, j: (0, j)),
        ],
        out_shape=[
            jax.ShapeDtypeStruct(target, jnp.bfloat16),
            jax.ShapeDtypeStruct((1, width), jnp.float32),
        ],
        input_output_aliases=aliases,
        compiler_params=pltpu.CompilerParams(
            dimension_semantics=("arbitrary", "arbitrary"), vmem_limit_bytes=48 * 1024 * 1024
        ),
        cost_estimate=pl.CostEstimate(
            flops=2 * count * tokens * depth * width,
            transcendentals=0,
            bytes_accessed=2 * count * tokens * (depth + width) + 2 * depth * width,
        ),
        name="weight_grad",
    )(*args)


def interleave_qkv(q, k, v):
    lead = q.shape[:-1]
    pairs = q.shape[-1] // PAIR
    stacked = jnp.stack([q, k, v], axis=-2).reshape(lead + (3, pairs, PAIR))
    return jnp.swapaxes(stacked, -3, -2).reshape(lead + (3 * pairs * PAIR,))


def split_qkv(packed):
    lead = packed.shape[:-1]
    pairs = packed.shape[-1] // (3 * PAIR)
    grouped = packed.reshape(lead + (pairs, 3, PAIR))
    return [grouped[..., which, :].reshape(lead + (pairs * PAIR,)) for which in range(3)]


def as_columns(vectors, count):
    rows = jnp.stack(vectors, axis=0)
    rows = jnp.pad(rows, ((0, count - rows.shape[0]), (0, 0)))
    return rows.T


def to_hidden_order(values, groups=4):
    lead, n = values.shape[:-1], values.shape[-1]
    return jnp.swapaxes(values.reshape(lead + (n // groups, groups)), -1, -2).reshape(lead + (n,))


def from_hidden_order(values, groups=4):
    lead, n = values.shape[:-1], values.shape[-1]
    return jnp.swapaxes(values.reshape(lead + (groups, n // groups)), -1, -2).reshape(lead + (n,))


def pack_weights(weights):
    (qw, qb, kw, vw, vb, ow, ob, g1, s1, iw, ib, uw, ub, g2, s2) = weights
    rows, width = qw.shape
    wide = iw.shape[1]
    inner_rows = ib.reshape(rows, -1).T
    columns = as_columns([qb, vb, ob, g1, s1, ub, g2, s2] + list(inner_rows), PAIR)
    return jnp.concatenate(
        [interleave_qkv(qw, kw, vw), ow, to_hidden_order(iw), uw.reshape(rows, wide), columns],
        axis=1,
    )


def gather_weights(weights):
    rows, width = weights[0].shape
    wide = weights[9].shape[1]
    packed = lax.all_gather(pack_weights(weights), AXES, axis=0, tiled=True)
    full = packed.shape[0]
    shards = full // rows
    three = 3 * width
    at = 0
    pieces = []
    for count in (three, width, wide, wide, PAIR):
        pieces.append(packed[:, at : at + count])
        at += count
    qkv, out, inner, outer_rows, cols = pieces
    groups = wide // width
    outer = jnp.concatenate(
        [outer_rows[:, c * width : (c + 1) * width] for c in range(groups)], axis=0
    )
    outer = lax.optimization_barrier(outer)
    cols = cols.astype(jnp.float32)
    (qb, vb, ob, g1, s1, ub, g2, s2) = [cols[:, i] for i in range(8)]
    ib = cols[:, 8 : 8 + groups].reshape(shards, rows, groups)
    return dict(
        qkv=qkv,
        qkv_bias=interleave_qkv(qb, jnp.zeros_like(qb), vb),
        out=out,
        out_bias=ob,
        g1=g1,
        s1=s1,
        inner=inner,
        inner_bias=ib.transpose(2, 0, 1).reshape(-1),
        outer=outer,
        outer_bias=ub,
        g2=g2,
        s2=s2,
    )


def layer_forward(w, hidden_state):
    rows_low = hidden_state.astype(jnp.bfloat16)
    qkv = (product(rows_low, w["qkv"]) + w["qkv_bias"]).astype(jnp.bfloat16)
    context_low, log_total = attention_forward(qkv)
    attended = product(context_low, w["out"]) + w["out_bias"]
    first_out, first_normed, first_inverse = layer_norm(hidden_state + attended, w["g1"], w["s1"])
    first_low = first_out.astype(jnp.bfloat16)
    inner_pre = product(first_low, w["inner"]) + w["inner_bias"]
    inner_act, inner_slope = gelu_tanh(inner_pre)
    inner_low = inner_act.astype(jnp.bfloat16)
    outer_out = product(inner_low, w["outer"]) + w["outer_bias"]
    result, second_normed, second_inverse = layer_norm(first_out + outer_out, w["g2"], w["s2"])
    kept = dict(
        rows_low=rows_low,
        qkv=qkv,
        log_total=log_total,
        context_low=context_low,
        first_normed=first_normed,
        first_inverse=first_inverse,
        first_low=first_low,
        inner_slope=inner_slope,
        inner_low=inner_low,
        second_normed=second_normed,
        second_inverse=second_inverse,
    )
    return result, kept


def layer_backward(w, kept, upstream):
    second_gain_grad = jnp.sum(upstream * kept["second_normed"], axis=0)
    second_shift_grad = jnp.sum(upstream, axis=0)
    second_grad = norm_backward(upstream, kept["second_normed"], kept["second_inverse"], w["g2"])
    outer_low = second_grad.astype(jnp.bfloat16)
    active_grad = product_nt(outer_low, w["outer"])
    inner_grad = (active_grad * kept["inner_slope"]).astype(jnp.bfloat16)
    first_grad = second_grad + product_nt(inner_grad, w["inner"])
    first_gain_grad = jnp.sum(first_grad * kept["first_normed"], axis=0)
    first_shift_grad = jnp.sum(first_grad, axis=0)
    attended_grad = norm_backward(first_grad, kept["first_normed"], kept["first_inverse"], w["g1"])
    attended_low = attended_grad.astype(jnp.bfloat16)
    context_grad = product_nt(attended_low, w["out"]).astype(jnp.bfloat16)
    qkv_grad = attention_backward(kept["qkv"], kept["log_total"], context_grad)
    below_grad = attended_grad + product_nt(qkv_grad, w["qkv"])
    saved = dict(
        outer_low=outer_low,
        inner_grad=inner_grad,
        attended_low=attended_low,
        qkv_grad=qkv_grad,
    )
    norms = (second_gain_grad, second_shift_grad, first_gain_grad, first_shift_grad)
    return below_grad, saved, norms


def scatter_grads(kept, saved, norms, shards):
    def across(source, name):
        return [item[name] for item in source]

    width = kept[0]["context_low"].shape[1]
    three = kept[0]["qkv"].shape[1]
    wide = kept[0]["inner_low"].shape[1]
    blocks = (three + width + 2 * wide) // width
    packed, qkv_b = weight_grad(
        across(kept, "rows_low"), across(saved, "qkv_grad"), columns=blocks * width + PAIR
    )
    at = three // width
    packed, out_b = weight_grad(
        across(kept, "context_low"), across(saved, "attended_low"), into=packed, at=at
    )
    at += 1
    packed, inner_b = weight_grad(
        across(kept, "first_low"), across(saved, "inner_grad"), into=packed, at=at
    )
    at += wide // width
    packed, outer_b = weight_grad(
        across(kept, "inner_low"), across(saved, "outer_low"), into=packed, at=at, stack=True
    )
    rows = width
    q_b, _, v_b = split_qkv(qkv_b[0])
    s2g, s2s, s1g, s1s = [sum(parts) for parts in zip(*norms)]
    inner_rows = list(inner_b[0].reshape(wide // rows, rows))
    columns = as_columns(
        [q_b, v_b, out_b[0], s1g, s1s, outer_b[0], s2g, s2s] + inner_rows, PAIR
    ).astype(jnp.bfloat16)
    packed = lax.dynamic_update_slice(packed, columns, (0, blocks * width))
    mine = lax.psum_scatter(packed, AXES, scatter_dimension=0, tiled=True).astype(jnp.float32)
    at = 0
    pieces = []
    for count in (three, width, wide, wide, PAIR):
        pieces.append(mine[:, at : at + count])
        at += count
    qkv_mine, out_mine, inner_mine, outer_mine, col_mine = pieces
    q_w, k_w, v_w = split_qkv(qkv_mine)
    c = [col_mine[:, i] for i in range(8)]
    ib_mine = col_mine[:, 8:12].reshape(-1)
    return (
        q_w,
        c[0],
        k_w,
        v_w,
        c[1],
        out_mine,
        c[2],
        c[3],
        c[4],
        from_hidden_order(inner_mine),
        ib_mine,
        outer_mine.reshape(-1, width),
        c[5],
        c[6],
        c[7],
    )


def per_device(shards, inputs, cotangent, masked, *weights):
    w = gather_weights(weights)
    hidden_state = inputs.astype(jnp.float32)
    kept = []
    for applied in range(LAYERS):
        hidden_state, kept_values = layer_forward(w, hidden_state)
        kept.append(kept_values)
    outputs = hidden_state.astype(jnp.bfloat16)
    upstream = cotangent.astype(jnp.float32) * masked.reshape(-1, 1).astype(jnp.float32)
    saved = [None] * LAYERS
    norms = [None] * LAYERS
    for applied in range(LAYERS - 1, -1, -1):
        upstream, saved[applied], norms[applied] = layer_backward(w, kept[applied], upstream)
    collected = scatter_grads(kept, saved, norms, shards)
    return (outputs, upstream.astype(jnp.bfloat16)) + tuple(collected)


def solution(mesh):
    rows = P(AXES, None)
    vec = P(AXES)
    in_specs = (rows, rows, rows, rows, vec, rows, rows, vec, rows, vec, vec, vec, rows, vec, rows, vec, vec, vec)
    out_specs = (rows, rows, rows, vec, rows, rows, vec, rows, vec, vec, vec, rows, vec, rows, vec, vec, vec)
    shards = mesh.shape["dp"] * mesh.shape["fsdp"]
    return jax.shard_map(
        functools.partial(per_device, shards),
        mesh=mesh,
        in_specs=in_specs,
        out_specs=out_specs,
        check_vma=False,
    )
```

```python
import functools

import jax
import jax.numpy as jnp
import numpy as np
from jax import lax
from jax.experimental import pallas as pl
from jax.experimental.pallas import tpu as pltpu
from jax.sharding import PartitionSpec as P

SEQ = 512
HEAD = 64
PAIR = 128
LAYERS = 3
AXES = ("dp", "fsdp")
NT = (((1,), (1,)), ((), ()))
TN = (((0,), (0,)), ((), ()))
norm_epsilon = 1e-05


def product(left, right):
    return jnp.dot(left, right, preferred_element_type=jnp.float32)


def product_nt(left, right):
    return lax.dot_general(left, right, NT, preferred_element_type=jnp.float32)


def gelu_tanh(values):
    root = np.sqrt(2 / np.pi).astype(np.float32)
    cube = values * values * values
    bent = jnp.tanh(root * (values + 0.044715 * cube))
    cdf = 0.5 * (1.0 + bent)
    slope = cdf + values * (0.5 * (1.0 - bent * bent) * root * (1.0 + 3 * 0.044715 * values * values))
    return values * cdf, slope


def layer_norm(summed, gain, shift):
    centre = summed - jnp.mean(summed, axis=-1, keepdims=True)
    inverse = lax.rsqrt(jnp.mean(centre * centre, axis=-1, keepdims=True) + norm_epsilon)
    normed = centre * inverse
    return (normed * gain + shift, normed, inverse)


def norm_backward(upstream, normed, inverse, gain):
    scaled = upstream * gain
    return inverse * (
        scaled
        - jnp.mean(scaled, axis=-1, keepdims=True)
        - normed * jnp.mean(scaled * normed, axis=-1, keepdims=True)
    )


def _head_masks(shape):
    lane = lax.broadcasted_iota(jnp.int32, shape, 1)
    first = lane < HEAD
    return first, jnp.logical_not(first)


def attention_forward_kernel(qkv_ref, ctx_ref, lt_ref):
    scale = HEAD ** (-0.5)
    q = qkv_ref[:, 0:PAIR]
    k = qkv_ref[:, PAIR : 2 * PAIR]
    v = qkv_ref[:, 2 * PAIR : 3 * PAIR]
    masks = _head_masks(q.shape)
    zero = jnp.zeros_like(q)
    context = None
    total = None
    for mask in masks:
        scores = product_nt(jnp.where(mask, q, zero), k) * scale
        top = jnp.max(scores, axis=-1, keepdims=True)
        weights = jnp.exp(scores - top)
        sums = jnp.sum(weights, axis=-1, keepdims=True)
        probs = (weights / sums).astype(jnp.bfloat16)
        part = jnp.dot(probs, v, preferred_element_type=jnp.float32)
        log_total = jnp.broadcast_to(top + jnp.log(sums), part.shape)
        context = part if context is None else jnp.where(mask, part, context)
        total = log_total if total is None else jnp.where(mask, log_total, total)
    ctx_ref[...] = context.astype(ctx_ref.dtype)
    lt_ref[...] = total


def attention_backward_kernel(qkv_ref, lt_ref, g_ref, out_ref):
    scale = HEAD ** (-0.5)
    q = qkv_ref[:, 0:PAIR]
    k = qkv_ref[:, PAIR : 2 * PAIR]
    v = qkv_ref[:, 2 * PAIR : 3 * PAIR]
    g = g_ref[...]
    lt_t = lt_ref[...].T
    masks = _head_masks(q.shape)
    zero = jnp.zeros_like(q)
    dq = dk = dv = None
    for h, mask in enumerate(masks):
        lt_row = lt_t[h * HEAD : h * HEAD + 1, :]
        scores_t = product_nt(jnp.where(mask, k, zero), q) * scale
        probs_t = jnp.exp(scores_t - lt_row)
        prob_grad_t = product_nt(jnp.where(mask, v, zero), g)
        value_part = jnp.dot(probs_t.astype(jnp.bfloat16), g, preferred_element_type=jnp.float32)
        row_sums = jnp.sum(probs_t * prob_grad_t, axis=0, keepdims=True)
        score_grad_t = (probs_t * (prob_grad_t - row_sums)).astype(jnp.bfloat16)
        key_part = jnp.dot(score_grad_t, q, preferred_element_type=jnp.float32) * scale
        query_part = lax.dot_general(score_grad_t, k, TN, preferred_element_type=jnp.float32) * scale
        if dq is None:
            dq, dk, dv = query_part, key_part, value_part
        else:
            dq = jnp.where(mask, query_part, dq)
            dk = jnp.where(mask, key_part, dk)
            dv = jnp.where(mask, value_part, dv)
    out_ref[:, 0:PAIR] = dq.astype(out_ref.dtype)
    out_ref[:, PAIR : 2 * PAIR] = dk.astype(out_ref.dtype)
    out_ref[:, 2 * PAIR : 3 * PAIR] = dv.astype(out_ref.dtype)


def attention_forward(qkv):
    tokens, width = qkv.shape
    grid = (tokens // SEQ, width // (3 * PAIR))
    steps = grid[0] * grid[1]
    pair = pl.BlockSpec((SEQ, PAIR), lambda s, h: (s, h))
    return pl.pallas_call(
        attention_forward_kernel,
        grid=grid,
        in_specs=[pl.BlockSpec((SEQ, 3 * PAIR), lambda s, h: (s, h))],
        out_specs=[pair, pair],
        out_shape=[
            jax.ShapeDtypeStruct((tokens, width // 3), jnp.bfloat16),
            jax.ShapeDtypeStruct((tokens, width // 3), jnp.float32),
        ],
        compiler_params=pltpu.CompilerParams(dimension_semantics=("parallel", "parallel")),
        cost_estimate=pl.CostEstimate(
            flops=steps * 8 * SEQ * SEQ * PAIR,
            transcendentals=steps * 2 * SEQ * SEQ,
            bytes_accessed=tokens * width * 4,
        ),
        name="attention_forward",
    )(qkv)


def attention_backward(qkv, log_total, context_grad):
    tokens, width = qkv.shape
    grid = (tokens // SEQ, width // (3 * PAIR))
    steps = grid[0] * grid[1]
    pair = pl.BlockSpec((SEQ, PAIR), lambda s, h: (s, h))
    triple = pl.BlockSpec((SEQ, 3 * PAIR), lambda s, h: (s, h))
    return pl.pallas_call(
        attention_backward_kernel,
        grid=grid,
        in_specs=[triple, pair, pair],
        out_specs=triple,
        out_shape=jax.ShapeDtypeStruct((tokens, width), jnp.bfloat16),
        compiler_params=pltpu.CompilerParams(dimension_semantics=("parallel", "parallel")),
        cost_estimate=pl.CostEstimate(
            flops=steps * 20 * SEQ * SEQ * PAIR,
            transcendentals=steps * 2 * SEQ * SEQ,
            bytes_accessed=tokens * width * 6,
        ),
        name="attention_backward",
    )(qkv, log_total, context_grad)


def weight_grad_kernel(*refs):
    count = (len(refs) - 2) // 2
    xs, gs = refs[:count], refs[count : 2 * count]
    out_ref, sum_ref = refs[-2], refs[-1]
    acc = None
    sums = None
    for x_ref, g_ref in zip(xs, gs):
        g = g_ref[...]
        part = lax.dot_general(x_ref[...], g, TN, preferred_element_type=jnp.float32)
        col = jnp.sum(g.astype(jnp.float32), axis=0, keepdims=True)
        acc = part if acc is None else acc + part
        sums = col if sums is None else sums + col
    out_ref[...] = acc.astype(out_ref.dtype)
    sum_ref[...] = sums


def weight_grad(xs, gs, into=None, at=0, stack=False, columns=None, block=768):
    tokens, depth = xs[0].shape
    width = gs[0].shape[1]
    bk = min(block, depth)
    bn = min(block, width)
    grid = (depth // bk, width // bn)
    count = len(xs)
    if stack:
        place = lambda i, j: (0, at + i * grid[1] + j)
        shape = (bk, depth // bk * width)
    else:
        place = lambda i, j: (i, at + j)
        shape = (depth, width)
    if into is not None:
        target = into.shape
    elif columns is not None:
        target = (shape[0], columns)
    else:
        target = shape
    in_specs = [pl.BlockSpec((tokens, bk), lambda i, j: (0, i))] * count + [
        pl.BlockSpec((tokens, bn), lambda i, j: (0, j))
    ] * count
    args = list(xs) + list(gs)
    aliases = {}
    kernel = weight_grad_kernel
    if into is not None:
        in_specs.append(pl.BlockSpec(memory_space=pl.ANY))
        args.append(into)
        aliases = {len(args) - 1: 0}
        kernel = lambda *refs: weight_grad_kernel(*refs[: 2 * count], *refs[2 * count + 1 :])
    return pl.pallas_call(
        kernel,
        grid=grid,
        in_specs=in_specs,
        out_specs=[
            pl.BlockSpec((bk, bn), place),
            pl.BlockSpec((1, bn), lambda i, j: (0, j)),
        ],
        out_shape=[
            jax.ShapeDtypeStruct(target, jnp.bfloat16),
            jax.ShapeDtypeStruct((1, width), jnp.float32),
        ],
        input_output_aliases=aliases,
        compiler_params=pltpu.CompilerParams(
            dimension_semantics=("arbitrary", "arbitrary"), vmem_limit_bytes=48 * 1024 * 1024
        ),
        cost_estimate=pl.CostEstimate(
            flops=2 * count * tokens * depth * width,
            transcendentals=0,
            bytes_accessed=2 * count * tokens * (depth + width) + 2 * depth * width,
        ),
        name="weight_grad",
    )(*args)


def interleave_qkv(q, k, v):
    lead = q.shape[:-1]
    pairs = q.shape[-1] // PAIR
    stacked = jnp.stack([q, k, v], axis=-2).reshape(lead + (3, pairs, PAIR))
    return jnp.swapaxes(stacked, -3, -2).reshape(lead + (3 * pairs * PAIR,))


def split_qkv(packed):
    pairs = packed.shape[-1] // (3 * PAIR)
    parts = [[], [], []]
    for h in range(pairs):
        for which in range(3):
            start = (3 * h + which) * PAIR
            parts[which].append(packed[..., start : start + PAIR])
    return [jnp.concatenate(p, axis=-1) for p in parts]


def split_qkv_rows(packed):
    pairs = packed.shape[-1] // (3 * PAIR)
    grouped = packed.reshape(pairs, 3, PAIR)
    return [grouped[:, which, :].reshape(-1) for which in range(3)]


def as_columns(vectors, count):
    rows = jnp.stack(vectors, axis=0)
    rows = jnp.pad(rows, ((0, count - rows.shape[0]), (0, 0)))
    return rows.T


def to_hidden_order(values, groups=4):
    lead, n = values.shape[:-1], values.shape[-1]
    return jnp.swapaxes(values.reshape(lead + (n // groups, groups)), -1, -2).reshape(lead + (n,))


def from_hidden_order(values, groups=4):
    lead, n = values.shape[:-1], values.shape[-1]
    return jnp.swapaxes(values.reshape(lead + (groups, n // groups)), -1, -2).reshape(lead + (n,))


def pack_weights(weights):
    (qw, qb, kw, vw, vb, ow, ob, g1, s1, iw, ib, uw, ub, g2, s2) = weights
    rows, width = qw.shape
    wide = iw.shape[1]
    columns = jnp.stack([qb, vb, ob, g1, s1, ub, g2, s2], axis=1)
    columns = jnp.concatenate([columns, ib.reshape(rows, -1)], axis=1)
    columns = jnp.pad(columns, ((0, 0), (0, PAIR - columns.shape[1])))
    return jnp.concatenate(
        [interleave_qkv(qw, kw, vw), ow, to_hidden_order(iw), uw.reshape(rows, wide), columns],
        axis=1,
    )


def gather_weights(weights):
    rows, width = weights[0].shape
    wide = weights[9].shape[1]
    packed = lax.all_gather(pack_weights(weights), AXES, axis=0, tiled=True)
    full = packed.shape[0]
    shards = full // rows
    three = 3 * width
    at = 0
    pieces = []
    for count in (three, width, wide, wide, PAIR):
        pieces.append(packed[:, at : at + count])
        at += count
    qkv, out, inner, outer_rows, cols = pieces
    groups = wide // width
    outer = jnp.concatenate(
        [outer_rows[:, c * width : (c + 1) * width] for c in range(groups)], axis=0
    )
    outer = lax.optimization_barrier(outer)
    cols = cols.astype(jnp.float32)
    (qb, vb, ob, g1, s1, ub, g2, s2) = [cols[:, i] for i in range(8)]
    ib = cols[:, 8 : 8 + groups].reshape(shards, rows, groups)
    return dict(
        qkv=qkv,
        qkv_bias=interleave_qkv(qb, jnp.zeros_like(qb), vb),
        out=out,
        out_bias=ob,
        g1=g1,
        s1=s1,
        inner=inner,
        inner_bias=ib.transpose(2, 0, 1).reshape(-1),
        outer=outer,
        outer_bias=ub,
        g2=g2,
        s2=s2,
    )


def layer_forward(w, hidden_state):
    rows_low = hidden_state.astype(jnp.bfloat16)
    qkv = (product(rows_low, w["qkv"]) + w["qkv_bias"]).astype(jnp.bfloat16)
    context_low, log_total = attention_forward(qkv)
    attended = product(context_low, w["out"]) + w["out_bias"]
    first_out, first_normed, first_inverse = layer_norm(hidden_state + attended, w["g1"], w["s1"])
    first_low = first_out.astype(jnp.bfloat16)
    inner_pre = product(first_low, w["inner"]) + w["inner_bias"]
    inner_act, inner_slope = gelu_tanh(inner_pre)
    inner_low = inner_act.astype(jnp.bfloat16)
    outer_out = product(inner_low, w["outer"]) + w["outer_bias"]
    result, second_normed, second_inverse = layer_norm(first_out + outer_out, w["g2"], w["s2"])
    kept = dict(
        rows_low=rows_low,
        qkv=qkv,
        log_total=log_total,
        context_low=context_low,
        first_normed=first_normed,
        first_inverse=first_inverse,
        first_low=first_low,
        inner_slope=inner_slope,
        inner_low=inner_low,
        second_normed=second_normed,
        second_inverse=second_inverse,
    )
    return result, kept


def layer_backward(w, kept, upstream):
    second_gain_grad = jnp.sum(upstream * kept["second_normed"], axis=0)
    second_shift_grad = jnp.sum(upstream, axis=0)
    second_grad = norm_backward(upstream, kept["second_normed"], kept["second_inverse"], w["g2"])
    outer_low = second_grad.astype(jnp.bfloat16)
    active_grad = product_nt(outer_low, w["outer"])
    inner_grad = (active_grad * kept["inner_slope"]).astype(jnp.bfloat16)
    first_grad = second_grad + product_nt(inner_grad, w["inner"])
    first_gain_grad = jnp.sum(first_grad * kept["first_normed"], axis=0)
    first_shift_grad = jnp.sum(first_grad, axis=0)
    attended_grad = norm_backward(first_grad, kept["first_normed"], kept["first_inverse"], w["g1"])
    attended_low = attended_grad.astype(jnp.bfloat16)
    context_grad = product_nt(attended_low, w["out"]).astype(jnp.bfloat16)
    qkv_grad = attention_backward(kept["qkv"], kept["log_total"], context_grad)
    below_grad = attended_grad + product_nt(qkv_grad, w["qkv"])
    saved = dict(
        outer_low=outer_low,
        inner_grad=inner_grad,
        attended_low=attended_low,
        qkv_grad=qkv_grad,
    )
    norms = (second_gain_grad, second_shift_grad, first_gain_grad, first_shift_grad)
    return below_grad, saved, norms


def scatter_grads(kept, saved, norms, shards):
    def across(source, name):
        return [item[name] for item in source]

    width = kept[0]["context_low"].shape[1]
    three = kept[0]["qkv"].shape[1]
    wide = kept[0]["inner_low"].shape[1]
    blocks = (three + width + 2 * wide) // width
    packed, qkv_b = weight_grad(
        across(kept, "rows_low"), across(saved, "qkv_grad"), columns=blocks * width + PAIR
    )
    at = three // width
    packed, out_b = weight_grad(
        across(kept, "context_low"), across(saved, "attended_low"), into=packed, at=at
    )
    at += 1
    packed, inner_b = weight_grad(
        across(kept, "first_low"), across(saved, "inner_grad"), into=packed, at=at
    )
    at += wide // width
    packed, outer_b = weight_grad(
        across(kept, "inner_low"), across(saved, "outer_low"), into=packed, at=at, stack=True
    )
    rows = width
    q_b, _, v_b = split_qkv_rows(qkv_b[0])
    s2g, s2s, s1g, s1s = [sum(parts) for parts in zip(*norms)]
    inner_rows = list(inner_b[0].reshape(wide // rows, rows))
    columns = as_columns(
        [q_b, v_b, out_b[0], s1g, s1s, outer_b[0], s2g, s2s] + inner_rows, PAIR
    ).astype(jnp.bfloat16)
    packed = lax.dynamic_update_slice(packed, columns, (0, blocks * width))
    mine = lax.psum_scatter(packed, AXES, scatter_dimension=0, tiled=True).astype(jnp.float32)
    at = 0
    pieces = []
    for count in (three, width, wide, wide, PAIR):
        pieces.append(mine[:, at : at + count])
        at += count
    qkv_mine, out_mine, inner_mine, outer_mine, col_mine = pieces
    q_w, k_w, v_w = split_qkv(qkv_mine)
    c = [col_mine[:, i] for i in range(8)]
    ib_mine = col_mine[:, 8:12].reshape(-1)
    return (
        q_w,
        c[0],
        k_w,
        v_w,
        c[1],
        out_mine,
        c[2],
        c[3],
        c[4],
        from_hidden_order(inner_mine),
        ib_mine,
        outer_mine.reshape(-1, width),
        c[5],
        c[6],
        c[7],
    )


def per_device(shards, inputs, cotangent, masked, *weights):
    w = gather_weights(weights)
    hidden_state = inputs.astype(jnp.float32)
    kept = []
    for applied in range(LAYERS):
        hidden_state, kept_values = layer_forward(w, hidden_state)
        kept.append(kept_values)
    outputs = hidden_state.astype(jnp.bfloat16)
    upstream = cotangent.astype(jnp.float32) * masked.reshape(-1, 1).astype(jnp.float32)
    saved = [None] * LAYERS
    norms = [None] * LAYERS
    for applied in range(LAYERS - 1, -1, -1):
        upstream, saved[applied], norms[applied] = layer_backward(w, kept[applied], upstream)
    collected = scatter_grads(kept, saved, norms, shards)
    return (outputs, upstream.astype(jnp.bfloat16)) + tuple(collected)


def solution(mesh):
    rows = P(AXES, None)
    vec = P(AXES)
    in_specs = (rows, rows, rows, rows, vec, rows, rows, vec, rows, vec, vec, vec, rows, vec, rows, vec, vec, vec)
    out_specs = (rows, rows, rows, vec, rows, rows, vec, rows, vec, vec, vec, rows, vec, rows, vec, vec, vec)
    shards = mesh.shape["dp"] * mesh.shape["fsdp"]
    return jax.shard_map(
        functools.partial(per_device, shards),
        mesh=mesh,
        in_specs=in_specs,
        out_specs=out_specs,
        check_vma=False,
    )
```

```python
import functools

import jax
import jax.numpy as jnp
import numpy as np
from jax import lax
from jax.experimental import pallas as pl
from jax.experimental.pallas import tpu as pltpu
from jax.sharding import PartitionSpec as P

SEQ = 512
HEAD = 64
PAIR = 128
GROUP = 2
LAYERS = 3
AXES = ("dp", "fsdp")
NT = (((1,), (1,)), ((), ()))
TN = (((0,), (0,)), ((), ()))
norm_epsilon = 1e-05


def product(left, right):
    return jnp.dot(left, right, preferred_element_type=jnp.float32)


def product_nt(left, right):
    return lax.dot_general(left, right, NT, preferred_element_type=jnp.float32)


def gelu_tanh(values):
    root = np.sqrt(2 / np.pi).astype(np.float32)
    cube = values * values * values
    bent = jnp.tanh(root * (values + 0.044715 * cube))
    cdf = 0.5 * (1.0 + bent)
    slope = cdf + values * (0.5 * (1.0 - bent * bent) * root * (1.0 + 3 * 0.044715 * values * values))
    return values * cdf, slope


def layer_norm(summed, gain, shift):
    centre = summed - jnp.mean(summed, axis=-1, keepdims=True)
    inverse = lax.rsqrt(jnp.mean(centre * centre, axis=-1, keepdims=True) + norm_epsilon)
    normed = centre * inverse
    return (normed * gain + shift, normed, inverse)


def norm_backward(upstream, normed, inverse, gain):
    scaled = upstream * gain
    return inverse * (
        scaled
        - jnp.mean(scaled, axis=-1, keepdims=True)
        - normed * jnp.mean(scaled * normed, axis=-1, keepdims=True)
    )


def _head_masks(shape):
    lane = lax.broadcasted_iota(jnp.int32, shape, 1)
    first = lane < HEAD
    return first, jnp.logical_not(first)


def attention_forward_kernel(qkv_ref, ctx_ref, lt_ref):
    for p in range(ctx_ref.shape[1] // PAIR):
        attention_forward_pair(qkv_ref, ctx_ref, lt_ref, 3 * PAIR * p, PAIR * p)


def attention_forward_pair(qkv_ref, ctx_ref, lt_ref, at, out_at):
    scale = HEAD ** (-0.5)
    q = qkv_ref[:, at : at + PAIR]
    k = qkv_ref[:, at + PAIR : at + 2 * PAIR]
    v = qkv_ref[:, at + 2 * PAIR : at + 3 * PAIR]
    masks = _head_masks(q.shape)
    zero = jnp.zeros_like(q)
    context = None
    total = None
    for mask in masks:
        scores = product_nt(jnp.where(mask, q, zero), k) * scale
        top = jnp.max(scores, axis=-1, keepdims=True)
        weights = jnp.exp(scores - top)
        sums = jnp.sum(weights, axis=-1, keepdims=True)
        probs = (weights / sums).astype(jnp.bfloat16)
        part = jnp.dot(probs, v, preferred_element_type=jnp.float32)
        log_total = jnp.broadcast_to(top + jnp.log(sums), part.shape)
        context = part if context is None else jnp.where(mask, part, context)
        total = log_total if total is None else jnp.where(mask, log_total, total)
    ctx_ref[:, out_at : out_at + PAIR] = context.astype(ctx_ref.dtype)
    lt_ref[:, out_at : out_at + PAIR] = total


def attention_backward_kernel(qkv_ref, lt_ref, g_ref, out_ref):
    for p in range(g_ref.shape[1] // PAIR):
        attention_backward_pair(qkv_ref, lt_ref, g_ref, out_ref, 3 * PAIR * p, PAIR * p)


def attention_backward_pair(qkv_ref, lt_ref, g_ref, out_ref, at, in_at):
    scale = HEAD ** (-0.5)
    q = qkv_ref[:, at : at + PAIR]
    k = qkv_ref[:, at + PAIR : at + 2 * PAIR]
    v = qkv_ref[:, at + 2 * PAIR : at + 3 * PAIR]
    g = g_ref[:, in_at : in_at + PAIR]
    lt_t = lt_ref[:, in_at : in_at + PAIR].T
    masks = _head_masks(q.shape)
    zero = jnp.zeros_like(q)
    dq = dk = dv = None
    for h, mask in enumerate(masks):
        lt_row = lt_t[h * HEAD : h * HEAD + 1, :]
        scores_t = product_nt(jnp.where(mask, k, zero), q) * scale
        probs_t = jnp.exp(scores_t - lt_row)
        prob_grad_t = product_nt(jnp.where(mask, v, zero), g)
        value_part = jnp.dot(probs_t.astype(jnp.bfloat16), g, preferred_element_type=jnp.float32)
        row_sums = jnp.sum(probs_t * prob_grad_t, axis=0, keepdims=True)
        score_grad_t = (probs_t * (prob_grad_t - row_sums)).astype(jnp.bfloat16)
        key_part = jnp.dot(score_grad_t, q, preferred_element_type=jnp.float32) * scale
        query_part = lax.dot_general(score_grad_t, k, TN, preferred_element_type=jnp.float32) * scale
        if dq is None:
            dq, dk, dv = query_part, key_part, value_part
        else:
            dq = jnp.where(mask, query_part, dq)
            dk = jnp.where(mask, key_part, dk)
            dv = jnp.where(mask, value_part, dv)
    out_ref[:, at : at + PAIR] = dq.astype(out_ref.dtype)
    out_ref[:, at + PAIR : at + 2 * PAIR] = dk.astype(out_ref.dtype)
    out_ref[:, at + 2 * PAIR : at + 3 * PAIR] = dv.astype(out_ref.dtype)


def attention_forward(qkv):
    tokens, width = qkv.shape
    group = GROUP if (width // (3 * PAIR)) % GROUP == 0 else 1
    grid = (tokens // SEQ, width // (3 * PAIR * group))
    steps = grid[0] * grid[1] * group
    pair = pl.BlockSpec((SEQ, PAIR * group), lambda s, h: (s, h))
    return pl.pallas_call(
        attention_forward_kernel,
        grid=grid,
        in_specs=[pl.BlockSpec((SEQ, 3 * PAIR * group), lambda s, h: (s, h))],
        out_specs=[pair, pair],
        out_shape=[
            jax.ShapeDtypeStruct((tokens, width // 3), jnp.bfloat16),
            jax.ShapeDtypeStruct((tokens, width // 3), jnp.float32),
        ],
        compiler_params=pltpu.CompilerParams(dimension_semantics=("parallel", "parallel")),
        cost_estimate=pl.CostEstimate(
            flops=steps * 8 * SEQ * SEQ * PAIR,
            transcendentals=steps * 2 * SEQ * SEQ,
            bytes_accessed=tokens * width * 4,
        ),
        name="attention_forward",
    )(qkv)


def attention_backward(qkv, log_total, context_grad):
    tokens, width = qkv.shape
    group = GROUP if (width // (3 * PAIR)) % GROUP == 0 else 1
    grid = (tokens // SEQ, width // (3 * PAIR * group))
    steps = grid[0] * grid[1] * group
    pair = pl.BlockSpec((SEQ, PAIR * group), lambda s, h: (s, h))
    triple = pl.BlockSpec((SEQ, 3 * PAIR * group), lambda s, h: (s, h))
    return pl.pallas_call(
        attention_backward_kernel,
        grid=grid,
        in_specs=[triple, pair, pair],
        out_specs=triple,
        out_shape=jax.ShapeDtypeStruct((tokens, width), jnp.bfloat16),
        compiler_params=pltpu.CompilerParams(dimension_semantics=("parallel", "parallel")),
        cost_estimate=pl.CostEstimate(
            flops=steps * 20 * SEQ * SEQ * PAIR,
            transcendentals=steps * 2 * SEQ * SEQ,
            bytes_accessed=tokens * width * 6,
        ),
        name="attention_backward",
    )(qkv, log_total, context_grad)


def weight_grad_kernel(*refs):
    count = (len(refs) - 2) // 2
    xs, gs = refs[:count], refs[count : 2 * count]
    out_ref, sum_ref = refs[-2], refs[-1]
    acc = None
    sums = None
    for x_ref, g_ref in zip(xs, gs):
        g = g_ref[...]
        part = lax.dot_general(x_ref[...], g, TN, preferred_element_type=jnp.float32)
        col = jnp.sum(g.astype(jnp.float32), axis=0, keepdims=True)
        acc = part if acc is None else acc + part
        sums = col if sums is None else sums + col
    out_ref[...] = acc.astype(out_ref.dtype)
    sum_ref[...] = sums


def weight_grad(xs, gs, into=None, at=0, stack=False, columns=None, block=768):
    tokens, depth = xs[0].shape
    width = gs[0].shape[1]
    bk = min(block, depth)
    bn = min(block, width)
    grid = (depth // bk, width // bn)
    count = len(xs)
    if stack:
        place = lambda i, j: (0, at + i * grid[1] + j)
        shape = (bk, depth // bk * width)
    else:
        place = lambda i, j: (i, at + j)
        shape = (depth, width)
    if into is not None:
        target = into.shape
    elif columns is not None:
        target = (shape[0], columns)
    else:
        target = shape
    in_specs = [pl.BlockSpec((tokens, bk), lambda i, j: (0, i))] * count + [
        pl.BlockSpec((tokens, bn), lambda i, j: (0, j))
    ] * count
    args = list(xs) + list(gs)
    aliases = {}
    kernel = weight_grad_kernel
    if into is not None:
        in_specs.append(pl.BlockSpec(memory_space=pl.ANY))
        args.append(into)
        aliases = {len(args) - 1: 0}
        kernel = lambda *refs: weight_grad_kernel(*refs[: 2 * count], *refs[2 * count + 1 :])
    return pl.pallas_call(
        kernel,
        grid=grid,
        in_specs=in_specs,
        out_specs=[
            pl.BlockSpec((bk, bn), place),
            pl.BlockSpec((1, bn), lambda i, j: (0, j)),
        ],
        out_shape=[
            jax.ShapeDtypeStruct(target, jnp.bfloat16),
            jax.ShapeDtypeStruct((1, width), jnp.float32),
        ],
        input_output_aliases=aliases,
        compiler_params=pltpu.CompilerParams(
            dimension_semantics=("arbitrary", "arbitrary"), vmem_limit_bytes=48 * 1024 * 1024
        ),
        cost_estimate=pl.CostEstimate(
            flops=2 * count * tokens * depth * width,
            transcendentals=0,
            bytes_accessed=2 * count * tokens * (depth + width) + 2 * depth * width,
        ),
        name="weight_grad",
    )(*args)


def interleave_qkv(q, k, v):
    lead = q.shape[:-1]
    pairs = q.shape[-1] // PAIR
    stacked = jnp.stack([q, k, v], axis=-2).reshape(lead + (3, pairs, PAIR))
    return jnp.swapaxes(stacked, -3, -2).reshape(lead + (3 * pairs * PAIR,))


def split_qkv(packed):
    pairs = packed.shape[-1] // (3 * PAIR)
    parts = [[], [], []]
    for h in range(pairs):
        for which in range(3):
            start = (3 * h + which) * PAIR
            parts[which].append(packed[..., start : start + PAIR])
    return [jnp.concatenate(p, axis=-1) for p in parts]


def to_hidden_order(values, groups=4):
    lead, n = values.shape[:-1], values.shape[-1]
    return jnp.swapaxes(values.reshape(lead + (n // groups, groups)), -1, -2).reshape(lead + (n,))


def from_hidden_order(values, groups=4):
    lead, n = values.shape[:-1], values.shape[-1]
    return jnp.swapaxes(values.reshape(lead + (groups, n // groups)), -1, -2).reshape(lead + (n,))


def pack_weights(weights):
    (qw, qb, kw, vw, vb, ow, ob, g1, s1, iw, ib, uw, ub, g2, s2) = weights
    rows, width = qw.shape
    wide = iw.shape[1]
    columns = jnp.stack([qb, vb, ob, g1, s1, ub, g2, s2], axis=1)
    columns = jnp.concatenate([columns, ib.reshape(rows, -1)], axis=1)
    columns = jnp.pad(columns, ((0, 0), (0, PAIR - columns.shape[1])))
    return jnp.concatenate(
        [interleave_qkv(qw, kw, vw), ow, to_hidden_order(iw), uw.reshape(rows, wide), columns],
        axis=1,
    )


def gather_weights(weights):
    rows, width = weights[0].shape
    wide = weights[9].shape[1]
    packed = lax.all_gather(pack_weights(weights), AXES, axis=0, tiled=True)
    full = packed.shape[0]
    shards = full // rows
    three = 3 * width
    at = 0
    pieces = []
    for count in (three, width, wide, wide, PAIR):
        pieces.append(packed[:, at : at + count])
        at += count
    qkv, out, inner, outer_rows, cols = pieces
    groups = wide // width
    outer = jnp.concatenate(
        [outer_rows[:, c * width : (c + 1) * width] for c in range(groups)], axis=0
    )
    outer = lax.optimization_barrier(outer)
    cols = cols.astype(jnp.float32)
    (qb, vb, ob, g1, s1, ub, g2, s2) = [cols[:, i] for i in range(8)]
    ib = cols[:, 8 : 8 + groups].reshape(shards, rows, groups)
    return dict(
        qkv=qkv,
        qkv_bias=interleave_qkv(qb, jnp.zeros_like(qb), vb),
        out=out,
        out_bias=ob,
        g1=g1,
        s1=s1,
        inner=inner,
        inner_bias=ib.transpose(2, 0, 1).reshape(-1),
        outer=outer,
        outer_bias=ub,
        g2=g2,
        s2=s2,
    )


def layer_forward(w, hidden_state):
    rows_low = hidden_state.astype(jnp.bfloat16)
    qkv = (product(rows_low, w["qkv"]) + w["qkv_bias"]).astype(jnp.bfloat16)
    context_low, log_total = attention_forward(qkv)
    attended = product(context_low, w["out"]) + w["out_bias"]
    first_out, first_normed, first_inverse = layer_norm(hidden_state + attended, w["g1"], w["s1"])
    first_low = first_out.astype(jnp.bfloat16)
    inner_pre = product(first_low, w["inner"]) + w["inner_bias"]
    inner_act, inner_slope = gelu_tanh(inner_pre)
    inner_low = inner_act.astype(jnp.bfloat16)
    outer_out = product(inner_low, w["outer"]) + w["outer_bias"]
    result, second_normed, second_inverse = layer_norm(first_out + outer_out, w["g2"], w["s2"])
    kept = dict(
        rows_low=rows_low,
        qkv=qkv,
        log_total=log_total,
        context_low=context_low,
        first_normed=first_normed,
        first_inverse=first_inverse,
        first_low=first_low,
        inner_slope=inner_slope,
        inner_low=inner_low,
        second_normed=second_normed,
        second_inverse=second_inverse,
    )
    return result, kept


def layer_backward(w, kept, upstream):
    second_gain_grad = jnp.sum(upstream * kept["second_normed"], axis=0)
    second_shift_grad = jnp.sum(upstream, axis=0)
    second_grad = norm_backward(upstream, kept["second_normed"], kept["second_inverse"], w["g2"])
    outer_low = second_grad.astype(jnp.bfloat16)
    active_grad = product_nt(outer_low, w["outer"])
    inner_grad = (active_grad * kept["inner_slope"]).astype(jnp.bfloat16)
    first_grad = second_grad + product_nt(inner_grad, w["inner"])
    first_gain_grad = jnp.sum(first_grad * kept["first_normed"], axis=0)
    first_shift_grad = jnp.sum(first_grad, axis=0)
    attended_grad = norm_backward(first_grad, kept["first_normed"], kept["first_inverse"], w["g1"])
    attended_low = attended_grad.astype(jnp.bfloat16)
    context_grad = product_nt(attended_low, w["out"]).astype(jnp.bfloat16)
    qkv_grad = attention_backward(kept["qkv"], kept["log_total"], context_grad)
    below_grad = attended_grad + product_nt(qkv_grad, w["qkv"])
    saved = dict(
        outer_low=outer_low,
        inner_grad=inner_grad,
        attended_low=attended_low,
        qkv_grad=qkv_grad,
    )
    norms = (second_gain_grad, second_shift_grad, first_gain_grad, first_shift_grad)
    return below_grad, saved, norms


def scatter_grads(kept, saved, norms, shards):
    def across(source, name):
        return [item[name] for item in source]

    width = kept[0]["context_low"].shape[1]
    three = kept[0]["qkv"].shape[1]
    wide = kept[0]["inner_low"].shape[1]
    blocks = (three + width + 2 * wide) // width
    packed, qkv_b = weight_grad(
        across(kept, "rows_low"), across(saved, "qkv_grad"), columns=blocks * width + PAIR
    )
    at = three // width
    packed, out_b = weight_grad(
        across(kept, "context_low"), across(saved, "attended_low"), into=packed, at=at
    )
    at += 1
    packed, inner_b = weight_grad(
        across(kept, "first_low"), across(saved, "inner_grad"), into=packed, at=at
    )
    at += wide // width
    packed, outer_b = weight_grad(
        across(kept, "inner_low"), across(saved, "outer_low"), into=packed, at=at, stack=True
    )
    rows = width
    q_b, _, v_b = split_qkv(qkv_b[0])
    s2g, s2s, s1g, s1s = [sum(parts) for parts in zip(*norms)]
    columns = jnp.stack([q_b, v_b, out_b[0], s1g, s1s, outer_b[0], s2g, s2s], axis=1)
    inner_cols = inner_b[0].reshape(wide // rows, rows).T
    columns = jnp.concatenate([columns, inner_cols], axis=1)
    columns = jnp.pad(columns, ((0, 0), (0, PAIR - columns.shape[1]))).astype(jnp.bfloat16)
    packed = lax.dynamic_update_slice(packed, columns, (0, blocks * width))
    mine = lax.psum_scatter(packed, AXES, scatter_dimension=0, tiled=True).astype(jnp.float32)
    at = 0
    pieces = []
    for count in (three, width, wide, wide, PAIR):
        pieces.append(mine[:, at : at + count])
        at += count
    qkv_mine, out_mine, inner_mine, outer_mine, col_mine = pieces
    q_w, k_w, v_w = split_qkv(qkv_mine)
    c = [col_mine[:, i] for i in range(8)]
    ib_mine = col_mine[:, 8:12].reshape(-1)
    return (
        q_w,
        c[0],
        k_w,
        v_w,
        c[1],
        out_mine,
        c[2],
        c[3],
        c[4],
        from_hidden_order(inner_mine),
        ib_mine,
        outer_mine.reshape(-1, width),
        c[5],
        c[6],
        c[7],
    )


def per_device(shards, inputs, cotangent, masked, *weights):
    w = gather_weights(weights)
    hidden_state = inputs.astype(jnp.float32)
    kept = []
    for applied in range(LAYERS):
        hidden_state, kept_values = layer_forward(w, hidden_state)
        kept.append(kept_values)
    outputs = hidden_state.astype(jnp.bfloat16)
    upstream = cotangent.astype(jnp.float32) * masked.reshape(-1, 1).astype(jnp.float32)
    saved = [None] * LAYERS
    norms = [None] * LAYERS
    for applied in range(LAYERS - 1, -1, -1):
        upstream, saved[applied], norms[applied] = layer_backward(w, kept[applied], upstream)
    collected = scatter_grads(kept, saved, norms, shards)
    return (outputs, upstream.astype(jnp.bfloat16)) + tuple(collected)


def solution(mesh):
    rows = P(AXES, None)
    vec = P(AXES)
    in_specs = (rows, rows, rows, rows, vec, rows, rows, vec, rows, vec, vec, vec, rows, vec, rows, vec, vec, vec)
    out_specs = (rows, rows, rows, vec, rows, rows, vec, rows, vec, vec, vec, rows, vec, rows, vec, vec, vec)
    shards = mesh.shape["dp"] * mesh.shape["fsdp"]
    return jax.shard_map(
        functools.partial(per_device, shards),
        mesh=mesh,
        in_specs=in_specs,
        out_specs=out_specs,
        check_vma=False,
    )
```

```python
import functools

import jax
import jax.numpy as jnp
import numpy as np
from jax import lax
from jax.experimental import pallas as pl
from jax.experimental.pallas import tpu as pltpu
from jax.sharding import PartitionSpec as P

SEQ = 512
HEAD = 64
PAIR = 128
GROUP = 2
LAYERS = 3
AXES = ("dp", "fsdp")
NT = (((1,), (1,)), ((), ()))
TN = (((0,), (0,)), ((), ()))
norm_epsilon = 1e-05


def product(left, right):
    return jnp.dot(left, right, preferred_element_type=jnp.float32)


def product_nt(left, right):
    return lax.dot_general(left, right, NT, preferred_element_type=jnp.float32)


def gelu_tanh(values):
    root = np.sqrt(2 / np.pi).astype(np.float32)
    cube = values * values * values
    bent = jnp.tanh(root * (values + 0.044715 * cube))
    cdf = 0.5 * (1.0 + bent)
    slope = cdf + values * (0.5 * (1.0 - bent * bent) * root * (1.0 + 3 * 0.044715 * values * values))
    return values * cdf, slope


def layer_norm(summed, gain, shift):
    centre = summed - jnp.mean(summed, axis=-1, keepdims=True)
    inverse = lax.rsqrt(jnp.mean(centre * centre, axis=-1, keepdims=True) + norm_epsilon)
    normed = centre * inverse
    return (normed * gain + shift, normed, inverse)


def norm_backward(upstream, normed, inverse, gain):
    scaled = upstream * gain
    return inverse * (
        scaled
        - jnp.mean(scaled, axis=-1, keepdims=True)
        - normed * jnp.mean(scaled * normed, axis=-1, keepdims=True)
    )


def _head_masks(shape):
    lane = lax.broadcasted_iota(jnp.int32, shape, 1)
    first = lane < HEAD
    return first, jnp.logical_not(first)


def attention_forward_kernel(qkv_ref, ctx_ref, lt_ref):
    for p in range(ctx_ref.shape[1] // PAIR):
        attention_forward_pair(qkv_ref, ctx_ref, lt_ref, 3 * PAIR * p, PAIR * p)


def attention_forward_pair(qkv_ref, ctx_ref, lt_ref, at, out_at):
    scale = HEAD ** (-0.5)
    q = qkv_ref[:, at : at + PAIR]
    k = qkv_ref[:, at + PAIR : at + 2 * PAIR]
    v = qkv_ref[:, at + 2 * PAIR : at + 3 * PAIR]
    masks = _head_masks(q.shape)
    zero = jnp.zeros_like(q)
    context = None
    total = None
    for mask in masks:
        scores = product_nt(jnp.where(mask, q, zero), k) * scale
        top = jnp.max(scores, axis=-1, keepdims=True)
        weights = jnp.exp(scores - top)
        sums = jnp.sum(weights, axis=-1, keepdims=True)
        probs = (weights / sums).astype(jnp.bfloat16)
        part = jnp.dot(probs, v, preferred_element_type=jnp.float32)
        log_total = jnp.broadcast_to(top + jnp.log(sums), part.shape)
        context = part if context is None else jnp.where(mask, part, context)
        total = log_total if total is None else jnp.where(mask, log_total, total)
    ctx_ref[:, out_at : out_at + PAIR] = context.astype(ctx_ref.dtype)
    lt_ref[:, out_at : out_at + PAIR] = total


def attention_backward_kernel(qkv_ref, lt_ref, g_ref, out_ref):
    for p in range(g_ref.shape[1] // PAIR):
        attention_backward_pair(qkv_ref, lt_ref, g_ref, out_ref, 3 * PAIR * p, PAIR * p)


def attention_backward_pair(qkv_ref, lt_ref, g_ref, out_ref, at, in_at):
    scale = HEAD ** (-0.5)
    q = qkv_ref[:, at : at + PAIR]
    k = qkv_ref[:, at + PAIR : at + 2 * PAIR]
    v = qkv_ref[:, at + 2 * PAIR : at + 3 * PAIR]
    g = g_ref[:, in_at : in_at + PAIR]
    lt_t = lt_ref[:, in_at : in_at + PAIR].T
    masks = _head_masks(q.shape)
    zero = jnp.zeros_like(q)
    dq = dk = dv = None
    for h, mask in enumerate(masks):
        lt_row = lt_t[h * HEAD : h * HEAD + 1, :]
        scores_t = product_nt(jnp.where(mask, k, zero), q) * scale
        probs_t = jnp.exp(scores_t - lt_row)
        prob_grad_t = product_nt(jnp.where(mask, v, zero), g)
        value_part = jnp.dot(probs_t.astype(jnp.bfloat16), g, preferred_element_type=jnp.float32)
        row_sums = jnp.sum(probs_t * prob_grad_t, axis=0, keepdims=True)
        score_grad_t = (probs_t * (prob_grad_t - row_sums)).astype(jnp.bfloat16)
        key_part = jnp.dot(score_grad_t, q, preferred_element_type=jnp.float32) * scale
        query_part = lax.dot_general(score_grad_t, k, TN, preferred_element_type=jnp.float32) * scale
        if dq is None:
            dq, dk, dv = query_part, key_part, value_part
        else:
            dq = jnp.where(mask, query_part, dq)
            dk = jnp.where(mask, key_part, dk)
            dv = jnp.where(mask, value_part, dv)
    out_ref[:, at : at + PAIR] = dq.astype(out_ref.dtype)
    out_ref[:, at + PAIR : at + 2 * PAIR] = dk.astype(out_ref.dtype)
    out_ref[:, at + 2 * PAIR : at + 3 * PAIR] = dv.astype(out_ref.dtype)


def attention_forward(qkv):
    tokens, width = qkv.shape
    group = GROUP if (width // (3 * PAIR)) % GROUP == 0 else 1
    grid = (tokens // SEQ, width // (3 * PAIR * group))
    steps = grid[0] * grid[1] * group
    pair = pl.BlockSpec((SEQ, PAIR * group), lambda s, h: (s, h))
    return pl.pallas_call(
        attention_forward_kernel,
        grid=grid,
        in_specs=[pl.BlockSpec((SEQ, 3 * PAIR * group), lambda s, h: (s, h))],
        out_specs=[pair, pair],
        out_shape=[
            jax.ShapeDtypeStruct((tokens, width // 3), jnp.bfloat16),
            jax.ShapeDtypeStruct((tokens, width // 3), jnp.float32),
        ],
        compiler_params=pltpu.CompilerParams(dimension_semantics=("parallel", "parallel")),
        cost_estimate=pl.CostEstimate(
            flops=steps * 8 * SEQ * SEQ * PAIR,
            transcendentals=steps * 2 * SEQ * SEQ,
            bytes_accessed=tokens * width * 4,
        ),
        name="attention_forward",
    )(qkv)


def attention_backward(qkv, log_total, context_grad):
    tokens, width = qkv.shape
    group = GROUP if (width // (3 * PAIR)) % GROUP == 0 else 1
    grid = (tokens // SEQ, width // (3 * PAIR * group))
    steps = grid[0] * grid[1] * group
    pair = pl.BlockSpec((SEQ, PAIR * group), lambda s, h: (s, h))
    triple = pl.BlockSpec((SEQ, 3 * PAIR * group), lambda s, h: (s, h))
    return pl.pallas_call(
        attention_backward_kernel,
        grid=grid,
        in_specs=[triple, pair, pair],
        out_specs=triple,
        out_shape=jax.ShapeDtypeStruct((tokens, width), jnp.bfloat16),
        compiler_params=pltpu.CompilerParams(dimension_semantics=("parallel", "parallel")),
        cost_estimate=pl.CostEstimate(
            flops=steps * 20 * SEQ * SEQ * PAIR,
            transcendentals=steps * 2 * SEQ * SEQ,
            bytes_accessed=tokens * width * 6,
        ),
        name="attention_backward",
    )(qkv, log_total, context_grad)


def weight_grad_kernel(*refs):
    count = (len(refs) - 2) // 2
    xs, gs = refs[:count], refs[count : 2 * count]
    out_ref, sum_ref = refs[-2], refs[-1]
    acc = None
    sums = None
    for x_ref, g_ref in zip(xs, gs):
        g = g_ref[...]
        part = lax.dot_general(x_ref[...], g, TN, preferred_element_type=jnp.float32)
        col = jnp.sum(g.astype(jnp.float32), axis=0, keepdims=True)
        acc = part if acc is None else acc + part
        sums = col if sums is None else sums + col
    out_ref[...] = acc.astype(out_ref.dtype)
    sum_ref[...] = sums


def weight_grad(xs, gs, into=None, at=0, stack=False, columns=None, block=768):
    tokens, depth = xs[0].shape
    width = gs[0].shape[1]
    bk = min(block, depth)
    bn = min(block, width)
    grid = (depth // bk, width // bn)
    count = len(xs)
    if stack:
        place = lambda i, j: (0, at + i * grid[1] + j)
        shape = (bk, depth // bk * width)
    else:
        place = lambda i, j: (i, at + j)
        shape = (depth, width)
    if into is not None:
        target = into.shape
    elif columns is not None:
        target = (shape[0], columns)
    else:
        target = shape
    in_specs = [pl.BlockSpec((tokens, bk), lambda i, j: (0, i))] * count + [
        pl.BlockSpec((tokens, bn), lambda i, j: (0, j))
    ] * count
    args = list(xs) + list(gs)
    aliases = {}
    kernel = weight_grad_kernel
    if into is not None:
        in_specs.append(pl.BlockSpec(memory_space=pl.ANY))
        args.append(into)
        aliases = {len(args) - 1: 0}
        kernel = lambda *refs: weight_grad_kernel(*refs[: 2 * count], *refs[2 * count + 1 :])
    return pl.pallas_call(
        kernel,
        grid=grid,
        in_specs=in_specs,
        out_specs=[
            pl.BlockSpec((bk, bn), place),
            pl.BlockSpec((1, bn), lambda i, j: (0, j)),
        ],
        out_shape=[
            jax.ShapeDtypeStruct(target, jnp.bfloat16),
            jax.ShapeDtypeStruct((1, width), jnp.float32),
        ],
        input_output_aliases=aliases,
        compiler_params=pltpu.CompilerParams(
            dimension_semantics=("arbitrary", "arbitrary"), vmem_limit_bytes=48 * 1024 * 1024
        ),
        cost_estimate=pl.CostEstimate(
            flops=2 * count * tokens * depth * width,
            transcendentals=0,
            bytes_accessed=2 * count * tokens * (depth + width) + 2 * depth * width,
        ),
        name="weight_grad",
    )(*args)


def interleave_qkv(q, k, v):
    lead = q.shape[:-1]
    pairs = q.shape[-1] // PAIR
    stacked = jnp.stack([q, k, v], axis=-2).reshape(lead + (3, pairs, PAIR))
    return jnp.swapaxes(stacked, -3, -2).reshape(lead + (3 * pairs * PAIR,))


def split_qkv(packed):
    pairs = packed.shape[-1] // (3 * PAIR)
    parts = [[], [], []]
    for h in range(pairs):
        for which in range(3):
            start = (3 * h + which) * PAIR
            parts[which].append(packed[..., start : start + PAIR])
    return [jnp.concatenate(p, axis=-1) for p in parts]


def to_hidden_order(values, groups=4):
    lead, n = values.shape[:-1], values.shape[-1]
    return jnp.swapaxes(values.reshape(lead + (n // groups, groups)), -1, -2).reshape(lead + (n,))


def from_hidden_order(values, groups=4):
    lead, n = values.shape[:-1], values.shape[-1]
    return jnp.swapaxes(values.reshape(lead + (groups, n // groups)), -1, -2).reshape(lead + (n,))


def pack_weights(weights):
    (qw, qb, kw, vw, vb, ow, ob, g1, s1, iw, ib, uw, ub, g2, s2) = weights
    rows, width = qw.shape
    wide = iw.shape[1]
    columns = jnp.stack([qb, vb, ob, g1, s1, ub, g2, s2], axis=1)
    columns = jnp.concatenate([columns, ib.reshape(rows, -1)], axis=1)
    columns = jnp.pad(columns, ((0, 0), (0, PAIR - columns.shape[1])))
    return jnp.concatenate(
        [interleave_qkv(qw, kw, vw), ow, to_hidden_order(iw), uw.reshape(rows, wide), columns],
        axis=1,
    )


def gather_weights(weights):
    rows, width = weights[0].shape
    wide = weights[9].shape[1]
    packed = lax.all_gather(pack_weights(weights), AXES, axis=0, tiled=True)
    full = packed.shape[0]
    shards = full // rows
    three = 3 * width
    at = 0
    pieces = []
    for count in (three, width, wide, wide, PAIR):
        pieces.append(packed[:, at : at + count])
        at += count
    qkv, out, inner, outer_rows, cols = pieces
    groups = wide // width
    outer = jnp.concatenate(
        [outer_rows[:, c * width : (c + 1) * width] for c in range(groups)], axis=0
    )
    outer = lax.optimization_barrier(outer)
    cols = cols.astype(jnp.float32)
    (qb, vb, ob, g1, s1, ub, g2, s2) = [cols[:, i] for i in range(8)]
    ib = cols[:, 8 : 8 + groups].reshape(shards, rows, groups)
    return dict(
        qkv=qkv,
        qkv_bias=interleave_qkv(qb, jnp.zeros_like(qb), vb),
        out=out,
        out_bias=ob,
        g1=g1,
        s1=s1,
        inner=inner,
        inner_bias=ib.transpose(2, 0, 1).reshape(-1),
        outer=outer,
        outer_bias=ub,
        g2=g2,
        s2=s2,
    )


def layer_forward(w, hidden_state):
    rows_low = hidden_state.astype(jnp.bfloat16)
    qkv = (product(rows_low, w["qkv"]) + w["qkv_bias"]).astype(jnp.bfloat16)
    context_low, log_total = attention_forward(qkv)
    attended = product(context_low, w["out"]) + w["out_bias"]
    first_out, first_normed, first_inverse = layer_norm(hidden_state + attended, w["g1"], w["s1"])
    first_low = first_out.astype(jnp.bfloat16)
    inner_pre = product(first_low, w["inner"]) + w["inner_bias"]
    inner_act, inner_slope = gelu_tanh(inner_pre)
    inner_low = inner_act.astype(jnp.bfloat16)
    outer_out = product(inner_low, w["outer"]) + w["outer_bias"]
    result, second_normed, second_inverse = layer_norm(first_out + outer_out, w["g2"], w["s2"])
    kept = dict(
        rows_low=rows_low,
        qkv=qkv,
        log_total=log_total,
        context_low=context_low,
        first_normed=first_normed,
        first_inverse=first_inverse,
        first_low=first_low,
        inner_slope=inner_slope,
        inner_low=inner_low,
        second_normed=second_normed,
        second_inverse=second_inverse,
    )
    return result, kept


def layer_backward(w, kept, upstream):
    second_gain_grad = jnp.sum(upstream * kept["second_normed"], axis=0)
    second_shift_grad = jnp.sum(upstream, axis=0)
    second_grad = norm_backward(upstream, kept["second_normed"], kept["second_inverse"], w["g2"])
    outer_low = second_grad.astype(jnp.bfloat16)
    active_grad = product_nt(outer_low, w["outer"])
    inner_grad = (active_grad * kept["inner_slope"]).astype(jnp.bfloat16)
    first_grad = second_grad + product_nt(inner_grad, w["inner"])
    first_gain_grad = jnp.sum(first_grad * kept["first_normed"], axis=0)
    first_shift_grad = jnp.sum(first_grad, axis=0)
    attended_grad = norm_backward(first_grad, kept["first_normed"], kept["first_inverse"], w["g1"])
    attended_low = attended_grad.astype(jnp.bfloat16)
    context_grad = product_nt(attended_low, w["out"]).astype(jnp.bfloat16)
    qkv_grad = attention_backward(kept["qkv"], kept["log_total"], context_grad)
    below_grad = attended_grad + product_nt(qkv_grad, w["qkv"])
    saved = dict(
        outer_low=outer_low,
        inner_grad=inner_grad,
        attended_low=attended_low,
        qkv_grad=qkv_grad,
    )
    norms = (second_gain_grad, second_shift_grad, first_gain_grad, first_shift_grad)
    return below_grad, saved, norms


def scatter_grads(kept, saved, norms, shards):
    def across(source, name):
        return [item[name] for item in source]

    width = kept[0]["context_low"].shape[1]
    three = kept[0]["qkv"].shape[1]
    wide = kept[0]["inner_low"].shape[1]
    blocks = (three + width + 2 * wide) // width
    packed, qkv_b = weight_grad(
        across(kept, "rows_low"), across(saved, "qkv_grad"), columns=blocks * width + PAIR
    )
    at = three // width
    packed, out_b = weight_grad(
        across(kept, "context_low"), across(saved, "attended_low"), into=packed, at=at
    )
    at += 1
    packed, inner_b = weight_grad(
        across(kept, "first_low"), across(saved, "inner_grad"), into=packed, at=at
    )
    at += wide // width
    packed, outer_b = weight_grad(
        across(kept, "inner_low"), across(saved, "outer_low"), into=packed, at=at, stack=True
    )
    rows = width
    q_b, _, v_b = split_qkv(qkv_b[0])
    s2g, s2s, s1g, s1s = [sum(parts) for parts in zip(*norms)]
    columns = jnp.stack([q_b, v_b, out_b[0], s1g, s1s, outer_b[0], s2g, s2s], axis=1)
    inner_cols = inner_b[0].reshape(wide // rows, rows).T
    columns = jnp.concatenate([columns, inner_cols], axis=1)
    columns = jnp.pad(columns, ((0, 0), (0, PAIR - columns.shape[1]))).astype(jnp.bfloat16)
    packed = lax.dynamic_update_slice(packed, columns, (0, blocks * width))
    mine = lax.psum_scatter(packed, AXES, scatter_dimension=0, tiled=True)
    at = 0
    pieces = []
    for count in (three, width, wide, wide, PAIR):
        pieces.append(mine[:, at : at + count])
        at += count
    qkv_mine, out_mine, inner_mine, outer_mine, col_mine = pieces
    q_w, k_w, v_w = split_qkv(qkv_mine)
    c = [col_mine[:, i] for i in range(8)]
    ib_mine = col_mine[:, 8:12].reshape(-1)
    found = (
        q_w,
        c[0],
        k_w,
        v_w,
        c[1],
        out_mine,
        c[2],
        c[3],
        c[4],
        from_hidden_order(inner_mine),
        ib_mine,
        outer_mine.reshape(-1, width),
        c[5],
        c[6],
        c[7],
    )
    return tuple(piece.astype(jnp.float32) for piece in found)


def per_device(shards, inputs, cotangent, masked, *weights):
    w = gather_weights(weights)
    hidden_state = inputs.astype(jnp.float32)
    kept = []
    for applied in range(LAYERS):
        hidden_state, kept_values = layer_forward(w, hidden_state)
        kept.append(kept_values)
    outputs = hidden_state.astype(jnp.bfloat16)
    upstream = cotangent.astype(jnp.float32) * masked.reshape(-1, 1).astype(jnp.float32)
    saved = [None] * LAYERS
    norms = [None] * LAYERS
    for applied in range(LAYERS - 1, -1, -1):
        upstream, saved[applied], norms[applied] = layer_backward(w, kept[applied], upstream)
    collected = scatter_grads(kept, saved, norms, shards)
    return (outputs, upstream.astype(jnp.bfloat16)) + tuple(collected)


def solution(mesh):
    rows = P(AXES, None)
    vec = P(AXES)
    in_specs = (rows, rows, rows, rows, vec, rows, rows, vec, rows, vec, vec, vec, rows, vec, rows, vec, vec, vec)
    out_specs = (rows, rows, rows, vec, rows, rows, vec, rows, vec, vec, vec, rows, vec, rows, vec, vec, vec)
    shards = mesh.shape["dp"] * mesh.shape["fsdp"]
    return jax.shard_map(
        functools.partial(per_device, shards),
        mesh=mesh,
        in_specs=in_specs,
        out_specs=out_specs,
        check_vma=False,
    )
```

```python
import functools

import jax
import jax.numpy as jnp
import numpy as np
from jax import lax
from jax.experimental import pallas as pl
from jax.experimental.pallas import tpu as pltpu
from jax.sharding import PartitionSpec as P

SEQ = 512
HEAD = 64
PAIR = 128
GROUP = 2
LAYERS = 3
AXES = ("dp", "fsdp")
NT = (((1,), (1,)), ((), ()))
TN = (((0,), (0,)), ((), ()))
norm_epsilon = 1e-05


def product(left, right):
    return jnp.dot(left, right, preferred_element_type=jnp.float32)


def product_nt(left, right):
    return lax.dot_general(left, right, NT, preferred_element_type=jnp.float32)


def gelu_tanh(values):
    root = np.sqrt(2 / np.pi).astype(np.float32)
    cube = values * values * values
    bent = jnp.tanh(root * (values + 0.044715 * cube))
    cdf = 0.5 * (1.0 + bent)
    slope = cdf + values * (0.5 * (1.0 - bent * bent) * root * (1.0 + 3 * 0.044715 * values * values))
    return values * cdf, slope


def layer_norm(summed, gain, shift):
    centre = summed - jnp.mean(summed, axis=-1, keepdims=True)
    inverse = lax.rsqrt(jnp.mean(centre * centre, axis=-1, keepdims=True) + norm_epsilon)
    normed = centre * inverse
    return (normed * gain + shift, normed, inverse)


def norm_backward(upstream, normed, inverse, gain):
    scaled = upstream * gain
    return inverse * (
        scaled
        - jnp.mean(scaled, axis=-1, keepdims=True)
        - normed * jnp.mean(scaled * normed, axis=-1, keepdims=True)
    )


def _head_masks(shape):
    lane = lax.broadcasted_iota(jnp.int32, shape, 1)
    first = lane < HEAD
    return first, jnp.logical_not(first)


def attention_forward_kernel(qkv_ref, ctx_ref, lt_ref):
    for p in range(ctx_ref.shape[1] // PAIR):
        attention_forward_pair(qkv_ref, ctx_ref, lt_ref, 3 * PAIR * p, PAIR * p)


def attention_forward_pair(qkv_ref, ctx_ref, lt_ref, at, out_at):
    scale = HEAD ** (-0.5)
    q = qkv_ref[:, at : at + PAIR]
    k = qkv_ref[:, at + PAIR : at + 2 * PAIR]
    v = qkv_ref[:, at + 2 * PAIR : at + 3 * PAIR]
    masks = _head_masks(q.shape)
    zero = jnp.zeros_like(q)
    context = None
    total = None
    for mask in masks:
        scores = product_nt(jnp.where(mask, q, zero), k) * scale
        top = jnp.max(scores, axis=-1, keepdims=True)
        weights = jnp.exp(scores - top)
        sums = jnp.sum(weights, axis=-1, keepdims=True)
        probs = (weights / sums).astype(jnp.bfloat16)
        part = jnp.dot(probs, v, preferred_element_type=jnp.float32)
        log_total = jnp.broadcast_to(top + jnp.log(sums), part.shape)
        context = part if context is None else jnp.where(mask, part, context)
        total = log_total if total is None else jnp.where(mask, log_total, total)
    ctx_ref[:, out_at : out_at + PAIR] = context.astype(ctx_ref.dtype)
    lt_ref[:, out_at : out_at + PAIR] = total


def attention_backward_kernel(qkv_ref, lt_ref, g_ref, out_ref):
    for p in range(g_ref.shape[1] // PAIR):
        attention_backward_pair(qkv_ref, lt_ref, g_ref, out_ref, 3 * PAIR * p, PAIR * p)


def attention_backward_pair(qkv_ref, lt_ref, g_ref, out_ref, at, in_at):
    scale = HEAD ** (-0.5)
    q = qkv_ref[:, at : at + PAIR]
    k = qkv_ref[:, at + PAIR : at + 2 * PAIR]
    v = qkv_ref[:, at + 2 * PAIR : at + 3 * PAIR]
    g = g_ref[:, in_at : in_at + PAIR]
    lt_t = lt_ref[:, in_at : in_at + PAIR].T
    masks = _head_masks(q.shape)
    zero = jnp.zeros_like(q)
    dq = dk = dv = None
    for h, mask in enumerate(masks):
        lt_row = lt_t[h * HEAD : h * HEAD + 1, :]
        scores_t = product_nt(jnp.where(mask, k, zero), q) * scale
        probs_t = jnp.exp(scores_t - lt_row)
        prob_grad_t = product_nt(jnp.where(mask, v, zero), g)
        value_part = jnp.dot(probs_t.astype(jnp.bfloat16), g, preferred_element_type=jnp.float32)
        row_sums = jnp.sum(probs_t * prob_grad_t, axis=0, keepdims=True)
        score_grad_t = (probs_t * (prob_grad_t - row_sums)).astype(jnp.bfloat16)
        key_part = jnp.dot(score_grad_t, q, preferred_element_type=jnp.float32) * scale
        query_part = lax.dot_general(score_grad_t, k, TN, preferred_element_type=jnp.float32) * scale
        if dq is None:
            dq, dk, dv = query_part, key_part, value_part
        else:
            dq = jnp.where(mask, query_part, dq)
            dk = jnp.where(mask, key_part, dk)
            dv = jnp.where(mask, value_part, dv)
    out_ref[:, at : at + PAIR] = dq.astype(out_ref.dtype)
    out_ref[:, at + PAIR : at + 2 * PAIR] = dk.astype(out_ref.dtype)
    out_ref[:, at + 2 * PAIR : at + 3 * PAIR] = dv.astype(out_ref.dtype)


def attention_forward(qkv):
    tokens, width = qkv.shape
    group = GROUP if (width // (3 * PAIR)) % GROUP == 0 else 1
    grid = (tokens // SEQ, width // (3 * PAIR * group))
    steps = grid[0] * grid[1] * group
    pair = pl.BlockSpec((SEQ, PAIR * group), lambda s, h: (s, h))
    return pl.pallas_call(
        attention_forward_kernel,
        grid=grid,
        in_specs=[pl.BlockSpec((SEQ, 3 * PAIR * group), lambda s, h: (s, h))],
        out_specs=[pair, pair],
        out_shape=[
            jax.ShapeDtypeStruct((tokens, width // 3), jnp.bfloat16),
            jax.ShapeDtypeStruct((tokens, width // 3), jnp.float32),
        ],
        compiler_params=pltpu.CompilerParams(dimension_semantics=("parallel", "parallel")),
        cost_estimate=pl.CostEstimate(
            flops=steps * 8 * SEQ * SEQ * PAIR,
            transcendentals=steps * 2 * SEQ * SEQ,
            bytes_accessed=tokens * width * 4,
        ),
        name="attention_forward",
    )(qkv)


def attention_backward(qkv, log_total, context_grad):
    tokens, width = qkv.shape
    group = GROUP if (width // (3 * PAIR)) % GROUP == 0 else 1
    grid = (tokens // SEQ, width // (3 * PAIR * group))
    steps = grid[0] * grid[1] * group
    pair = pl.BlockSpec((SEQ, PAIR * group), lambda s, h: (s, h))
    triple = pl.BlockSpec((SEQ, 3 * PAIR * group), lambda s, h: (s, h))
    return pl.pallas_call(
        attention_backward_kernel,
        grid=grid,
        in_specs=[triple, pair, pair],
        out_specs=triple,
        out_shape=jax.ShapeDtypeStruct((tokens, width), jnp.bfloat16),
        compiler_params=pltpu.CompilerParams(dimension_semantics=("parallel", "parallel")),
        cost_estimate=pl.CostEstimate(
            flops=steps * 20 * SEQ * SEQ * PAIR,
            transcendentals=steps * 2 * SEQ * SEQ,
            bytes_accessed=tokens * width * 6,
        ),
        name="attention_backward",
    )(qkv, log_total, context_grad)


def weight_grad_kernel(*refs):
    count = (len(refs) - 2) // 2
    xs, gs = refs[:count], refs[count : 2 * count]
    out_ref, sum_ref = refs[-2], refs[-1]
    acc = None
    sums = None
    for x_ref, g_ref in zip(xs, gs):
        g = g_ref[...]
        part = lax.dot_general(x_ref[...], g, TN, preferred_element_type=jnp.float32)
        col = jnp.sum(g.astype(jnp.float32), axis=0, keepdims=True)
        acc = part if acc is None else acc + part
        sums = col if sums is None else sums + col
    out_ref[...] = acc.astype(out_ref.dtype)
    sum_ref[...] = sums


def weight_grad(xs, gs, into=None, at=0, stack=False, columns=None, block=768, wide_block=1536):
    tokens, depth = xs[0].shape
    width = gs[0].shape[1]
    bk = min(block, depth)
    bn = min(block, width)
    if not stack and width % wide_block == 0:
        bn = wide_block
    elif not stack and width % (block * 3 // 2) == 0 and width > block:
        bn = block * 3 // 2
    at = at * block // bn
    grid = (depth // bk, width // bn)
    count = len(xs)
    if stack:
        place = lambda i, j: (0, at + i * grid[1] + j)
        shape = (bk, depth // bk * width)
    else:
        place = lambda i, j: (i, at + j)
        shape = (depth, width)
    if into is not None:
        target = into.shape
    elif columns is not None:
        target = (shape[0], columns)
    else:
        target = shape
    in_specs = [pl.BlockSpec((tokens, bk), lambda i, j: (0, i))] * count + [
        pl.BlockSpec((tokens, bn), lambda i, j: (0, j))
    ] * count
    args = list(xs) + list(gs)
    aliases = {}
    kernel = weight_grad_kernel
    if into is not None:
        in_specs.append(pl.BlockSpec(memory_space=pl.ANY))
        args.append(into)
        aliases = {len(args) - 1: 0}
        kernel = lambda *refs: weight_grad_kernel(*refs[: 2 * count], *refs[2 * count + 1 :])
    return pl.pallas_call(
        kernel,
        grid=grid,
        in_specs=in_specs,
        out_specs=[
            pl.BlockSpec((bk, bn), place),
            pl.BlockSpec((1, bn), lambda i, j: (0, j)),
        ],
        out_shape=[
            jax.ShapeDtypeStruct(target, jnp.bfloat16),
            jax.ShapeDtypeStruct((1, width), jnp.float32),
        ],
        input_output_aliases=aliases,
        compiler_params=pltpu.CompilerParams(
            dimension_semantics=("arbitrary", "arbitrary"), vmem_limit_bytes=48 * 1024 * 1024
        ),
        cost_estimate=pl.CostEstimate(
            flops=2 * count * tokens * depth * width,
            transcendentals=0,
            bytes_accessed=2 * count * tokens * (depth + width) + 2 * depth * width,
        ),
        name="weight_grad",
    )(*args)


def interleave_qkv(q, k, v):
    lead = q.shape[:-1]
    pairs = q.shape[-1] // PAIR
    stacked = jnp.stack([q, k, v], axis=-2).reshape(lead + (3, pairs, PAIR))
    return jnp.swapaxes(stacked, -3, -2).reshape(lead + (3 * pairs * PAIR,))


def split_qkv(packed):
    pairs = packed.shape[-1] // (3 * PAIR)
    parts = [[], [], []]
    for h in range(pairs):
        for which in range(3):
            start = (3 * h + which) * PAIR
            parts[which].append(packed[..., start : start + PAIR])
    return [jnp.concatenate(p, axis=-1) for p in parts]


def to_hidden_order(values, groups=4):
    lead, n = values.shape[:-1], values.shape[-1]
    return jnp.swapaxes(values.reshape(lead + (n // groups, groups)), -1, -2).reshape(lead + (n,))


def from_hidden_order(values, groups=4):
    lead, n = values.shape[:-1], values.shape[-1]
    return jnp.swapaxes(values.reshape(lead + (groups, n // groups)), -1, -2).reshape(lead + (n,))


def pack_weights(weights):
    (qw, qb, kw, vw, vb, ow, ob, g1, s1, iw, ib, uw, ub, g2, s2) = weights
    rows, width = qw.shape
    wide = iw.shape[1]
    columns = jnp.stack([qb, vb, ob, g1, s1, ub, g2, s2], axis=1)
    columns = jnp.concatenate([columns, ib.reshape(rows, -1)], axis=1)
    columns = jnp.pad(columns, ((0, 0), (0, PAIR - columns.shape[1])))
    return jnp.concatenate(
        [interleave_qkv(qw, kw, vw), ow, to_hidden_order(iw), uw.reshape(rows, wide), columns],
        axis=1,
    )


def gather_weights(weights):
    rows, width = weights[0].shape
    wide = weights[9].shape[1]
    packed = lax.all_gather(pack_weights(weights), AXES, axis=0, tiled=True)
    full = packed.shape[0]
    shards = full // rows
    three = 3 * width
    at = 0
    pieces = []
    for count in (three, width, wide, wide, PAIR):
        pieces.append(packed[:, at : at + count])
        at += count
    qkv, out, inner, outer_rows, cols = pieces
    groups = wide // width
    outer = jnp.concatenate(
        [outer_rows[:, c * width : (c + 1) * width] for c in range(groups)], axis=0
    )
    outer = lax.optimization_barrier(outer)
    cols = cols.astype(jnp.float32)
    (qb, vb, ob, g1, s1, ub, g2, s2) = [cols[:, i] for i in range(8)]
    ib = cols[:, 8 : 8 + groups].reshape(shards, rows, groups)
    return dict(
        qkv=qkv,
        qkv_bias=interleave_qkv(qb, jnp.zeros_like(qb), vb),
        out=out,
        out_bias=ob,
        g1=g1,
        s1=s1,
        inner=inner,
        inner_bias=ib.transpose(2, 0, 1).reshape(-1),
        outer=outer,
        outer_bias=ub,
        g2=g2,
        s2=s2,
    )


def layer_forward(w, hidden_state):
    rows_low = hidden_state.astype(jnp.bfloat16)
    qkv = (product(rows_low, w["qkv"]) + w["qkv_bias"]).astype(jnp.bfloat16)
    context_low, log_total = attention_forward(qkv)
    attended = product(context_low, w["out"]) + w["out_bias"]
    first_out, first_normed, first_inverse = layer_norm(hidden_state + attended, w["g1"], w["s1"])
    first_low = first_out.astype(jnp.bfloat16)
    inner_pre = product(first_low, w["inner"]) + w["inner_bias"]
    inner_act, inner_slope = gelu_tanh(inner_pre)
    inner_low = inner_act.astype(jnp.bfloat16)
    outer_out = product(inner_low, w["outer"]) + w["outer_bias"]
    result, second_normed, second_inverse = layer_norm(first_out + outer_out, w["g2"], w["s2"])
    kept = dict(
        rows_low=rows_low,
        qkv=qkv,
        log_total=log_total,
        context_low=context_low,
        first_normed=first_normed,
        first_inverse=first_inverse,
        first_low=first_low,
        inner_slope=inner_slope,
        inner_low=inner_low,
        second_normed=second_normed,
        second_inverse=second_inverse,
    )
    return result, kept


def layer_backward(w, kept, upstream):
    second_gain_grad = jnp.sum(upstream * kept["second_normed"], axis=0)
    second_shift_grad = jnp.sum(upstream, axis=0)
    second_grad = norm_backward(upstream, kept["second_normed"], kept["second_inverse"], w["g2"])
    outer_low = second_grad.astype(jnp.bfloat16)
    active_grad = product_nt(outer_low, w["outer"])
    inner_grad = (active_grad * kept["inner_slope"]).astype(jnp.bfloat16)
    first_grad = second_grad + product_nt(inner_grad, w["inner"])
    first_gain_grad = jnp.sum(first_grad * kept["first_normed"], axis=0)
    first_shift_grad = jnp.sum(first_grad, axis=0)
    attended_grad = norm_backward(first_grad, kept["first_normed"], kept["first_inverse"], w["g1"])
    attended_low = attended_grad.astype(jnp.bfloat16)
    context_grad = product_nt(attended_low, w["out"]).astype(jnp.bfloat16)
    qkv_grad = attention_backward(kept["qkv"], kept["log_total"], context_grad)
    below_grad = attended_grad + product_nt(qkv_grad, w["qkv"])
    saved = dict(
        outer_low=outer_low,
        inner_grad=inner_grad,
        attended_low=attended_low,
        qkv_grad=qkv_grad,
    )
    norms = (second_gain_grad, second_shift_grad, first_gain_grad, first_shift_grad)
    return below_grad, saved, norms


def scatter_grads(kept, saved, norms, shards):
    def across(source, name):
        return [item[name] for item in source]

    width = kept[0]["context_low"].shape[1]
    three = kept[0]["qkv"].shape[1]
    wide = kept[0]["inner_low"].shape[1]
    blocks = (three + width + 2 * wide) // width
    packed, qkv_b = weight_grad(
        across(kept, "rows_low"), across(saved, "qkv_grad"), columns=blocks * width + PAIR
    )
    at = three // width
    packed, out_b = weight_grad(
        across(kept, "context_low"), across(saved, "attended_low"), into=packed, at=at
    )
    at += 1
    packed, inner_b = weight_grad(
        across(kept, "first_low"), across(saved, "inner_grad"), into=packed, at=at
    )
    at += wide // width
    packed, outer_b = weight_grad(
        across(kept, "inner_low"), across(saved, "outer_low"), into=packed, at=at, stack=True
    )
    rows = width
    q_b, _, v_b = split_qkv(qkv_b[0])
    s2g, s2s, s1g, s1s = [sum(parts) for parts in zip(*norms)]
    columns = jnp.stack([q_b, v_b, out_b[0], s1g, s1s, outer_b[0], s2g, s2s], axis=1)
    inner_cols = inner_b[0].reshape(wide // rows, rows).T
    columns = jnp.concatenate([columns, inner_cols], axis=1)
    columns = jnp.pad(columns, ((0, 0), (0, PAIR - columns.shape[1]))).astype(jnp.bfloat16)
    packed = lax.dynamic_update_slice(packed, columns, (0, blocks * width))
    mine = lax.psum_scatter(packed, AXES, scatter_dimension=0, tiled=True).astype(jnp.float32)
    at = 0
    pieces = []
    for count in (three, width, wide, wide, PAIR):
        pieces.append(mine[:, at : at + count])
        at += count
    qkv_mine, out_mine, inner_mine, outer_mine, col_mine = pieces
    q_w, k_w, v_w = split_qkv(qkv_mine)
    c = [col_mine[:, i] for i in range(8)]
    ib_mine = col_mine[:, 8:12].reshape(-1)
    return (
        q_w,
        c[0],
        k_w,
        v_w,
        c[1],
        out_mine,
        c[2],
        c[3],
        c[4],
        from_hidden_order(inner_mine),
        ib_mine,
        outer_mine.reshape(-1, width),
        c[5],
        c[6],
        c[7],
    )


def per_device(shards, inputs, cotangent, masked, *weights):
    w = gather_weights(weights)
    hidden_state = inputs.astype(jnp.float32)
    kept = []
    for applied in range(LAYERS):
        hidden_state, kept_values = layer_forward(w, hidden_state)
        kept.append(kept_values)
    outputs = hidden_state.astype(jnp.bfloat16)
    upstream = cotangent.astype(jnp.float32) * masked.reshape(-1, 1).astype(jnp.float32)
    saved = [None] * LAYERS
    norms = [None] * LAYERS
    for applied in range(LAYERS - 1, -1, -1):
        upstream, saved[applied], norms[applied] = layer_backward(w, kept[applied], upstream)
    collected = scatter_grads(kept, saved, norms, shards)
    return (outputs, upstream.astype(jnp.bfloat16)) + tuple(collected)


def solution(mesh):
    rows = P(AXES, None)
    vec = P(AXES)
    in_specs = (rows, rows, rows, rows, vec, rows, rows, vec, rows, vec, vec, vec, rows, vec, rows, vec, vec, vec)
    out_specs = (rows, rows, rows, vec, rows, rows, vec, rows, vec, vec, vec, rows, vec, rows, vec, vec, vec)
    shards = mesh.shape["dp"] * mesh.shape["fsdp"]
    return jax.shard_map(
        functools.partial(per_device, shards),
        mesh=mesh,
        in_specs=in_specs,
        out_specs=out_specs,
        check_vma=False,
    )
```

```python
import functools

import jax
import jax.numpy as jnp
import numpy as np
from jax import lax
from jax.experimental import pallas as pl
from jax.experimental.pallas import tpu as pltpu
from jax.sharding import PartitionSpec as P

SEQ = 512
HEAD = 64
PAIR = 128
GROUP = 2
LAYERS = 3
AXES = ("dp", "fsdp")
NT = (((1,), (1,)), ((), ()))
TN = (((0,), (0,)), ((), ()))
norm_epsilon = 1e-05


def product(left, right):
    return jnp.dot(left, right, preferred_element_type=jnp.float32)


def product_nt(left, right):
    return lax.dot_general(left, right, NT, preferred_element_type=jnp.float32)


def gelu_tanh(values):
    root = np.sqrt(2 / np.pi).astype(np.float32)
    cube = values * values * values
    bent = jnp.tanh(root * (values + 0.044715 * cube))
    cdf = 0.5 * (1.0 + bent)
    slope = cdf + values * (0.5 * (1.0 - bent * bent) * root * (1.0 + 3 * 0.044715 * values * values))
    return values * cdf, slope


def layer_norm(summed, gain, shift):
    centre = summed - jnp.mean(summed, axis=-1, keepdims=True)
    inverse = lax.rsqrt(jnp.mean(centre * centre, axis=-1, keepdims=True) + norm_epsilon)
    normed = centre * inverse
    return (normed * gain + shift, normed, inverse)


def norm_backward(upstream, normed, inverse, gain):
    scaled = upstream * gain
    return inverse * (
        scaled
        - jnp.mean(scaled, axis=-1, keepdims=True)
        - normed * jnp.mean(scaled * normed, axis=-1, keepdims=True)
    )


def _head_masks(shape):
    lane = lax.broadcasted_iota(jnp.int32, shape, 1)
    first = lane < HEAD
    return first, jnp.logical_not(first)


def attention_forward_kernel(qkv_ref, ctx_ref, lt_ref):
    for p in range(ctx_ref.shape[1] // PAIR):
        attention_forward_pair(qkv_ref, ctx_ref, lt_ref, 3 * PAIR * p, PAIR * p)


def attention_forward_pair(qkv_ref, ctx_ref, lt_ref, at, out_at):
    scale = HEAD ** (-0.5)
    q = qkv_ref[:, at : at + PAIR]
    k = qkv_ref[:, at + PAIR : at + 2 * PAIR]
    v = qkv_ref[:, at + 2 * PAIR : at + 3 * PAIR]
    masks = _head_masks(q.shape)
    zero = jnp.zeros_like(q)
    context = None
    total = None
    for mask in masks:
        scores = product_nt(jnp.where(mask, q, zero), k) * scale
        top = jnp.max(scores, axis=-1, keepdims=True)
        weights = jnp.exp(scores - top)
        sums = jnp.sum(weights, axis=-1, keepdims=True)
        probs = (weights / sums).astype(jnp.bfloat16)
        part = jnp.dot(probs, v, preferred_element_type=jnp.float32)
        log_total = jnp.broadcast_to(top + jnp.log(sums), part.shape)
        context = part if context is None else jnp.where(mask, part, context)
        total = log_total if total is None else jnp.where(mask, log_total, total)
    ctx_ref[:, out_at : out_at + PAIR] = context.astype(ctx_ref.dtype)
    lt_ref[:, out_at : out_at + PAIR] = total


def attention_backward_kernel(qkv_ref, lt_ref, g_ref, out_ref):
    for p in range(g_ref.shape[1] // PAIR):
        attention_backward_pair(qkv_ref, lt_ref, g_ref, out_ref, 3 * PAIR * p, PAIR * p)


def attention_backward_pair(qkv_ref, lt_ref, g_ref, out_ref, at, in_at):
    scale = HEAD ** (-0.5)
    q = qkv_ref[:, at : at + PAIR]
    k = qkv_ref[:, at + PAIR : at + 2 * PAIR]
    v = qkv_ref[:, at + 2 * PAIR : at + 3 * PAIR]
    g = g_ref[:, in_at : in_at + PAIR]
    lt_t = lt_ref[:, in_at : in_at + PAIR].T
    masks = _head_masks(q.shape)
    zero = jnp.zeros_like(q)
    dq = dk = dv = None
    for h, mask in enumerate(masks):
        lt_row = lt_t[h * HEAD : h * HEAD + 1, :]
        scores_t = product_nt(jnp.where(mask, k, zero), q) * scale
        probs_t = jnp.exp(scores_t - lt_row)
        prob_grad_t = product_nt(jnp.where(mask, v, zero), g)
        value_part = jnp.dot(probs_t.astype(jnp.bfloat16), g, preferred_element_type=jnp.float32)
        row_sums = jnp.sum(probs_t * prob_grad_t, axis=0, keepdims=True)
        score_grad_t = (probs_t * (prob_grad_t - row_sums)).astype(jnp.bfloat16)
        key_part = jnp.dot(score_grad_t, q, preferred_element_type=jnp.float32) * scale
        query_part = lax.dot_general(score_grad_t, k, TN, preferred_element_type=jnp.float32) * scale
        if dq is None:
            dq, dk, dv = query_part, key_part, value_part
        else:
            dq = jnp.where(mask, query_part, dq)
            dk = jnp.where(mask, key_part, dk)
            dv = jnp.where(mask, value_part, dv)
    out_ref[:, at : at + PAIR] = dq.astype(out_ref.dtype)
    out_ref[:, at + PAIR : at + 2 * PAIR] = dk.astype(out_ref.dtype)
    out_ref[:, at + 2 * PAIR : at + 3 * PAIR] = dv.astype(out_ref.dtype)


def attention_forward(qkv):
    tokens, width = qkv.shape
    group = GROUP if (width // (3 * PAIR)) % GROUP == 0 else 1
    grid = (tokens // SEQ, width // (3 * PAIR * group))
    steps = grid[0] * grid[1] * group
    pair = pl.BlockSpec((SEQ, PAIR * group), lambda s, h: (s, h))
    return pl.pallas_call(
        attention_forward_kernel,
        grid=grid,
        in_specs=[pl.BlockSpec((SEQ, 3 * PAIR * group), lambda s, h: (s, h))],
        out_specs=[pair, pair],
        out_shape=[
            jax.ShapeDtypeStruct((tokens, width // 3), jnp.bfloat16),
            jax.ShapeDtypeStruct((tokens, width // 3), jnp.float32),
        ],
        compiler_params=pltpu.CompilerParams(dimension_semantics=("parallel", "parallel")),
        cost_estimate=pl.CostEstimate(
            flops=steps * 8 * SEQ * SEQ * PAIR,
            transcendentals=steps * 2 * SEQ * SEQ,
            bytes_accessed=tokens * width * 4,
        ),
        name="attention_forward",
    )(qkv)


def attention_backward(qkv, log_total, context_grad):
    tokens, width = qkv.shape
    group = GROUP if (width // (3 * PAIR)) % GROUP == 0 else 1
    grid = (tokens // SEQ, width // (3 * PAIR * group))
    steps = grid[0] * grid[1] * group
    pair = pl.BlockSpec((SEQ, PAIR * group), lambda s, h: (s, h))
    triple = pl.BlockSpec((SEQ, 3 * PAIR * group), lambda s, h: (s, h))
    return pl.pallas_call(
        attention_backward_kernel,
        grid=grid,
        in_specs=[triple, pair, pair],
        out_specs=triple,
        out_shape=jax.ShapeDtypeStruct((tokens, width), jnp.bfloat16),
        compiler_params=pltpu.CompilerParams(dimension_semantics=("parallel", "parallel")),
        cost_estimate=pl.CostEstimate(
            flops=steps * 20 * SEQ * SEQ * PAIR,
            transcendentals=steps * 2 * SEQ * SEQ,
            bytes_accessed=tokens * width * 6,
        ),
        name="attention_backward",
    )(qkv, log_total, context_grad)


def weight_grad_kernel(*refs):
    count = (len(refs) - 2) // 2
    xs, gs = refs[:count], refs[count : 2 * count]
    out_ref, sum_ref = refs[-2], refs[-1]
    acc = None
    sums = None
    for x_ref, g_ref in zip(xs, gs):
        g = g_ref[...]
        part = lax.dot_general(x_ref[...], g, TN, preferred_element_type=jnp.float32)
        col = jnp.sum(g.astype(jnp.float32), axis=0, keepdims=True)
        acc = part if acc is None else acc + part
        sums = col if sums is None else sums + col
    out_ref[...] = acc.astype(out_ref.dtype)
    sum_ref[...] = sums


def weight_grad(xs, gs, into=None, at=0, stack=False, columns=None, block=768):
    tokens, depth = xs[0].shape
    width = gs[0].shape[1]
    bk = min(block, depth)
    bn = min(block, width)
    grid = (depth // bk, width // bn)
    count = len(xs)
    if stack:
        place = lambda i, j: (0, at + i * grid[1] + j)
        shape = (bk, depth // bk * width)
    else:
        place = lambda i, j: (i, at + j)
        shape = (depth, width)
    if into is not None:
        target = into.shape
    elif columns is not None:
        target = (shape[0], columns)
    else:
        target = shape
    in_specs = [pl.BlockSpec((tokens, bk), lambda i, j: (0, i))] * count + [
        pl.BlockSpec((tokens, bn), lambda i, j: (0, j))
    ] * count
    args = list(xs) + list(gs)
    aliases = {}
    kernel = weight_grad_kernel
    if into is not None:
        in_specs.append(pl.BlockSpec(memory_space=pl.ANY))
        args.append(into)
        aliases = {len(args) - 1: 0}
        kernel = lambda *refs: weight_grad_kernel(*refs[: 2 * count], *refs[2 * count + 1 :])
    return pl.pallas_call(
        kernel,
        grid=grid,
        in_specs=in_specs,
        out_specs=[
            pl.BlockSpec((bk, bn), place),
            pl.BlockSpec((1, bn), lambda i, j: (0, j)),
        ],
        out_shape=[
            jax.ShapeDtypeStruct(target, jnp.bfloat16),
            jax.ShapeDtypeStruct((1, width), jnp.float32),
        ],
        input_output_aliases=aliases,
        compiler_params=pltpu.CompilerParams(
            dimension_semantics=("arbitrary", "arbitrary"), vmem_limit_bytes=48 * 1024 * 1024
        ),
        cost_estimate=pl.CostEstimate(
            flops=2 * count * tokens * depth * width,
            transcendentals=0,
            bytes_accessed=2 * count * tokens * (depth + width) + 2 * depth * width,
        ),
        name="weight_grad",
    )(*args)


def interleave_qkv(q, k, v):
    lead = q.shape[:-1]
    pairs = q.shape[-1] // PAIR
    stacked = jnp.stack([q, k, v], axis=-2).reshape(lead + (3, pairs, PAIR))
    return jnp.swapaxes(stacked, -3, -2).reshape(lead + (3 * pairs * PAIR,))


def split_qkv(packed):
    pairs = packed.shape[-1] // (3 * PAIR)
    parts = [[], [], []]
    for h in range(pairs):
        for which in range(3):
            start = (3 * h + which) * PAIR
            parts[which].append(packed[..., start : start + PAIR])
    return [jnp.concatenate(p, axis=-1) for p in parts]


def to_hidden_order(values, groups=4):
    lead, n = values.shape[:-1], values.shape[-1]
    return jnp.swapaxes(values.reshape(lead + (n // groups, groups)), -1, -2).reshape(lead + (n,))


def from_hidden_order(values, groups=4):
    lead, n = values.shape[:-1], values.shape[-1]
    return jnp.swapaxes(values.reshape(lead + (groups, n // groups)), -1, -2).reshape(lead + (n,))


def pack_weights(weights):
    (qw, qb, kw, vw, vb, ow, ob, g1, s1, iw, ib, uw, ub, g2, s2) = weights
    rows, width = qw.shape
    wide = iw.shape[1]
    columns = jnp.stack([qb, vb, ob, g1, s1, ub, g2, s2], axis=1)
    columns = jnp.concatenate([columns, ib.reshape(rows, -1)], axis=1)
    columns = jnp.pad(columns, ((0, 0), (0, PAIR - columns.shape[1])))
    return jnp.concatenate(
        [interleave_qkv(qw, kw, vw), ow, to_hidden_order(iw), uw.reshape(rows, wide), columns],
        axis=1,
    )


def gather_weights(weights):
    rows, width = weights[0].shape
    wide = weights[9].shape[1]
    packed = lax.all_gather(pack_weights(weights), AXES, axis=0, tiled=True)
    full = packed.shape[0]
    shards = full // rows
    three = 3 * width
    at = 0
    pieces = []
    for count in (three, width, wide, wide, PAIR):
        pieces.append(packed[:, at : at + count])
        at += count
    qkv, out, inner, outer_rows, cols = pieces
    groups = wide // width
    outer = jnp.concatenate(
        [outer_rows[:, c * width : (c + 1) * width] for c in range(groups)], axis=0
    )
    outer = lax.optimization_barrier(outer)
    cols = cols.astype(jnp.float32)
    (qb, vb, ob, g1, s1, ub, g2, s2) = [cols[:, i] for i in range(8)]
    ib = cols[:, 8 : 8 + groups].reshape(shards, rows, groups)
    return dict(
        qkv=qkv,
        qkv_bias=interleave_qkv(qb, jnp.zeros_like(qb), vb),
        out=out,
        out_bias=ob,
        g1=g1,
        s1=s1,
        inner=inner,
        inner_bias=ib.transpose(2, 0, 1).reshape(-1),
        outer=outer,
        outer_bias=ub,
        g2=g2,
        s2=s2,
    )


def layer_forward(w, hidden_state):
    rows_low = hidden_state.astype(jnp.bfloat16)
    qkv = (product(rows_low, w["qkv"]) + w["qkv_bias"]).astype(jnp.bfloat16)
    context_low, log_total = attention_forward(qkv)
    attended = product(context_low, w["out"]) + w["out_bias"]
    first_out, first_normed, first_inverse = layer_norm(hidden_state + attended, w["g1"], w["s1"])
    first_low = first_out.astype(jnp.bfloat16)
    inner_pre = product(first_low, w["inner"]) + w["inner_bias"]
    inner_act, inner_slope = gelu_tanh(inner_pre)
    inner_low = inner_act.astype(jnp.bfloat16)
    outer_out = product(inner_low, w["outer"]) + w["outer_bias"]
    result, second_normed, second_inverse = layer_norm(first_out + outer_out, w["g2"], w["s2"])
    kept = dict(
        rows_low=rows_low,
        qkv=qkv,
        log_total=log_total,
        context_low=context_low,
        first_normed=first_normed,
        first_inverse=first_inverse,
        first_low=first_low,
        inner_slope=inner_slope,
        inner_low=inner_low,
        second_normed=second_normed,
        second_inverse=second_inverse,
    )
    return result, kept


def layer_backward(w, kept, upstream):
    second_gain_grad = jnp.sum(upstream * kept["second_normed"], axis=0)
    second_shift_grad = jnp.sum(upstream, axis=0)
    second_grad = norm_backward(upstream, kept["second_normed"], kept["second_inverse"], w["g2"])
    outer_low = second_grad.astype(jnp.bfloat16)
    active_grad = product_nt(outer_low, w["outer"])
    inner_grad = (active_grad * kept["inner_slope"]).astype(jnp.bfloat16)
    first_grad = second_grad + product_nt(inner_grad, w["inner"])
    first_gain_grad = jnp.sum(first_grad * kept["first_normed"], axis=0)
    first_shift_grad = jnp.sum(first_grad, axis=0)
    attended_grad = norm_backward(first_grad, kept["first_normed"], kept["first_inverse"], w["g1"])
    attended_low = attended_grad.astype(jnp.bfloat16)
    context_grad = product_nt(attended_low, w["out"]).astype(jnp.bfloat16)
    qkv_grad = attention_backward(kept["qkv"], kept["log_total"], context_grad)
    below_grad = attended_grad + product_nt(qkv_grad, w["qkv"])
    saved = dict(
        outer_low=outer_low,
        inner_grad=inner_grad,
        attended_low=attended_low,
        qkv_grad=qkv_grad,
    )
    norms = (second_gain_grad, second_shift_grad, first_gain_grad, first_shift_grad)
    return below_grad, saved, norms


def scatter_grads(kept, saved, norms, shards):
    def across(source, name):
        return [item[name] for item in source]

    width = kept[0]["context_low"].shape[1]
    three = kept[0]["qkv"].shape[1]
    wide = kept[0]["inner_low"].shape[1]
    blocks = (three + width + 2 * wide) // width
    packed, qkv_b = weight_grad(
        across(kept, "rows_low"), across(saved, "qkv_grad"), columns=blocks * width + PAIR
    )
    at = three // width
    packed, out_b = weight_grad(
        across(kept, "context_low"), across(saved, "attended_low"), into=packed, at=at
    )
    at += 1
    packed, inner_b = weight_grad(
        across(kept, "first_low"), across(saved, "inner_grad"), into=packed, at=at
    )
    at += wide // width
    packed, outer_b = weight_grad(
        across(kept, "inner_low"), across(saved, "outer_low"), into=packed, at=at, stack=True
    )
    rows = width
    q_b, _, v_b = split_qkv(qkv_b[0])
    s2g, s2s, s1g, s1s = [sum(parts) for parts in zip(*norms)]
    columns = jnp.stack([q_b, v_b, out_b[0], s1g, s1s, outer_b[0], s2g, s2s], axis=1)
    inner_cols = inner_b[0].reshape(wide // rows, rows).T
    columns = jnp.concatenate([columns, inner_cols], axis=1)
    columns = jnp.pad(columns, ((0, 0), (0, PAIR - columns.shape[1]))).astype(jnp.bfloat16)
    packed = lax.dynamic_update_slice(packed, columns, (0, blocks * width))
    mine = lax.psum_scatter(packed, AXES, scatter_dimension=0, tiled=True).astype(jnp.float32)
    at = 0
    pieces = []
    for count in (three, width, wide, wide, PAIR):
        pieces.append(mine[:, at : at + count])
        at += count
    qkv_mine, out_mine, inner_mine, outer_mine, col_mine = pieces
    q_w, k_w, v_w = split_qkv(qkv_mine)
    col_rows = col_mine[:, :12].T
    c = [col_rows[i] for i in range(8)]
    ib_mine = col_rows[8:12].T.reshape(-1)
    return (
        q_w,
        c[0],
        k_w,
        v_w,
        c[1],
        out_mine,
        c[2],
        c[3],
        c[4],
        from_hidden_order(inner_mine),
        ib_mine,
        outer_mine.reshape(-1, width),
        c[5],
        c[6],
        c[7],
    )


def per_device(shards, inputs, cotangent, masked, *weights):
    w = gather_weights(weights)
    hidden_state = inputs.astype(jnp.float32)
    kept = []
    for applied in range(LAYERS):
        hidden_state, kept_values = layer_forward(w, hidden_state)
        kept.append(kept_values)
    outputs = hidden_state.astype(jnp.bfloat16)
    upstream = cotangent.astype(jnp.float32) * masked.reshape(-1, 1).astype(jnp.float32)
    saved = [None] * LAYERS
    norms = [None] * LAYERS
    for applied in range(LAYERS - 1, -1, -1):
        upstream, saved[applied], norms[applied] = layer_backward(w, kept[applied], upstream)
    collected = scatter_grads(kept, saved, norms, shards)
    return (outputs, upstream.astype(jnp.bfloat16)) + tuple(collected)


def solution(mesh):
    rows = P(AXES, None)
    vec = P(AXES)
    in_specs = (rows, rows, rows, rows, vec, rows, rows, vec, rows, vec, vec, vec, rows, vec, rows, vec, vec, vec)
    out_specs = (rows, rows, rows, vec, rows, rows, vec, rows, vec, vec, vec, rows, vec, rows, vec, vec, vec)
    shards = mesh.shape["dp"] * mesh.shape["fsdp"]
    return jax.shard_map(
        functools.partial(per_device, shards),
        mesh=mesh,
        in_specs=in_specs,
        out_specs=out_specs,
        check_vma=False,
    )
```
